32 devices in a mesh: groups: 2 (over y), lon: 16 (over z, x, core).
Axes of the slice: x: 2, y: 2, z: 4, core: 2. Of those that a mesh axis runs over, the one named last changes fastest.
Arguments:
- features: bfloat16 [4, 256, 32, 256], P(None, ('groups', 'lon')), parts along dimension 1, may hold values from -6 to 6
- target: bfloat16 [256, 32, 256], P(('groups', 'lon')), parts along dimension 0, may hold values from -6 to 6
- south_rim: bfloat16 [4, 256, 3, 256], P(None, ('groups', 'lon')), parts along dimension 1, may hold values from -6 to 6
- kmt: int32 [256, 32], P(('groups', 'lon')), parts along dimension 0, may hold values from 0 to 19
- dw_kernel: float32 [7, 7, 256], replicated, may hold values from -0.875 to 0.875
- dw_bias: float32 [256], replicated, may hold values from -3 to 3
- ln_gain: float32 [256], replicated, may hold values from 0.25 to 1.75
- ln_bias: float32 [256], replicated, may hold values from -3 to 3
- w_in: bfloat16 [256, 1024], replicated, may hold values from -0.375 to 0.375
- b_in: float32 [1024], replicated, may hold values from -3 to 3
- w_out: bfloat16 [1024, 256], replicated, may hold values from -0.1875 to 0.1875
- b_out: float32 [256], replicated, may hold values from -3 to 3
- layer_scale: float32 [256], replicated, may hold values from 0.3 to 1.5
Outputs:
- predicted: bfloat16 [4, 256, 32, 256], P(None, ('groups', 'lon')), parts along dimension 1
- crps_field: float32 [256, 32, 256], P(('groups', 'lon')), parts along dimension 0
- grad_features: bfloat16 [4, 256, 32, 256], P(None, ('groups', 'lon')), parts along dimension 1
- grad_kernel: float32 [14, 7, 256], P('groups'), parts along dimension 0
- grad_dw_bias: float32 [512], P('groups'), parts along dimension 0
- grad_ln_gain: float32 [512], P('groups'), parts along dimension 0
- grad_ln_bias: float32 [512], P('groups'), parts along dimension 0
- grad_w_in: float32 [512, 1024], P('groups'), parts along dimension 0
- grad_b_in: float32 [2048], P('groups'), parts along dimension 0
- grad_w_out: float32 [2048, 256], P('groups'), parts along dimension 0
- grad_b_out: float32 [512], P('groups'), parts along dimension 0
- grad_scale: float32 [512], P('groups'), parts along dimension 0
The draws below stay inside these ranges and needn't reach their ends.
There are 2 independent parts, one for each index of `groups`. The reference program is written for one: setup_inputs(seed, part) draws one part's arguments, and reference() takes and returns one part's arrays. A program takes and returns all parts, laid end to end along the dimension named above; an argument that names none is the same for every part. Nothing has to cross between parts.
All inputs are finite; a program needn't handle non-finite values.
Results may differ from the reference program's by a relative error of at most 0.0075.
Values may be sent and summed in bfloat16 or wider, within the bound.
No kernel may reach another device: no remote copies, remote signals or barrier semaphores. Data moves between devices by JAX's collectives and lax.ppermute only.
A program may use at most 64 MiB of HBM per device.

```python
import math
import jax
import jax.numpy as jnp
from jax import lax

C = 256
HID = 1024
LEVELS = 19
MEMBERS = 4
LON_DEV = 8
LAT = 32
NLON = 128
N_LON = 16


def touch_ends(array, key, least, high):
    longest = array.shape.index(max(array.shape))
    spots = []
    for shift in (0, 1):
        where = [jax.random.randint(jax.random.fold_in(key, axis), (), 0, length) for axis, length in enumerate(array.shape)]
        where[longest] = (where[longest] + shift) % array.shape[longest]
        spots.append(tuple(where))
    return array.at[spots[0]].set(least).at[spots[1]].set(high)


def block_scale(own_key, dims, cuts, least, largest):
    factor_of, own = 1.0, jax.random.fold_in(own_key, 6)
    for dim, blocks in cuts:
        steps = jnp.exp(jax.random.uniform(jax.random.fold_in(own, dim), (blocks,), jnp.float32, least / len(cuts), largest / len(cuts)))
        factor_of = factor_of * jnp.repeat(steps, dims[dim] // blocks).reshape([-1 if axis == dim else 1 for axis in range(len(dims))])
    return factor_of


def bell_draw(own_key, shape, scale, most, pieces=(), held_as=jnp.bfloat16):
    loudness = block_scale(own_key, shape, pieces, -0.22, 0.18) if pieces else 1.0
    drawn = jax.random.normal(own_key, shape, jnp.float32) * scale * loudness
    return jnp.minimum(jnp.maximum(drawn, -most), most).astype(held_as)


def setup_inputs(seed: int = 0, part: int = 0) -> dict:
    arg_keys = jax.random.split(jax.random.key(seed), 14)
    part_keys = jax.random.split(jax.random.fold_in(arg_keys[13], part), 14)
    features = bell_draw(part_keys[0], (MEMBERS, NLON, LAT, C), 1.0, 6.0, ((1, 16),))
    target = bell_draw(part_keys[1], (NLON, LAT, C), 1.0, 6.0, ((0, 16),))
    south_rim = bell_draw(part_keys[2], (MEMBERS, NLON, 3, C), 1.0, 6.0, ((1, 16),))
    kmt = touch_ends(jax.random.randint(part_keys[3], (NLON, LAT), 0, LEVELS + 1), jax.random.fold_in(part_keys[3], 1), 0, LEVELS).astype(jnp.int32)
    dw_kernel = bell_draw(arg_keys[4], (7, 7, C), 49 ** -0.5, 0.875, (), jnp.float32)
    dw_bias = bell_draw(arg_keys[5], (C,), 0.5, 3.0, (), jnp.float32)
    ln_gain = jnp.clip(1.0 + 0.15 * jax.random.normal(arg_keys[6], (C,), jnp.float32), 0.25, 1.75)
    ln_bias = bell_draw(arg_keys[7], (C,), 0.5, 3.0, (), jnp.float32)
    w_in = bell_draw(arg_keys[8], (C, HID), C ** -0.5, 0.375)
    b_in = bell_draw(arg_keys[9], (HID,), 0.5, 3.0, (), jnp.float32)
    w_out = bell_draw(arg_keys[10], (HID, C), HID ** -0.5, 0.1875)
    b_out = bell_draw(arg_keys[11], (C,), 0.5, 3.0, (), jnp.float32)
    layer_scale = jnp.clip(jnp.exp(jax.random.uniform(arg_keys[12], (C,), jnp.float32, math.log(0.3), math.log(1.5))), 0.3, 1.5)
    return dict(features=features, target=target, south_rim=south_rim, kmt=kmt, dw_kernel=dw_kernel, dw_bias=dw_bias, ln_gain=ln_gain, ln_bias=ln_bias, w_in=w_in, b_in=b_in, w_out=w_out, b_out=b_out, layer_scale=layer_scale)


SMOOTH = 0.25
EPSILON = 1e-06

def smooth_abs(value):
    return jnp.sqrt(value * value + SMOOTH * SMOOTH) - SMOOTH

def smooth_slope(value):
    return value / jnp.sqrt(value * value + SMOOTH * SMOOTH)

def local_step(extended, features, target, kmt, dw_kernel, dw_bias, ln_gain, ln_bias, w_in, b_in, w_out, b_out, layer_scale):
    members, lon_dev, lat_rows, chans = features.shape
    depth = jnp.zeros(features.shape, jnp.float32) + dw_bias
    for lon_off in range(7):
        for lat_off in range(7):
            depth = depth + dw_kernel[lon_off, lat_off] * extended[:, lon_off:lon_off + lon_dev, lat_off:lat_off + lat_rows, :].astype(jnp.float32)
    mean_val = lax.optimization_barrier(jnp.mean(depth, axis=-1, keepdims=True))
    centred = depth - mean_val
    variance = lax.optimization_barrier(jnp.mean(centred * centred, axis=-1, keepdims=True))
    inv_std = lax.rsqrt(variance + EPSILON)
    unit = centred * inv_std
    normed = (unit * ln_gain + ln_bias).astype(jnp.bfloat16)
    level_of = jnp.arange(chans, dtype=jnp.int32) * LEVELS // chans
    wet_mask = (level_of[None, None, :] < kmt[:, :, None]).astype(jnp.float32)
    rows = lon_dev * lat_rows
    pre_acts = []
    hiddens = []
    outputs = []
    for member in range(members):
        flat_rows = normed[member].reshape(rows, chans)
        pre_act = jnp.dot(flat_rows, w_in, preferred_element_type=jnp.float32) + b_in
        hidden = jax.nn.gelu(pre_act).astype(jnp.bfloat16)
        pre_acts.append(pre_act)
        hiddens.append(hidden)
        outputs.append((jnp.dot(hidden, w_out, preferred_element_type=jnp.float32) + b_out).reshape(lon_dev, lat_rows, chans))
    branch = jnp.stack(outputs)
    pred = wet_mask * (features.astype(jnp.float32) + layer_scale * branch)
    target_full = target.astype(jnp.float32)
    pair_weight = 1.0 / (members * (members - 1))
    skill = jnp.zeros(target.shape, jnp.float32)
    spread = jnp.zeros(target.shape, jnp.float32)
    for member in range(members):
        skill = skill + smooth_abs(pred[member] - target_full)
        for other in range(member + 1, members):
            spread = spread + smooth_abs(pred[member] - pred[other])
    crps_field = wet_mask * (skill / members - pair_weight * spread)
    grad_list = []
    for member in range(members):
        slope_sum = jnp.zeros(target.shape, jnp.float32)
        for other in range(members):
            if other != member:
                slope_sum = slope_sum + smooth_slope(pred[member] - pred[other])
        grad_list.append(wet_mask * (smooth_slope(pred[member] - target_full) / members - pair_weight * slope_sum))
    grad_pred = jnp.stack(grad_list)
    grad_scale = lax.optimization_barrier(jnp.sum(grad_pred * branch, axis=(0, 1, 2)))
    grad_b_out = jnp.zeros((chans,), jnp.float32)
    grad_w_out = jnp.zeros(w_out.shape, jnp.float32)
    grad_b_in = jnp.zeros(b_in.shape, jnp.float32)
    grad_w_in = jnp.zeros(w_in.shape, jnp.float32)
    normed_grads = []
    contract_rows = (((0,), (0,)), ((), ()))
    contract_cols = (((1,), (1,)), ((), ()))
    for member in range(members):
        grad_out = (grad_pred[member] * layer_scale).reshape(rows, chans)
        grad_b_out = grad_b_out + lax.optimization_barrier(jnp.sum(grad_out, axis=0))
        out_half = grad_out.astype(jnp.bfloat16)
        grad_w_out = grad_w_out + lax.dot_general(hiddens[member], out_half, contract_rows, preferred_element_type=jnp.float32)
        grad_hidden = lax.dot_general(out_half, w_out, contract_cols, preferred_element_type=jnp.float32)
        grad_pre = jax.vjp(jax.nn.gelu, pre_acts[member])[1](grad_hidden)[0]
        grad_b_in = grad_b_in + lax.optimization_barrier(jnp.sum(grad_pre, axis=0))
        pre_half = grad_pre.astype(jnp.bfloat16)
        grad_w_in = grad_w_in + lax.dot_general(normed[member].reshape(rows, chans), pre_half, contract_rows, preferred_element_type=jnp.float32)
        normed_grads.append(lax.dot_general(pre_half, w_in, contract_cols, preferred_element_type=jnp.float32).reshape(lon_dev, lat_rows, chans))
    grad_normed = jnp.stack(normed_grads)
    grad_ln_gain = lax.optimization_barrier(jnp.sum(grad_normed * unit, axis=(0, 1, 2)))
    grad_ln_bias = lax.optimization_barrier(jnp.sum(grad_normed, axis=(0, 1, 2)))
    grad_unit = grad_normed * ln_gain
    grad_depth = inv_std * (grad_unit - lax.optimization_barrier(jnp.mean(grad_unit, axis=-1, keepdims=True)) - unit * lax.optimization_barrier(jnp.mean(grad_unit * unit, axis=-1, keepdims=True)))
    grad_dw_bias = lax.optimization_barrier(jnp.sum(grad_depth, axis=(0, 1, 2)))
    kernel_rows = []
    for lon_off in range(7):
        kernel_cols = []
        for lat_off in range(7):
            kernel_cols.append(lax.optimization_barrier(jnp.sum(grad_depth * extended[:, lon_off:lon_off + lon_dev, lat_off:lat_off + lat_rows, :].astype(jnp.float32), axis=(0, 1, 2))))
        kernel_rows.append(jnp.stack(kernel_cols))
    grad_kernel = jnp.stack(kernel_rows)
    grads = (grad_kernel, grad_dw_bias, grad_ln_gain, grad_ln_bias, grad_w_in, grad_b_in, grad_w_out, grad_b_out, grad_scale)
    return (pred.astype(jnp.bfloat16), crps_field, grad_pred, grad_depth, grads)

def reference(features, target, south_rim, kmt, dw_kernel, dw_bias, ln_gain, ln_bias, w_in, b_in, w_out, b_out, layer_scale):
    north = features[:, ::-1, LAT - 3:, :][:, :, ::-1, :]
    extended = jnp.concatenate([south_rim, features, north], axis=2)
    wrapped = jnp.concatenate([extended[:, NLON - 3:], extended, extended[:, :3]], axis=1)
    zero_grads = (jnp.zeros((7, 7, C), jnp.float32), jnp.zeros((C,), jnp.float32), jnp.zeros((C,), jnp.float32), jnp.zeros((C,), jnp.float32), jnp.zeros((C, HID), jnp.float32), jnp.zeros((HID,), jnp.float32), jnp.zeros((HID, C), jnp.float32), jnp.zeros((C,), jnp.float32), jnp.zeros((C,), jnp.float32))

    def block(carry, index):
        start = (index * LON_DEV).astype(jnp.int32)
        ext_block = lax.dynamic_slice_in_dim(wrapped, start, LON_DEV + 6, 1)
        feat_block = lax.dynamic_slice_in_dim(features, start, LON_DEV, 1)
        targ_block = lax.dynamic_slice_in_dim(target, start, LON_DEV, 0)
        kmt_block = lax.dynamic_slice_in_dim(kmt, start, LON_DEV, 0)
        pred, crps_block, grad_pred, grad_depth, grads = local_step(ext_block, feat_block, targ_block, kmt_block, dw_kernel, dw_bias, ln_gain, ln_bias, w_in, b_in, w_out, b_out, layer_scale)
        carry = tuple((total + term for total, term in zip(carry, grads)))
        return (carry, (pred, crps_block, grad_pred, grad_depth))
    totals, stacked = lax.scan(block, zero_grads, jnp.arange(N_LON, dtype=jnp.int32))
    predicted = jnp.moveaxis(stacked[0], 0, 1).reshape(MEMBERS, NLON, LAT, C)
    crps_field = stacked[1].reshape(NLON, LAT, C)
    grad_pred = jnp.moveaxis(stacked[2], 0, 1).reshape(MEMBERS, NLON, LAT, C)
    grad_depth = jnp.moveaxis(stacked[3], 0, 1).reshape(MEMBERS, NLON, LAT, C)
    grad_wrap = jnp.concatenate([grad_depth[:, NLON - 3:], grad_depth, grad_depth[:, :3]], axis=1)
    padded = jnp.pad(grad_wrap, ((0, 0), (0, 0), (6, 6), (0, 0)))
    grad_ext = jnp.zeros((MEMBERS, NLON, LAT + 6, C), jnp.float32)
    for lon_off in range(7):
        for lat_off in range(7):
            grad_ext = grad_ext + dw_kernel[lon_off, lat_off] * padded[:, 6 - lon_off:6 - lon_off + NLON, 6 - lat_off:6 - lat_off + LAT + 6, :]
    back_rows = grad_ext[:, ::-1, LAT + 3:, :][:, :, ::-1, :]
    inner = grad_pred + grad_ext[:, :, 3:LAT + 3, :]
    grad_features = jnp.concatenate([inner[:, :, :LAT - 3, :], inner[:, :, LAT - 3:, :] + back_rows], axis=2).astype(jnp.bfloat16)
    factor = 1.0 / math.sqrt(MEMBERS * LAT * NLON)
    return (predicted, crps_field, grad_features, totals[0] * factor, totals[1] * factor, totals[2] * factor, totals[3] * factor, totals[4] * factor, totals[5] * factor, totals[6] * factor, totals[7] * factor, totals[8] * factor)
```

```python
import math

import jax
import jax.numpy as jnp
from jax import lax
from jax.sharding import PartitionSpec as P

LEVELS = 19


SMOOTH = 0.25
EPSILON = 1e-06


def swapped(x, axis, bit):
    return lax.ppermute(x, axis, [(i, i ^ 1 << bit) for i in range(lax.axis_size(axis))])


def with_halo(x, sides, width):
    for axis, dim in sides:
        size, length = (lax.axis_size(axis), x.shape[dim])
        up = [(i, (i + 1) % size) for i in range(size)]
        down = [(j, i) for i, j in up]
        last = lax.slice_in_dim(x, length - width, length, axis=dim)
        leading = lax.slice_in_dim(x, 0, width, axis=dim)
        before = lax.ppermute(last, axis, up)
        after = lax.ppermute(leading, axis, down)
        x = jnp.concatenate([before, x, after], axis=dim)
    return x


def smooth_abs(value):
    return jnp.sqrt(value * value + SMOOTH * SMOOTH) - SMOOTH


def smooth_slope(value):
    return value / jnp.sqrt(value * value + SMOOTH * SMOOTH)


def local_step(
    extended,
    features,
    target,
    kmt,
    dw_kernel,
    dw_bias,
    ln_gain,
    ln_bias,
    w_in,
    b_in,
    w_out,
    b_out,
    layer_scale,
):
    members, lon_dev, lat_rows, chans = features.shape
    depth = jnp.zeros(features.shape, jnp.float32) + dw_bias
    for lon_off in range(7):
        for lat_off in range(7):
            depth = depth + dw_kernel[lon_off, lat_off] * extended[
                :, lon_off : lon_off + lon_dev, lat_off : lat_off + lat_rows, :
            ].astype(jnp.float32)
    mean_val = jnp.mean(depth, axis=-1, keepdims=True)
    centred = depth - mean_val
    variance = jnp.mean(centred * centred, axis=-1, keepdims=True)
    inv_std = lax.rsqrt(variance + EPSILON)
    unit = centred * inv_std
    normed = (unit * ln_gain + ln_bias).astype(jnp.bfloat16)
    level_of = jnp.arange(chans, dtype=jnp.int32) * LEVELS // chans
    wet_mask = (level_of[None, None, :] < kmt[:, :, None]).astype(jnp.float32)
    rows = lon_dev * lat_rows
    pre_acts = []
    hiddens = []
    outputs = []
    for member in range(members):
        flat_rows = normed[member].reshape(rows, chans)
        pre_act = jnp.dot(flat_rows, w_in, preferred_element_type=jnp.float32) + b_in
        hidden = jax.nn.gelu(pre_act).astype(jnp.bfloat16)
        pre_acts.append(pre_act)
        hiddens.append(hidden)
        outputs.append(
            (jnp.dot(hidden, w_out, preferred_element_type=jnp.float32) + b_out).reshape(
                lon_dev, lat_rows, chans
            )
        )
    branch = jnp.stack(outputs)
    pred = wet_mask * (features.astype(jnp.float32) + layer_scale * branch)
    target_full = target.astype(jnp.float32)
    pair_weight = 1.0 / (members * (members - 1))
    skill = jnp.zeros(target.shape, jnp.float32)
    spread = jnp.zeros(target.shape, jnp.float32)
    for member in range(members):
        skill = skill + smooth_abs(pred[member] - target_full)
        for other in range(member + 1, members):
            spread = spread + smooth_abs(pred[member] - pred[other])
    crps_field = wet_mask * (skill / members - pair_weight * spread)
    grad_list = []
    for member in range(members):
        slope_sum = jnp.zeros(target.shape, jnp.float32)
        for other in range(members):
            if other != member:
                slope_sum = slope_sum + smooth_slope(pred[member] - pred[other])
        grad_list.append(
            wet_mask
            * (smooth_slope(pred[member] - target_full) / members - pair_weight * slope_sum)
        )
    grad_pred = jnp.stack(grad_list)
    grad_scale = jnp.sum(grad_pred * branch, axis=(0, 1, 2))
    grad_b_out = jnp.zeros((chans,), jnp.float32)
    grad_w_out = jnp.zeros(w_out.shape, jnp.float32)
    grad_b_in = jnp.zeros(b_in.shape, jnp.float32)
    grad_w_in = jnp.zeros(w_in.shape, jnp.float32)
    normed_grads = []
    contract_rows = (((0,), (0,)), ((), ()))
    contract_cols = (((1,), (1,)), ((), ()))
    for member in range(members):
        grad_out = (grad_pred[member] * layer_scale).reshape(rows, chans)
        grad_b_out = grad_b_out + jnp.sum(grad_out, axis=0)
        out_half = grad_out.astype(jnp.bfloat16)
        grad_w_out = grad_w_out + lax.dot_general(
            hiddens[member], out_half, contract_rows, preferred_element_type=jnp.float32
        )
        grad_hidden = lax.dot_general(
            out_half, w_out, contract_cols, preferred_element_type=jnp.float32
        )
        grad_pre = jax.vjp(jax.nn.gelu, pre_acts[member])[1](grad_hidden)[0]
        grad_b_in = grad_b_in + jnp.sum(grad_pre, axis=0)
        pre_half = grad_pre.astype(jnp.bfloat16)
        grad_w_in = grad_w_in + lax.dot_general(
            normed[member].reshape(rows, chans),
            pre_half,
            contract_rows,
            preferred_element_type=jnp.float32,
        )
        normed_grads.append(
            lax.dot_general(
                pre_half, w_in, contract_cols, preferred_element_type=jnp.float32
            ).reshape(lon_dev, lat_rows, chans)
        )
    grad_normed = jnp.stack(normed_grads)
    grad_ln_gain = jnp.sum(grad_normed * unit, axis=(0, 1, 2))
    grad_ln_bias = jnp.sum(grad_normed, axis=(0, 1, 2))
    grad_unit = grad_normed * ln_gain
    grad_depth = inv_std * (
        grad_unit
        - jnp.mean(grad_unit, axis=-1, keepdims=True)
        - unit * jnp.mean(grad_unit * unit, axis=-1, keepdims=True)
    )
    grad_dw_bias = jnp.sum(grad_depth, axis=(0, 1, 2))
    kernel_rows = []
    for lon_off in range(7):
        kernel_cols = []
        for lat_off in range(7):
            kernel_cols.append(
                jnp.sum(
                    grad_depth
                    * extended[
                        :, lon_off : lon_off + lon_dev, lat_off : lat_off + lat_rows, :
                    ].astype(jnp.float32),
                    axis=(0, 1, 2),
                )
            )
        kernel_rows.append(jnp.stack(kernel_cols))
    grad_kernel = jnp.stack(kernel_rows)
    grads = (
        grad_kernel,
        grad_dw_bias,
        grad_ln_gain,
        grad_ln_bias,
        grad_w_in,
        grad_b_in,
        grad_w_out,
        grad_b_out,
        grad_scale,
    )
    return (pred.astype(jnp.bfloat16), crps_field, grad_pred, grad_depth, grads)


def mirrored(x, axis):
    size = lax.axis_size(axis)
    return lax.ppermute(x, axis, [(i, size - 1 - i) for i in range(size)])


def mirror_rows(top_rows):
    return mirrored(top_rows, "lon")[:, ::-1, ::-1, :]


def mirror_grads(fold_rows):
    picked = mirrored(fold_rows.astype(jnp.bfloat16), "lon").astype(fold_rows.dtype)
    return picked[:, ::-1, ::-1, :]


def halving_allreduce(flat, axis, gather_dtype):
    size = lax.axis_size(axis)
    bits = size.bit_length() - 1
    idx = lax.axis_index(axis)
    cur = flat
    for bit in range(bits):
        half = cur.shape[0] // 2
        mine = (idx >> bit) & 1
        keep = lax.dynamic_slice_in_dim(cur, mine * half, half)
        send = lax.dynamic_slice_in_dim(cur, (1 - mine) * half, half)
        cur = keep + swapped(send, axis, bit)
    cur = cur.astype(gather_dtype)
    for bit in reversed(range(bits)):
        mine = (idx >> bit) & 1
        recv = swapped(cur, axis, bit)
        cur = jnp.where(mine == 0, jnp.concatenate([cur, recv]), jnp.concatenate([recv, cur]))
    return cur.astype(flat.dtype)


def butterfly_allreduce(flat, axis):
    for bit in range(lax.axis_size(axis).bit_length() - 1):
        flat = flat + swapped(flat, axis, bit)
    return flat


def pack(arrays, multiple):
    flat = jnp.concatenate([a.reshape(-1) for a in arrays])
    extra = -flat.shape[0] % multiple
    return jnp.pad(flat, (0, extra))


def unpack(flat, arrays):
    out, at = [], 0
    for a in arrays:
        out.append(flat[at : at + a.size].reshape(a.shape))
        at += a.size
    return out


def on_device(
    features,
    target,
    south_rim,
    kmt,
    dw_kernel,
    dw_bias,
    ln_gain,
    ln_bias,
    w_in,
    b_in,
    w_out,
    b_out,
    layer_scale,
):
    members, lon_dev, lat_rows, chans = features.shape
    params = (dw_kernel, dw_bias, ln_gain, ln_bias, w_in, b_in, w_out, b_out, layer_scale)
    north_rows = mirror_rows(features[:, :, lat_rows - 3 :, :])
    joined = jnp.concatenate([south_rim, features, north_rows], axis=2)
    extended = with_halo(joined, (("lon", 1),), 3)
    predicted, crps_field, grad_pred, grad_depth, grads = local_step(
        extended, features, target, kmt, *params
    )
    grad_halo = with_halo(grad_depth, (("lon", 1),), 3)
    padded = jnp.pad(grad_halo, ((0, 0), (0, 0), (6, 6), (0, 0)))
    grad_ext = jnp.zeros((members, lon_dev, lat_rows + 6, chans), jnp.float32)
    for lon_off in range(7):
        for lat_off in range(7):
            grad_ext = (
                grad_ext
                + dw_kernel[lon_off, lat_off]
                * padded[
                    :,
                    6 - lon_off : 6 - lon_off + lon_dev,
                    6 - lat_off : 6 - lat_off + lat_rows + 6,
                    :,
                ]
            )
    back_rows = mirror_grads(grad_ext[:, :, lat_rows + 3 :, :])
    inner = grad_pred + grad_ext[:, :, 3 : lat_rows + 3, :]
    grad_features = jnp.concatenate(
        [inner[:, :, : lat_rows - 3, :], inner[:, :, lat_rows - 3 :, :] + back_rows], axis=2
    ).astype(jnp.bfloat16)
    (
        kernel_sum,
        dw_bias_sum,
        gain_sum,
        bias_sum,
        w_in_sum,
        b_in_sum,
        w_out_sum,
        b_out_sum,
        scale_sum,
    ) = grads
    lon_size = lax.axis_size("lon")
    big = (w_in_sum, w_out_sum, b_in_sum, b_out_sum, scale_sum, gain_sum, bias_sum)
    big_tot = unpack(
        halving_allreduce(pack(big, lon_size * 1024), "lon", jnp.bfloat16), big
    )
    small = (kernel_sum, dw_bias_sum)
    small_tot = unpack(butterfly_allreduce(pack(small, 128), "lon"), small)
    totals = (
        small_tot[0],
        small_tot[1],
        big_tot[5],
        big_tot[6],
        big_tot[0],
        big_tot[2],
        big_tot[1],
        big_tot[3],
        big_tot[4],
    )
    factor = 1.0 / math.sqrt(members * lat_rows * lon_dev * lax.axis_size("lon"))
    return (
        predicted,
        crps_field,
        grad_features,
        totals[0] * factor,
        totals[1] * factor,
        totals[2] * factor,
        totals[3] * factor,
        totals[4] * factor,
        totals[5] * factor,
        totals[6] * factor,
        totals[7] * factor,
        totals[8] * factor,
    )


def solution(mesh):
    placed = (
        P(None, ("groups", "lon"), None, None),
        P(("groups", "lon"), None, None),
        P(None, ("groups", "lon"), None, None),
        P(("groups", "lon"), None),
        P(),
        P(),
        P(),
        P(),
        P(),
        P(),
        P(),
        P(),
        P(),
    )
    return jax.shard_map(
        on_device,
        mesh=mesh,
        in_specs=placed,
        out_specs=(
            P(None, ("groups", "lon"), None, None),
            P(("groups", "lon"), None, None),
            P(None, ("groups", "lon"), None, None),
            P("groups", None, None),
            P("groups"),
            P("groups"),
            P("groups"),
            P("groups", None),
            P("groups"),
            P("groups", None),
            P("groups"),
            P("groups"),
        ),
        check_vma=False,
    )
```

```python
import math

import jax
import jax.numpy as jnp
from jax import lax
from jax.sharding import PartitionSpec as P

LEVELS = 19


SMOOTH = 0.25
EPSILON = 1e-06


def swapped(x, axis, bit):
    return lax.ppermute(x, axis, [(i, i ^ 1 << bit) for i in range(lax.axis_size(axis))])


def with_halo(x, sides, width):
    for axis, dim in sides:
        size, length = (lax.axis_size(axis), x.shape[dim])
        up = [(i, (i + 1) % size) for i in range(size)]
        down = [(j, i) for i, j in up]
        last = lax.slice_in_dim(x, length - width, length, axis=dim)
        leading = lax.slice_in_dim(x, 0, width, axis=dim)
        before = lax.ppermute(last, axis, up)
        after = lax.ppermute(leading, axis, down)
        x = jnp.concatenate([before, x, after], axis=dim)
    return x


def smooth_abs(value):
    return jnp.sqrt(value * value + SMOOTH * SMOOTH) - SMOOTH


def smooth_slope(value):
    return value / jnp.sqrt(value * value + SMOOTH * SMOOTH)


def local_step(
    extended,
    features,
    target,
    kmt,
    dw_kernel,
    dw_bias,
    ln_gain,
    ln_bias,
    w_in,
    b_in,
    w_out,
    b_out,
    layer_scale,
):
    members, lon_dev, lat_rows, chans = features.shape
    depth = jnp.zeros(features.shape, jnp.float32) + dw_bias
    for lon_off in range(7):
        for lat_off in range(7):
            depth = depth + dw_kernel[lon_off, lat_off] * extended[
                :, lon_off : lon_off + lon_dev, lat_off : lat_off + lat_rows, :
            ].astype(jnp.float32)
    mean_val = jnp.mean(depth, axis=-1, keepdims=True)
    centred = depth - mean_val
    variance = jnp.mean(centred * centred, axis=-1, keepdims=True)
    inv_std = lax.rsqrt(variance + EPSILON)
    unit = centred * inv_std
    normed = (unit * ln_gain + ln_bias).astype(jnp.bfloat16)
    level_of = jnp.arange(chans, dtype=jnp.int32) * LEVELS // chans
    wet_mask = (level_of[None, None, :] < kmt[:, :, None]).astype(jnp.float32)
    rows = lon_dev * lat_rows
    pre_acts = []
    hiddens = []
    outputs = []
    for member in range(members):
        flat_rows = normed[member].reshape(rows, chans)
        pre_act = jnp.dot(flat_rows, w_in, preferred_element_type=jnp.float32) + b_in
        hidden = jax.nn.gelu(pre_act).astype(jnp.bfloat16)
        pre_acts.append(pre_act)
        hiddens.append(hidden)
        outputs.append(
            (jnp.dot(hidden, w_out, preferred_element_type=jnp.float32) + b_out).reshape(
                lon_dev, lat_rows, chans
            )
        )
    branch = jnp.stack(outputs)
    pred = wet_mask * (features.astype(jnp.float32) + layer_scale * branch)
    target_full = target.astype(jnp.float32)
    pair_weight = 1.0 / (members * (members - 1))
    skill = jnp.zeros(target.shape, jnp.float32)
    spread = jnp.zeros(target.shape, jnp.float32)
    for member in range(members):
        skill = skill + smooth_abs(pred[member] - target_full)
        for other in range(member + 1, members):
            spread = spread + smooth_abs(pred[member] - pred[other])
    crps_field = wet_mask * (skill / members - pair_weight * spread)
    grad_list = []
    for member in range(members):
        slope_sum = jnp.zeros(target.shape, jnp.float32)
        for other in range(members):
            if other != member:
                slope_sum = slope_sum + smooth_slope(pred[member] - pred[other])
        grad_list.append(
            wet_mask
            * (smooth_slope(pred[member] - target_full) / members - pair_weight * slope_sum)
        )
    grad_pred = jnp.stack(grad_list)
    grad_scale = jnp.sum(grad_pred * branch, axis=(0, 1, 2))
    grad_b_out = jnp.zeros((chans,), jnp.float32)
    grad_w_out = jnp.zeros(w_out.shape, jnp.float32)
    grad_b_in = jnp.zeros(b_in.shape, jnp.float32)
    grad_w_in = jnp.zeros(w_in.shape, jnp.float32)
    normed_grads = []
    contract_rows = (((0,), (0,)), ((), ()))
    contract_cols = (((1,), (1,)), ((), ()))
    for member in range(members):
        grad_out = (grad_pred[member] * layer_scale).reshape(rows, chans)
        grad_b_out = grad_b_out + jnp.sum(grad_out, axis=0)
        out_half = grad_out.astype(jnp.bfloat16)
        grad_w_out = grad_w_out + lax.dot_general(
            hiddens[member], out_half, contract_rows, preferred_element_type=jnp.float32
        )
        grad_hidden = lax.dot_general(
            out_half, w_out, contract_cols, preferred_element_type=jnp.float32
        )
        grad_pre = jax.vjp(jax.nn.gelu, pre_acts[member])[1](grad_hidden)[0]
        grad_b_in = grad_b_in + jnp.sum(grad_pre, axis=0)
        pre_half = grad_pre.astype(jnp.bfloat16)
        grad_w_in = grad_w_in + lax.dot_general(
            normed[member].reshape(rows, chans),
            pre_half,
            contract_rows,
            preferred_element_type=jnp.float32,
        )
        normed_grads.append(
            lax.dot_general(
                pre_half, w_in, contract_cols, preferred_element_type=jnp.float32
            ).reshape(lon_dev, lat_rows, chans)
        )
    grad_normed = jnp.stack(normed_grads)
    grad_ln_gain = jnp.sum(grad_normed * unit, axis=(0, 1, 2))
    grad_ln_bias = jnp.sum(grad_normed, axis=(0, 1, 2))
    grad_unit = grad_normed * ln_gain
    grad_depth = inv_std * (
        grad_unit
        - jnp.mean(grad_unit, axis=-1, keepdims=True)
        - unit * jnp.mean(grad_unit * unit, axis=-1, keepdims=True)
    )
    grad_dw_bias = jnp.sum(grad_depth, axis=(0, 1, 2))
    kernel_rows = []
    for lon_off in range(7):
        kernel_cols = []
        for lat_off in range(7):
            kernel_cols.append(
                jnp.sum(
                    grad_depth
                    * extended[
                        :, lon_off : lon_off + lon_dev, lat_off : lat_off + lat_rows, :
                    ].astype(jnp.float32),
                    axis=(0, 1, 2),
                )
            )
        kernel_rows.append(jnp.stack(kernel_cols))
    grad_kernel = jnp.stack(kernel_rows)
    grads = (
        grad_kernel,
        grad_dw_bias,
        grad_ln_gain,
        grad_ln_bias,
        grad_w_in,
        grad_b_in,
        grad_w_out,
        grad_b_out,
        grad_scale,
    )
    return (pred.astype(jnp.bfloat16), crps_field, grad_pred, grad_depth, grads)


def mirrored(x, axis):
    size = lax.axis_size(axis)
    return lax.ppermute(x, axis, [(i, size - 1 - i) for i in range(size)])


def mirror_rows(top_rows):
    return mirrored(top_rows, "lon")[:, ::-1, ::-1, :]


def mirror_grads(fold_rows):
    picked = mirrored(fold_rows.astype(jnp.bfloat16), "lon").astype(fold_rows.dtype)
    return picked[:, ::-1, ::-1, :]


def halving_allreduce(flat, axis, gather_dtype, order):
    idx = lax.axis_index(axis)
    cur = flat
    for bit in order:
        half = cur.shape[0] // 2
        mine = (idx >> bit) & 1
        keep = lax.dynamic_slice_in_dim(cur, mine * half, half)
        send = lax.dynamic_slice_in_dim(cur, (1 - mine) * half, half)
        cur = keep + swapped(send, axis, bit)
    cur = cur.astype(gather_dtype)
    for bit in reversed(order):
        mine = (idx >> bit) & 1
        recv = swapped(cur, axis, bit)
        cur = jnp.where(mine == 0, jnp.concatenate([cur, recv]), jnp.concatenate([recv, cur]))
    return cur.astype(flat.dtype)


def split_allreduce(flat, axis, gather_dtype):
    bits = list(range(lax.axis_size(axis).bit_length() - 1))
    orders = [bits]
    if len(bits) > 2:
        orders.append([bits[0], bits[2], bits[1]] + bits[3:])
    length = flat.shape[0] // len(orders)
    parts = [
        halving_allreduce(flat[k * length : (k + 1) * length], axis, gather_dtype, order)
        for k, order in enumerate(orders)
    ]
    return jnp.concatenate(parts)


def butterfly_allreduce(flat, axis):
    for bit in range(lax.axis_size(axis).bit_length() - 1):
        flat = flat + swapped(flat, axis, bit)
    return flat


def pack(arrays, multiple):
    flat = jnp.concatenate([a.reshape(-1) for a in arrays])
    extra = -flat.shape[0] % multiple
    return jnp.pad(flat, (0, extra))


def unpack(flat, arrays):
    out, at = [], 0
    for a in arrays:
        out.append(flat[at : at + a.size].reshape(a.shape))
        at += a.size
    return out


def on_device(
    features,
    target,
    south_rim,
    kmt,
    dw_kernel,
    dw_bias,
    ln_gain,
    ln_bias,
    w_in,
    b_in,
    w_out,
    b_out,
    layer_scale,
):
    members, lon_dev, lat_rows, chans = features.shape
    params = (dw_kernel, dw_bias, ln_gain, ln_bias, w_in, b_in, w_out, b_out, layer_scale)
    north_rows = mirror_rows(features[:, :, lat_rows - 3 :, :])
    joined = jnp.concatenate([south_rim, features, north_rows], axis=2)
    extended = with_halo(joined, (("lon", 1),), 3)
    predicted, crps_field, grad_pred, grad_depth, grads = local_step(
        extended, features, target, kmt, *params
    )
    grad_halo = with_halo(grad_depth, (("lon", 1),), 3)
    padded = jnp.pad(grad_halo, ((0, 0), (0, 0), (6, 6), (0, 0)))
    grad_ext = jnp.zeros((members, lon_dev, lat_rows + 6, chans), jnp.float32)
    for lon_off in range(7):
        for lat_off in range(7):
            grad_ext = (
                grad_ext
                + dw_kernel[lon_off, lat_off]
                * padded[
                    :,
                    6 - lon_off : 6 - lon_off + lon_dev,
                    6 - lat_off : 6 - lat_off + lat_rows + 6,
                    :,
                ]
            )
    back_rows = mirror_grads(grad_ext[:, :, lat_rows + 3 :, :])
    inner = grad_pred + grad_ext[:, :, 3 : lat_rows + 3, :]
    grad_features = jnp.concatenate(
        [inner[:, :, : lat_rows - 3, :], inner[:, :, lat_rows - 3 :, :] + back_rows], axis=2
    ).astype(jnp.bfloat16)
    (
        kernel_sum,
        dw_bias_sum,
        gain_sum,
        bias_sum,
        w_in_sum,
        b_in_sum,
        w_out_sum,
        b_out_sum,
        scale_sum,
    ) = grads
    lon_size = lax.axis_size("lon")
    early = (w_out_sum, b_out_sum, scale_sum)
    early_tot = unpack(
        split_allreduce(pack(early, lon_size * 2048), "lon", jnp.bfloat16), early
    )
    late = (w_in_sum, b_in_sum, gain_sum, bias_sum)
    late_tot = unpack(split_allreduce(pack(late, lon_size * 2048), "lon", jnp.bfloat16), late)
    big_tot = (late_tot[0], early_tot[0], late_tot[1], early_tot[1], early_tot[2], late_tot[2], late_tot[3])
    small = (kernel_sum, dw_bias_sum)
    small_tot = unpack(butterfly_allreduce(pack(small, 128), "lon"), small)
    totals = (
        small_tot[0],
        small_tot[1],
        big_tot[5],
        big_tot[6],
        big_tot[0],
        big_tot[2],
        big_tot[1],
        big_tot[3],
        big_tot[4],
    )
    factor = 1.0 / math.sqrt(members * lat_rows * lon_dev * lax.axis_size("lon"))
    return (
        predicted,
        crps_field,
        grad_features,
        totals[0] * factor,
        totals[1] * factor,
        totals[2] * factor,
        totals[3] * factor,
        totals[4] * factor,
        totals[5] * factor,
        totals[6] * factor,
        totals[7] * factor,
        totals[8] * factor,
    )


def solution(mesh):
    placed = (
        P(None, ("groups", "lon"), None, None),
        P(("groups", "lon"), None, None),
        P(None, ("groups", "lon"), None, None),
        P(("groups", "lon"), None),
        P(),
        P(),
        P(),
        P(),
        P(),
        P(),
        P(),
        P(),
        P(),
    )
    return jax.shard_map(
        on_device,
        mesh=mesh,
        in_specs=placed,
        out_specs=(
            P(None, ("groups", "lon"), None, None),
            P(("groups", "lon"), None, None),
            P(None, ("groups", "lon"), None, None),
            P("groups", None, None),
            P("groups"),
            P("groups"),
            P("groups"),
            P("groups", None),
            P("groups"),
            P("groups", None),
            P("groups"),
            P("groups"),
        ),
        check_vma=False,
    )
```

```python
import math

import jax
import jax.numpy as jnp
from jax import lax
from jax.sharding import PartitionSpec as P

LEVELS = 19


SMOOTH = 0.25
EPSILON = 1e-06


def swapped(x, axis, bit):
    return lax.ppermute(x, axis, [(i, i ^ 1 << bit) for i in range(lax.axis_size(axis))])


def with_halo(x, sides, width):
    for axis, dim in sides:
        size, length = (lax.axis_size(axis), x.shape[dim])
        up = [(i, (i + 1) % size) for i in range(size)]
        down = [(j, i) for i, j in up]
        last = lax.slice_in_dim(x, length - width, length, axis=dim)
        leading = lax.slice_in_dim(x, 0, width, axis=dim)
        before = lax.ppermute(last, axis, up)
        after = lax.ppermute(leading, axis, down)
        x = jnp.concatenate([before, x, after], axis=dim)
    return x


def smooth_abs(value):
    return jnp.sqrt(value * value + SMOOTH * SMOOTH) - SMOOTH


def smooth_slope(value):
    return value / jnp.sqrt(value * value + SMOOTH * SMOOTH)


def local_step(
    extended,
    features,
    target,
    kmt,
    dw_kernel,
    dw_bias,
    ln_gain,
    ln_bias,
    w_in,
    b_in,
    w_out,
    b_out,
    layer_scale,
):
    members, lon_dev, lat_rows, chans = features.shape
    depth = jnp.zeros(features.shape, jnp.float32) + dw_bias
    for lon_off in range(7):
        for lat_off in range(7):
            depth = depth + dw_kernel[lon_off, lat_off] * extended[
                :, lon_off : lon_off + lon_dev, lat_off : lat_off + lat_rows, :
            ].astype(jnp.float32)
    mean_val = jnp.mean(depth, axis=-1, keepdims=True)
    centred = depth - mean_val
    variance = jnp.mean(centred * centred, axis=-1, keepdims=True)
    inv_std = lax.rsqrt(variance + EPSILON)
    unit = centred * inv_std
    normed = (unit * ln_gain + ln_bias).astype(jnp.bfloat16)
    level_of = jnp.arange(chans, dtype=jnp.int32) * LEVELS // chans
    wet_mask = (level_of[None, None, :] < kmt[:, :, None]).astype(jnp.float32)
    rows = lon_dev * lat_rows
    pre_acts = []
    hiddens = []
    outputs = []
    for member in range(members):
        flat_rows = normed[member].reshape(rows, chans)
        pre_act = jnp.dot(flat_rows, w_in, preferred_element_type=jnp.float32) + b_in
        hidden = jax.nn.gelu(pre_act).astype(jnp.bfloat16)
        pre_acts.append(pre_act)
        hiddens.append(hidden)
        outputs.append(
            (jnp.dot(hidden, w_out, preferred_element_type=jnp.float32) + b_out).reshape(
                lon_dev, lat_rows, chans
            )
        )
    branch = jnp.stack(outputs)
    pred = wet_mask * (features.astype(jnp.float32) + layer_scale * branch)
    target_full = target.astype(jnp.float32)
    pair_weight = 1.0 / (members * (members - 1))
    skill = jnp.zeros(target.shape, jnp.float32)
    spread = jnp.zeros(target.shape, jnp.float32)
    for member in range(members):
        skill = skill + smooth_abs(pred[member] - target_full)
        for other in range(member + 1, members):
            spread = spread + smooth_abs(pred[member] - pred[other])
    crps_field = wet_mask * (skill / members - pair_weight * spread)
    grad_list = []
    for member in range(members):
        slope_sum = jnp.zeros(target.shape, jnp.float32)
        for other in range(members):
            if other != member:
                slope_sum = slope_sum + smooth_slope(pred[member] - pred[other])
        grad_list.append(
            wet_mask
            * (smooth_slope(pred[member] - target_full) / members - pair_weight * slope_sum)
        )
    grad_pred = jnp.stack(grad_list)
    grad_scale = jnp.sum(grad_pred * branch, axis=(0, 1, 2))
    grad_b_out = jnp.zeros((chans,), jnp.float32)
    grad_w_out = jnp.zeros(w_out.shape, jnp.float32)
    grad_b_in = jnp.zeros(b_in.shape, jnp.float32)
    grad_w_in = jnp.zeros(w_in.shape, jnp.float32)
    normed_grads = []
    contract_rows = (((0,), (0,)), ((), ()))
    contract_cols = (((1,), (1,)), ((), ()))
    for member in range(members):
        grad_out = (grad_pred[member] * layer_scale).reshape(rows, chans)
        grad_b_out = grad_b_out + jnp.sum(grad_out, axis=0)
        out_half = grad_out.astype(jnp.bfloat16)
        grad_w_out = grad_w_out + lax.dot_general(
            hiddens[member], out_half, contract_rows, preferred_element_type=jnp.float32
        )
        grad_hidden = lax.dot_general(
            out_half, w_out, contract_cols, preferred_element_type=jnp.float32
        )
        grad_pre = jax.vjp(jax.nn.gelu, pre_acts[member])[1](grad_hidden)[0]
        grad_b_in = grad_b_in + jnp.sum(grad_pre, axis=0)
        pre_half = grad_pre.astype(jnp.bfloat16)
        grad_w_in = grad_w_in + lax.dot_general(
            normed[member].reshape(rows, chans),
            pre_half,
            contract_rows,
            preferred_element_type=jnp.float32,
        )
        normed_grads.append(
            lax.dot_general(
                pre_half, w_in, contract_cols, preferred_element_type=jnp.float32
            ).reshape(lon_dev, lat_rows, chans)
        )
    grad_normed = jnp.stack(normed_grads)
    grad_ln_gain = jnp.sum(grad_normed * unit, axis=(0, 1, 2))
    grad_ln_bias = jnp.sum(grad_normed, axis=(0, 1, 2))
    grad_unit = grad_normed * ln_gain
    grad_depth = inv_std * (
        grad_unit
        - jnp.mean(grad_unit, axis=-1, keepdims=True)
        - unit * jnp.mean(grad_unit * unit, axis=-1, keepdims=True)
    )
    grad_dw_bias = jnp.sum(grad_depth, axis=(0, 1, 2))
    kernel_rows = []
    for lon_off in range(7):
        kernel_cols = []
        for lat_off in range(7):
            kernel_cols.append(
                jnp.sum(
                    grad_depth
                    * extended[
                        :, lon_off : lon_off + lon_dev, lat_off : lat_off + lat_rows, :
                    ].astype(jnp.float32),
                    axis=(0, 1, 2),
                )
            )
        kernel_rows.append(jnp.stack(kernel_cols))
    grad_kernel = jnp.stack(kernel_rows)
    grads = (
        grad_kernel,
        grad_dw_bias,
        grad_ln_gain,
        grad_ln_bias,
        grad_w_in,
        grad_b_in,
        grad_w_out,
        grad_b_out,
        grad_scale,
    )
    return (pred.astype(jnp.bfloat16), crps_field, grad_pred, grad_depth, grads)


def mirrored(x, axis):
    size = lax.axis_size(axis)
    return lax.ppermute(x, axis, [(i, size - 1 - i) for i in range(size)])


def mirror_rows(top_rows):
    return mirrored(top_rows, "lon")[:, ::-1, ::-1, :]


def mirror_grads(fold_rows):
    picked = mirrored(fold_rows.astype(jnp.bfloat16), "lon").astype(fold_rows.dtype)
    return picked[:, ::-1, ::-1, :]


def halving_allreduce(flat, axis, gather_dtype, order):
    idx = lax.axis_index(axis)
    cur = flat
    for bit in order:
        half = cur.shape[0] // 2
        mine = (idx >> bit) & 1
        keep = lax.dynamic_slice_in_dim(cur, mine * half, half)
        send = lax.dynamic_slice_in_dim(cur, (1 - mine) * half, half)
        cur = keep + swapped(send, axis, bit)
    cur = cur.astype(gather_dtype)
    for bit in reversed(order):
        mine = (idx >> bit) & 1
        recv = swapped(cur, axis, bit)
        cur = jnp.where(mine == 0, jnp.concatenate([cur, recv]), jnp.concatenate([recv, cur]))
    return cur.astype(flat.dtype)


def split_allreduce(flat, axis, gather_dtype):
    bits = list(range(lax.axis_size(axis).bit_length() - 1))
    orders = [bits]
    if len(bits) > 2:
        orders.append([bits[0], bits[2], bits[1]] + bits[3:])
    length = flat.shape[0] // len(orders)
    parts = [
        halving_allreduce(flat[k * length : (k + 1) * length], axis, gather_dtype, order)
        for k, order in enumerate(orders)
    ]
    return jnp.concatenate(parts)


def butterfly_allreduce(flat, axis):
    for bit in range(lax.axis_size(axis).bit_length() - 1):
        flat = flat + swapped(flat, axis, bit)
    return flat


def pack(arrays, multiple):
    flat = jnp.concatenate([a.reshape(-1) for a in arrays])
    extra = -flat.shape[0] % multiple
    return jnp.pad(flat, (0, extra))


def unpack(flat, arrays):
    out, at = [], 0
    for a in arrays:
        out.append(flat[at : at + a.size].reshape(a.shape))
        at += a.size
    return out


def on_device(
    features,
    target,
    south_rim,
    kmt,
    dw_kernel,
    dw_bias,
    ln_gain,
    ln_bias,
    w_in,
    b_in,
    w_out,
    b_out,
    layer_scale,
):
    members, lon_dev, lat_rows, chans = features.shape
    params = (dw_kernel, dw_bias, ln_gain, ln_bias, w_in, b_in, w_out, b_out, layer_scale)
    top_rows = features[:, :, lat_rows - 3 :, :]
    north_rows = mirror_rows(top_rows)
    joined = jnp.concatenate([south_rim, features], axis=2)
    lon_size = lax.axis_size("lon")
    before = lax.ppermute(
        joined[:, lon_dev - 3 :], "lon", [(i, (i + 1) % lon_size) for i in range(lon_size)]
    )
    after = lax.ppermute(
        joined[:, :3], "lon", [((i + 1) % lon_size, i) for i in range(lon_size)]
    )
    north_before = lax.ppermute(
        top_rows[:, :3], "lon", [(i, (lon_size - i) % lon_size) for i in range(lon_size)]
    )[:, ::-1, ::-1, :]
    north_after = lax.ppermute(
        top_rows[:, lon_dev - 3 :],
        "lon",
        [(i, (2 * lon_size - 2 - i) % lon_size) for i in range(lon_size)],
    )[:, ::-1, ::-1, :]
    extended = jnp.concatenate(
        [
            jnp.concatenate([before, north_before], axis=2),
            jnp.concatenate([joined, north_rows], axis=2),
            jnp.concatenate([after, north_after], axis=2),
        ],
        axis=1,
    )
    predicted, crps_field, grad_pred, grad_depth, grads = local_step(
        extended, features, target, kmt, *params
    )
    grad_halo = with_halo(grad_depth, (("lon", 1),), 3)
    padded = jnp.pad(grad_halo, ((0, 0), (0, 0), (6, 6), (0, 0)))
    grad_ext = jnp.zeros((members, lon_dev, lat_rows + 6, chans), jnp.float32)
    for lon_off in range(7):
        for lat_off in range(7):
            grad_ext = (
                grad_ext
                + dw_kernel[lon_off, lat_off]
                * padded[
                    :,
                    6 - lon_off : 6 - lon_off + lon_dev,
                    6 - lat_off : 6 - lat_off + lat_rows + 6,
                    :,
                ]
            )
    back_rows = mirror_grads(grad_ext[:, :, lat_rows + 3 :, :])
    inner = grad_pred + grad_ext[:, :, 3 : lat_rows + 3, :]
    grad_features = jnp.concatenate(
        [inner[:, :, : lat_rows - 3, :], inner[:, :, lat_rows - 3 :, :] + back_rows], axis=2
    ).astype(jnp.bfloat16)
    (
        kernel_sum,
        dw_bias_sum,
        gain_sum,
        bias_sum,
        w_in_sum,
        b_in_sum,
        w_out_sum,
        b_out_sum,
        scale_sum,
    ) = grads
    lon_size = lax.axis_size("lon")
    big = (w_in_sum, w_out_sum, b_in_sum, b_out_sum, scale_sum, gain_sum, bias_sum)
    big_tot = unpack(split_allreduce(pack(big, lon_size * 2048), "lon", jnp.bfloat16), big)
    small = (kernel_sum, dw_bias_sum)
    small_tot = unpack(butterfly_allreduce(pack(small, 128), "lon"), small)
    totals = (
        small_tot[0],
        small_tot[1],
        big_tot[5],
        big_tot[6],
        big_tot[0],
        big_tot[2],
        big_tot[1],
        big_tot[3],
        big_tot[4],
    )
    factor = 1.0 / math.sqrt(members * lat_rows * lon_dev * lax.axis_size("lon"))
    return (
        predicted,
        crps_field,
        grad_features,
        totals[0] * factor,
        totals[1] * factor,
        totals[2] * factor,
        totals[3] * factor,
        totals[4] * factor,
        totals[5] * factor,
        totals[6] * factor,
        totals[7] * factor,
        totals[8] * factor,
    )


def solution(mesh):
    placed = (
        P(None, ("groups", "lon"), None, None),
        P(("groups", "lon"), None, None),
        P(None, ("groups", "lon"), None, None),
        P(("groups", "lon"), None),
        P(),
        P(),
        P(),
        P(),
        P(),
        P(),
        P(),
        P(),
        P(),
    )
    return jax.shard_map(
        on_device,
        mesh=mesh,
        in_specs=placed,
        out_specs=(
            P(None, ("groups", "lon"), None, None),
            P(("groups", "lon"), None, None),
            P(None, ("groups", "lon"), None, None),
            P("groups", None, None),
            P("groups"),
            P("groups"),
            P("groups"),
            P("groups", None),
            P("groups"),
            P("groups", None),
            P("groups"),
            P("groups"),
        ),
        check_vma=False,
    )
```

```python
import math

import jax
import jax.numpy as jnp
from jax import lax
from jax.sharding import PartitionSpec as P

LEVELS = 19


SMOOTH = 0.25
EPSILON = 1e-06


def swapped(x, axis, bit):
    return lax.ppermute(x, axis, [(i, i ^ 1 << bit) for i in range(lax.axis_size(axis))])


def with_halo(x, sides, width):
    for axis, dim in sides:
        size, length = (lax.axis_size(axis), x.shape[dim])
        up = [(i, (i + 1) % size) for i in range(size)]
        down = [(j, i) for i, j in up]
        last = lax.slice_in_dim(x, length - width, length, axis=dim)
        leading = lax.slice_in_dim(x, 0, width, axis=dim)
        before = lax.ppermute(last, axis, up)
        after = lax.ppermute(leading, axis, down)
        x = jnp.concatenate([before, x, after], axis=dim)
    return x


def smooth_abs(value):
    return jnp.sqrt(value * value + SMOOTH * SMOOTH) - SMOOTH


def smooth_slope(value):
    return value / jnp.sqrt(value * value + SMOOTH * SMOOTH)


def local_step(
    extended,
    features,
    target,
    kmt,
    dw_kernel,
    dw_bias,
    ln_gain,
    ln_bias,
    w_in,
    b_in,
    w_out,
    b_out,
    layer_scale,
):
    members, lon_dev, lat_rows, chans = features.shape
    depth = jnp.zeros(features.shape, jnp.float32) + dw_bias
    for lon_off in range(7):
        for lat_off in range(7):
            depth = depth + dw_kernel[lon_off, lat_off] * extended[
                :, lon_off : lon_off + lon_dev, lat_off : lat_off + lat_rows, :
            ].astype(jnp.float32)
    mean_val = jnp.mean(depth, axis=-1, keepdims=True)
    centred = depth - mean_val
    variance = jnp.mean(centred * centred, axis=-1, keepdims=True)
    inv_std = lax.rsqrt(variance + EPSILON)
    unit = centred * inv_std
    normed = (unit * ln_gain + ln_bias).astype(jnp.bfloat16)
    level_of = jnp.arange(chans, dtype=jnp.int32) * LEVELS // chans
    wet_mask = (level_of[None, None, :] < kmt[:, :, None]).astype(jnp.float32)
    rows = lon_dev * lat_rows
    pre_acts = []
    hiddens = []
    outputs = []
    for member in range(members):
        flat_rows = normed[member].reshape(rows, chans)
        pre_act = jnp.dot(flat_rows, w_in, preferred_element_type=jnp.float32) + b_in
        hidden = jax.nn.gelu(pre_act).astype(jnp.bfloat16)
        pre_acts.append(pre_act)
        hiddens.append(hidden)
        outputs.append(
            (jnp.dot(hidden, w_out, preferred_element_type=jnp.float32) + b_out).reshape(
                lon_dev, lat_rows, chans
            )
        )
    branch = jnp.stack(outputs)
    pred = wet_mask * (features.astype(jnp.float32) + layer_scale * branch)
    target_full = target.astype(jnp.float32)
    pair_weight = 1.0 / (members * (members - 1))
    skill = jnp.zeros(target.shape, jnp.float32)
    spread = jnp.zeros(target.shape, jnp.float32)
    for member in range(members):
        skill = skill + smooth_abs(pred[member] - target_full)
        for other in range(member + 1, members):
            spread = spread + smooth_abs(pred[member] - pred[other])
    crps_field = wet_mask * (skill / members - pair_weight * spread)
    grad_list = []
    for member in range(members):
        slope_sum = jnp.zeros(target.shape, jnp.float32)
        for other in range(members):
            if other != member:
                slope_sum = slope_sum + smooth_slope(pred[member] - pred[other])
        grad_list.append(
            wet_mask
            * (smooth_slope(pred[member] - target_full) / members - pair_weight * slope_sum)
        )
    grad_pred = jnp.stack(grad_list)
    grad_scale = jnp.sum(grad_pred * branch, axis=(0, 1, 2))
    grad_b_out = jnp.zeros((chans,), jnp.float32)
    grad_w_out = jnp.zeros(w_out.shape, jnp.float32)
    grad_b_in = jnp.zeros(b_in.shape, jnp.float32)
    grad_w_in = jnp.zeros(w_in.shape, jnp.float32)
    normed_grads = []
    contract_rows = (((0,), (0,)), ((), ()))
    contract_cols = (((1,), (1,)), ((), ()))
    for member in range(members):
        grad_out = (grad_pred[member] * layer_scale).reshape(rows, chans)
        grad_b_out = grad_b_out + jnp.sum(grad_out, axis=0)
        out_half = grad_out.astype(jnp.bfloat16)
        grad_w_out = grad_w_out + lax.dot_general(
            hiddens[member], out_half, contract_rows, preferred_element_type=jnp.float32
        )
        grad_hidden = lax.dot_general(
            out_half, w_out, contract_cols, preferred_element_type=jnp.float32
        )
        grad_pre = jax.vjp(jax.nn.gelu, pre_acts[member])[1](grad_hidden)[0]
        grad_b_in = grad_b_in + jnp.sum(grad_pre, axis=0)
        pre_half = grad_pre.astype(jnp.bfloat16)
        grad_w_in = grad_w_in + lax.dot_general(
            normed[member].reshape(rows, chans),
            pre_half,
            contract_rows,
            preferred_element_type=jnp.float32,
        )
        normed_grads.append(
            lax.dot_general(
                pre_half, w_in, contract_cols, preferred_element_type=jnp.float32
            ).reshape(lon_dev, lat_rows, chans)
        )
    grad_normed = jnp.stack(normed_grads)
    grad_ln_gain = jnp.sum(grad_normed * unit, axis=(0, 1, 2))
    grad_ln_bias = jnp.sum(grad_normed, axis=(0, 1, 2))
    grad_unit = grad_normed * ln_gain
    grad_depth = inv_std * (
        grad_unit
        - jnp.mean(grad_unit, axis=-1, keepdims=True)
        - unit * jnp.mean(grad_unit * unit, axis=-1, keepdims=True)
    )
    grad_dw_bias = jnp.sum(grad_depth, axis=(0, 1, 2))
    kernel_rows = []
    for lon_off in range(7):
        kernel_cols = []
        for lat_off in range(7):
            kernel_cols.append(
                jnp.sum(
                    grad_depth
                    * extended[
                        :, lon_off : lon_off + lon_dev, lat_off : lat_off + lat_rows, :
                    ].astype(jnp.float32),
                    axis=(0, 1, 2),
                )
            )
        kernel_rows.append(jnp.stack(kernel_cols))
    grad_kernel = jnp.stack(kernel_rows)
    grads = (
        grad_kernel,
        grad_dw_bias,
        grad_ln_gain,
        grad_ln_bias,
        grad_w_in,
        grad_b_in,
        grad_w_out,
        grad_b_out,
        grad_scale,
    )
    return (pred.astype(jnp.bfloat16), crps_field, grad_pred, grad_depth, grads)


def mirrored(x, axis):
    size = lax.axis_size(axis)
    return lax.ppermute(x, axis, [(i, size - 1 - i) for i in range(size)])


def mirror_rows(top_rows):
    return mirrored(top_rows, "lon")[:, ::-1, ::-1, :]


def mirror_grads(fold_rows):
    picked = mirrored(fold_rows.astype(jnp.bfloat16), "lon").astype(fold_rows.dtype)
    return picked[:, ::-1, ::-1, :]


def halving_allreduce(flat, axis, gather_dtype):
    size = lax.axis_size(axis)
    bits = size.bit_length() - 1
    idx = lax.axis_index(axis)
    cur = flat
    for bit in range(bits):
        half = cur.shape[0] // 2
        mine = (idx >> bit) & 1
        keep = lax.dynamic_slice_in_dim(cur, mine * half, half)
        send = lax.dynamic_slice_in_dim(cur, (1 - mine) * half, half)
        cur = keep + swapped(send, axis, bit)
    cur = cur.astype(gather_dtype)
    for bit in reversed(range(bits)):
        mine = (idx >> bit) & 1
        recv = swapped(cur, axis, bit)
        cur = jnp.where(mine == 0, jnp.concatenate([cur, recv]), jnp.concatenate([recv, cur]))
    return cur.astype(flat.dtype)


def radix_allreduce(flat, axis, gather_dtype):
    size = lax.axis_size(axis)
    nbits = size.bit_length() - 1
    groups = [list(range(b, min(b + 2, nbits))) for b in range(0, nbits, 2)]
    idx = lax.axis_index(axis)
    cur = flat
    for bits in groups:
        radix, low = 1 << len(bits), bits[0]
        sub = (idx >> low) & (radix - 1)
        part = cur.shape[0] // radix
        total = lax.dynamic_slice_in_dim(cur, sub * part, part)
        for d in range(1, radix):
            send = lax.dynamic_slice_in_dim(cur, (sub ^ d) * part, part)
            total = total + lax.ppermute(send, axis, [(i, i ^ (d << low)) for i in range(size)])
        cur = total
    cur = cur.astype(gather_dtype)
    for bits in reversed(groups):
        radix, low = 1 << len(bits), bits[0]
        sub = (idx >> low) & (radix - 1)
        part = cur.shape[0]
        full = lax.dynamic_update_slice_in_dim(
            jnp.zeros((part * radix,), cur.dtype), cur, sub * part, 0
        )
        for d in range(1, radix):
            recv = lax.ppermute(cur, axis, [(i, i ^ (d << low)) for i in range(size)])
            full = lax.dynamic_update_slice_in_dim(full, recv, (sub ^ d) * part, 0)
        cur = full
    return cur.astype(flat.dtype)


def butterfly_allreduce(flat, axis):
    for bit in range(lax.axis_size(axis).bit_length() - 1):
        flat = flat + swapped(flat, axis, bit)
    return flat


def pack(arrays, multiple):
    flat = jnp.concatenate([a.reshape(-1) for a in arrays])
    extra = -flat.shape[0] % multiple
    return jnp.pad(flat, (0, extra))


def unpack(flat, arrays):
    out, at = [], 0
    for a in arrays:
        out.append(flat[at : at + a.size].reshape(a.shape))
        at += a.size
    return out


def on_device(
    features,
    target,
    south_rim,
    kmt,
    dw_kernel,
    dw_bias,
    ln_gain,
    ln_bias,
    w_in,
    b_in,
    w_out,
    b_out,
    layer_scale,
):
    members, lon_dev, lat_rows, chans = features.shape
    params = (dw_kernel, dw_bias, ln_gain, ln_bias, w_in, b_in, w_out, b_out, layer_scale)
    north_rows = mirror_rows(features[:, :, lat_rows - 3 :, :])
    joined = jnp.concatenate([south_rim, features, north_rows], axis=2)
    extended = with_halo(joined, (("lon", 1),), 3)
    predicted, crps_field, grad_pred, grad_depth, grads = local_step(
        extended, features, target, kmt, *params
    )
    grad_halo = with_halo(grad_depth, (("lon", 1),), 3)
    padded = jnp.pad(grad_halo, ((0, 0), (0, 0), (6, 6), (0, 0)))
    grad_ext = jnp.zeros((members, lon_dev, lat_rows + 6, chans), jnp.float32)
    for lon_off in range(7):
        for lat_off in range(7):
            grad_ext = (
                grad_ext
                + dw_kernel[lon_off, lat_off]
                * padded[
                    :,
                    6 - lon_off : 6 - lon_off + lon_dev,
                    6 - lat_off : 6 - lat_off + lat_rows + 6,
                    :,
                ]
            )
    back_rows = mirror_grads(grad_ext[:, :, lat_rows + 3 :, :])
    inner = grad_pred + grad_ext[:, :, 3 : lat_rows + 3, :]
    grad_features = jnp.concatenate(
        [inner[:, :, : lat_rows - 3, :], inner[:, :, lat_rows - 3 :, :] + back_rows], axis=2
    ).astype(jnp.bfloat16)
    (
        kernel_sum,
        dw_bias_sum,
        gain_sum,
        bias_sum,
        w_in_sum,
        b_in_sum,
        w_out_sum,
        b_out_sum,
        scale_sum,
    ) = grads
    lon_size = lax.axis_size("lon")
    sums = (
        kernel_sum,
        dw_bias_sum,
        gain_sum,
        bias_sum,
        w_in_sum,
        b_in_sum,
        w_out_sum,
        b_out_sum,
        scale_sum,
    )
    totals = unpack(radix_allreduce(pack(sums, lon_size * 1024), "lon", jnp.bfloat16), sums)
    factor = 1.0 / math.sqrt(members * lat_rows * lon_dev * lax.axis_size("lon"))
    return (
        predicted,
        crps_field,
        grad_features,
        totals[0] * factor,
        totals[1] * factor,
        totals[2] * factor,
        totals[3] * factor,
        totals[4] * factor,
        totals[5] * factor,
        totals[6] * factor,
        totals[7] * factor,
        totals[8] * factor,
    )


def solution(mesh):
    placed = (
        P(None, ("groups", "lon"), None, None),
        P(("groups", "lon"), None, None),
        P(None, ("groups", "lon"), None, None),
        P(("groups", "lon"), None),
        P(),
        P(),
        P(),
        P(),
        P(),
        P(),
        P(),
        P(),
        P(),
    )
    return jax.shard_map(
        on_device,
        mesh=mesh,
        in_specs=placed,
        out_specs=(
            P(None, ("groups", "lon"), None, None),
            P(("groups", "lon"), None, None),
            P(None, ("groups", "lon"), None, None),
            P("groups", None, None),
            P("groups"),
            P("groups"),
            P("groups"),
            P("groups", None),
            P("groups"),
            P("groups", None),
            P("groups"),
            P("groups"),
        ),
        check_vma=False,
    )
```

```python
import math

import jax
import jax.numpy as jnp
from jax import lax
from jax.sharding import PartitionSpec as P

LEVELS = 19


SMOOTH = 0.25
EPSILON = 1e-06


def swapped(x, axis, bit):
    return lax.ppermute(x, axis, [(i, i ^ 1 << bit) for i in range(lax.axis_size(axis))])


def with_halo(x, sides, width):
    for axis, dim in sides:
        size, length = (lax.axis_size(axis), x.shape[dim])
        up = [(i, (i + 1) % size) for i in range(size)]
        down = [(j, i) for i, j in up]
        last = lax.slice_in_dim(x, length - width, length, axis=dim)
        leading = lax.slice_in_dim(x, 0, width, axis=dim)
        before = lax.ppermute(last, axis, up)
        after = lax.ppermute(leading, axis, down)
        x = jnp.concatenate([before, x, after], axis=dim)
    return x


def smooth_abs(value):
    return jnp.sqrt(value * value + SMOOTH * SMOOTH) - SMOOTH


def smooth_slope(value):
    return value / jnp.sqrt(value * value + SMOOTH * SMOOTH)


def local_step(
    extended,
    features,
    target,
    kmt,
    dw_kernel,
    dw_bias,
    ln_gain,
    ln_bias,
    w_in,
    b_in,
    w_out,
    b_out,
    layer_scale,
):
    members, lon_dev, lat_rows, chans = features.shape
    depth = jnp.zeros(features.shape, jnp.float32) + dw_bias
    for lon_off in range(7):
        for lat_off in range(7):
            depth = depth + dw_kernel[lon_off, lat_off] * extended[
                :, lon_off : lon_off + lon_dev, lat_off : lat_off + lat_rows, :
            ].astype(jnp.float32)
    mean_val = jnp.mean(depth, axis=-1, keepdims=True)
    centred = depth - mean_val
    variance = jnp.mean(centred * centred, axis=-1, keepdims=True)
    inv_std = lax.rsqrt(variance + EPSILON)
    unit = centred * inv_std
    normed = (unit * ln_gain + ln_bias).astype(jnp.bfloat16)
    level_of = jnp.arange(chans, dtype=jnp.int32) * LEVELS // chans
    wet_mask = (level_of[None, None, :] < kmt[:, :, None]).astype(jnp.float32)
    rows = lon_dev * lat_rows
    pre_acts = []
    hiddens = []
    outputs = []
    for member in range(members):
        flat_rows = normed[member].reshape(rows, chans)
        pre_act = jnp.dot(flat_rows, w_in, preferred_element_type=jnp.float32) + b_in
        hidden = jax.nn.gelu(pre_act).astype(jnp.bfloat16)
        pre_acts.append(pre_act)
        hiddens.append(hidden)
        outputs.append(
            (jnp.dot(hidden, w_out, preferred_element_type=jnp.float32) + b_out).reshape(
                lon_dev, lat_rows, chans
            )
        )
    branch = jnp.stack(outputs)
    pred = wet_mask * (features.astype(jnp.float32) + layer_scale * branch)
    target_full = target.astype(jnp.float32)
    pair_weight = 1.0 / (members * (members - 1))
    skill = jnp.zeros(target.shape, jnp.float32)
    spread = jnp.zeros(target.shape, jnp.float32)
    for member in range(members):
        skill = skill + smooth_abs(pred[member] - target_full)
        for other in range(member + 1, members):
            spread = spread + smooth_abs(pred[member] - pred[other])
    crps_field = wet_mask * (skill / members - pair_weight * spread)
    grad_list = []
    for member in range(members):
        slope_sum = jnp.zeros(target.shape, jnp.float32)
        for other in range(members):
            if other != member:
                slope_sum = slope_sum + smooth_slope(pred[member] - pred[other])
        grad_list.append(
            wet_mask
            * (smooth_slope(pred[member] - target_full) / members - pair_weight * slope_sum)
        )
    grad_pred = jnp.stack(grad_list)
    grad_scale = jnp.sum(grad_pred * branch, axis=(0, 1, 2))
    grad_b_out = jnp.zeros((chans,), jnp.float32)
    grad_w_out = jnp.zeros(w_out.shape, jnp.float32)
    grad_b_in = jnp.zeros(b_in.shape, jnp.float32)
    grad_w_in = jnp.zeros(w_in.shape, jnp.float32)
    normed_grads = []
    contract_rows = (((0,), (0,)), ((), ()))
    contract_cols = (((1,), (1,)), ((), ()))
    for member in range(members):
        grad_out = (grad_pred[member] * layer_scale).reshape(rows, chans)
        grad_b_out = grad_b_out + jnp.sum(grad_out, axis=0)
        out_half = grad_out.astype(jnp.bfloat16)
        grad_w_out = grad_w_out + lax.dot_general(
            hiddens[member], out_half, contract_rows, preferred_element_type=jnp.float32
        )
        grad_hidden = lax.dot_general(
            out_half, w_out, contract_cols, preferred_element_type=jnp.float32
        )
        grad_pre = jax.vjp(jax.nn.gelu, pre_acts[member])[1](grad_hidden)[0]
        grad_b_in = grad_b_in + jnp.sum(grad_pre, axis=0)
        pre_half = grad_pre.astype(jnp.bfloat16)
        grad_w_in = grad_w_in + lax.dot_general(
            normed[member].reshape(rows, chans),
            pre_half,
            contract_rows,
            preferred_element_type=jnp.float32,
        )
        normed_grads.append(
            lax.dot_general(
                pre_half, w_in, contract_cols, preferred_element_type=jnp.float32
            ).reshape(lon_dev, lat_rows, chans)
        )
    grad_normed = jnp.stack(normed_grads)
    grad_ln_gain = jnp.sum(grad_normed * unit, axis=(0, 1, 2))
    grad_ln_bias = jnp.sum(grad_normed, axis=(0, 1, 2))
    grad_unit = grad_normed * ln_gain
    grad_depth = inv_std * (
        grad_unit
        - jnp.mean(grad_unit, axis=-1, keepdims=True)
        - unit * jnp.mean(grad_unit * unit, axis=-1, keepdims=True)
    )
    grad_dw_bias = jnp.sum(grad_depth, axis=(0, 1, 2))
    kernel_rows = []
    for lon_off in range(7):
        kernel_cols = []
        for lat_off in range(7):
            kernel_cols.append(
                jnp.sum(
                    grad_depth
                    * extended[
                        :, lon_off : lon_off + lon_dev, lat_off : lat_off + lat_rows, :
                    ].astype(jnp.float32),
                    axis=(0, 1, 2),
                )
            )
        kernel_rows.append(jnp.stack(kernel_cols))
    grad_kernel = jnp.stack(kernel_rows)
    grads = (
        grad_kernel,
        grad_dw_bias,
        grad_ln_gain,
        grad_ln_bias,
        grad_w_in,
        grad_b_in,
        grad_w_out,
        grad_b_out,
        grad_scale,
    )
    return (pred.astype(jnp.bfloat16), crps_field, grad_pred, grad_depth, grads)


def mirrored(x, axis):
    size = lax.axis_size(axis)
    return lax.ppermute(x, axis, [(i, size - 1 - i) for i in range(size)])


def mirror_rows(top_rows):
    return mirrored(top_rows, "lon")[:, ::-1, ::-1, :]


def mirror_grads(fold_rows):
    picked = mirrored(fold_rows.astype(jnp.bfloat16), "lon").astype(fold_rows.dtype)
    return picked[:, ::-1, ::-1, :]


def halving_allreduce(flat, axis, gather_dtype):
    size = lax.axis_size(axis)
    bits = size.bit_length() - 1
    idx = lax.axis_index(axis)
    cur = flat
    for bit in range(bits):
        half = cur.shape[0] // 2
        mine = (idx >> bit) & 1
        keep = lax.dynamic_slice_in_dim(cur, mine * half, half)
        send = lax.dynamic_slice_in_dim(cur, (1 - mine) * half, half)
        cur = keep + swapped(send, axis, bit)
    cur = cur.astype(gather_dtype)
    for bit in reversed(range(bits)):
        mine = (idx >> bit) & 1
        recv = swapped(cur, axis, bit)
        cur = jnp.where(mine == 0, jnp.concatenate([cur, recv]), jnp.concatenate([recv, cur]))
    return cur.astype(flat.dtype)


def radix_allreduce(flat, axis, gather_dtype):
    size = lax.axis_size(axis)
    nbits = size.bit_length() - 1
    groups = [[0]] + [list(range(b, min(b + 2, nbits))) for b in range(1, nbits, 2)]
    idx = lax.axis_index(axis)
    cur = flat
    for bits in groups:
        radix, low = 1 << len(bits), bits[0]
        sub = (idx >> low) & (radix - 1)
        part = cur.shape[0] // radix
        total = lax.dynamic_slice_in_dim(cur, sub * part, part)
        for d in range(1, radix):
            send = lax.dynamic_slice_in_dim(cur, (sub ^ d) * part, part)
            total = total + lax.ppermute(send, axis, [(i, i ^ (d << low)) for i in range(size)])
        cur = total
    cur = cur.astype(gather_dtype)
    for bits in reversed(groups):
        radix, low = 1 << len(bits), bits[0]
        sub = (idx >> low) & (radix - 1)
        part = cur.shape[0]
        full = lax.dynamic_update_slice_in_dim(
            jnp.zeros((part * radix,), cur.dtype), cur, sub * part, 0
        )
        for d in range(1, radix):
            recv = lax.ppermute(cur, axis, [(i, i ^ (d << low)) for i in range(size)])
            full = lax.dynamic_update_slice_in_dim(full, recv, (sub ^ d) * part, 0)
        cur = full
    return cur.astype(flat.dtype)


def butterfly_allreduce(flat, axis):
    for bit in range(lax.axis_size(axis).bit_length() - 1):
        flat = flat + swapped(flat, axis, bit)
    return flat


def pack(arrays, multiple):
    flat = jnp.concatenate([a.reshape(-1) for a in arrays])
    extra = -flat.shape[0] % multiple
    return jnp.pad(flat, (0, extra))


def unpack(flat, arrays):
    out, at = [], 0
    for a in arrays:
        out.append(flat[at : at + a.size].reshape(a.shape))
        at += a.size
    return out


def on_device(
    features,
    target,
    south_rim,
    kmt,
    dw_kernel,
    dw_bias,
    ln_gain,
    ln_bias,
    w_in,
    b_in,
    w_out,
    b_out,
    layer_scale,
):
    members, lon_dev, lat_rows, chans = features.shape
    params = (dw_kernel, dw_bias, ln_gain, ln_bias, w_in, b_in, w_out, b_out, layer_scale)
    north_rows = mirror_rows(features[:, :, lat_rows - 3 :, :])
    joined = jnp.concatenate([south_rim, features, north_rows], axis=2)
    extended = with_halo(joined, (("lon", 1),), 3)
    predicted, crps_field, grad_pred, grad_depth, grads = local_step(
        extended, features, target, kmt, *params
    )
    grad_halo = with_halo(grad_depth, (("lon", 1),), 3)
    padded = jnp.pad(grad_halo, ((0, 0), (0, 0), (6, 6), (0, 0)))
    grad_ext = jnp.zeros((members, lon_dev, lat_rows + 6, chans), jnp.float32)
    for lon_off in range(7):
        for lat_off in range(7):
            grad_ext = (
                grad_ext
                + dw_kernel[lon_off, lat_off]
                * padded[
                    :,
                    6 - lon_off : 6 - lon_off + lon_dev,
                    6 - lat_off : 6 - lat_off + lat_rows + 6,
                    :,
                ]
            )
    back_rows = mirror_grads(grad_ext[:, :, lat_rows + 3 :, :])
    inner = grad_pred + grad_ext[:, :, 3 : lat_rows + 3, :]
    grad_features = jnp.concatenate(
        [inner[:, :, : lat_rows - 3, :], inner[:, :, lat_rows - 3 :, :] + back_rows], axis=2
    ).astype(jnp.bfloat16)
    (
        kernel_sum,
        dw_bias_sum,
        gain_sum,
        bias_sum,
        w_in_sum,
        b_in_sum,
        w_out_sum,
        b_out_sum,
        scale_sum,
    ) = grads
    lon_size = lax.axis_size("lon")
    sums = (
        kernel_sum,
        dw_bias_sum,
        gain_sum,
        bias_sum,
        w_in_sum,
        b_in_sum,
        w_out_sum,
        b_out_sum,
        scale_sum,
    )
    totals = unpack(radix_allreduce(pack(sums, lon_size * 1024), "lon", jnp.bfloat16), sums)
    factor = 1.0 / math.sqrt(members * lat_rows * lon_dev * lax.axis_size("lon"))
    return (
        predicted,
        crps_field,
        grad_features,
        totals[0] * factor,
        totals[1] * factor,
        totals[2] * factor,
        totals[3] * factor,
        totals[4] * factor,
        totals[5] * factor,
        totals[6] * factor,
        totals[7] * factor,
        totals[8] * factor,
    )


def solution(mesh):
    placed = (
        P(None, ("groups", "lon"), None, None),
        P(("groups", "lon"), None, None),
        P(None, ("groups", "lon"), None, None),
        P(("groups", "lon"), None),
        P(),
        P(),
        P(),
        P(),
        P(),
        P(),
        P(),
        P(),
        P(),
    )
    return jax.shard_map(
        on_device,
        mesh=mesh,
        in_specs=placed,
        out_specs=(
            P(None, ("groups", "lon"), None, None),
            P(("groups", "lon"), None, None),
            P(None, ("groups", "lon"), None, None),
            P("groups", None, None),
            P("groups"),
            P("groups"),
            P("groups"),
            P("groups", None),
            P("groups"),
            P("groups", None),
            P("groups"),
            P("groups"),
        ),
        check_vma=False,
    )
```

```python
import math

import jax
import jax.numpy as jnp
from jax import lax
from jax.sharding import PartitionSpec as P

LEVELS = 19


SMOOTH = 0.25
EPSILON = 1e-06


def swapped(x, axis, bit):
    return lax.ppermute(x, axis, [(i, i ^ 1 << bit) for i in range(lax.axis_size(axis))])


def with_halo(x, sides, width):
    for axis, dim in sides:
        size, length = (lax.axis_size(axis), x.shape[dim])
        up = [(i, (i + 1) % size) for i in range(size)]
        down = [(j, i) for i, j in up]
        last = lax.slice_in_dim(x, length - width, length, axis=dim)
        leading = lax.slice_in_dim(x, 0, width, axis=dim)
        before = lax.ppermute(last, axis, up)
        after = lax.ppermute(leading, axis, down)
        x = jnp.concatenate([before, x, after], axis=dim)
    return x


def smooth_abs(value):
    return jnp.sqrt(value * value + SMOOTH * SMOOTH) - SMOOTH


def smooth_slope(value):
    return value / jnp.sqrt(value * value + SMOOTH * SMOOTH)


def local_step(
    extended,
    features,
    target,
    kmt,
    dw_kernel,
    dw_bias,
    ln_gain,
    ln_bias,
    w_in,
    b_in,
    w_out,
    b_out,
    layer_scale,
):
    members, lon_dev, lat_rows, chans = features.shape
    depth = jnp.zeros(features.shape, jnp.float32) + dw_bias
    for lon_off in range(7):
        for lat_off in range(7):
            depth = depth + dw_kernel[lon_off, lat_off] * extended[
                :, lon_off : lon_off + lon_dev, lat_off : lat_off + lat_rows, :
            ].astype(jnp.float32)
    mean_val = jnp.mean(depth, axis=-1, keepdims=True)
    centred = depth - mean_val
    variance = jnp.mean(centred * centred, axis=-1, keepdims=True)
    inv_std = lax.rsqrt(variance + EPSILON)
    unit = centred * inv_std
    normed = (unit * ln_gain + ln_bias).astype(jnp.bfloat16)
    level_of = jnp.arange(chans, dtype=jnp.int32) * LEVELS // chans
    wet_mask = (level_of[None, None, :] < kmt[:, :, None]).astype(jnp.float32)
    rows = lon_dev * lat_rows
    pre_acts = []
    hiddens = []
    outputs = []
    for member in range(members):
        flat_rows = normed[member].reshape(rows, chans)
        pre_act = jnp.dot(flat_rows, w_in, preferred_element_type=jnp.float32) + b_in
        hidden = jax.nn.gelu(pre_act).astype(jnp.bfloat16)
        pre_acts.append(pre_act)
        hiddens.append(hidden)
        outputs.append(
            (jnp.dot(hidden, w_out, preferred_element_type=jnp.float32) + b_out).reshape(
                lon_dev, lat_rows, chans
            )
        )
    branch = jnp.stack(outputs)
    pred = wet_mask * (features.astype(jnp.float32) + layer_scale * branch)
    target_full = target.astype(jnp.float32)
    pair_weight = 1.0 / (members * (members - 1))
    skill = jnp.zeros(target.shape, jnp.float32)
    spread = jnp.zeros(target.shape, jnp.float32)
    for member in range(members):
        skill = skill + smooth_abs(pred[member] - target_full)
        for other in range(member + 1, members):
            spread = spread + smooth_abs(pred[member] - pred[other])
    crps_field = wet_mask * (skill / members - pair_weight * spread)
    grad_list = []
    for member in range(members):
        slope_sum = jnp.zeros(target.shape, jnp.float32)
        for other in range(members):
            if other != member:
                slope_sum = slope_sum + smooth_slope(pred[member] - pred[other])
        grad_list.append(
            wet_mask
            * (smooth_slope(pred[member] - target_full) / members - pair_weight * slope_sum)
        )
    grad_pred = jnp.stack(grad_list)
    grad_scale = jnp.sum(grad_pred * branch, axis=(0, 1, 2))
    grad_b_out = jnp.zeros((chans,), jnp.float32)
    grad_w_out = jnp.zeros(w_out.shape, jnp.float32)
    grad_b_in = jnp.zeros(b_in.shape, jnp.float32)
    grad_w_in = jnp.zeros(w_in.shape, jnp.float32)
    normed_grads = []
    contract_rows = (((0,), (0,)), ((), ()))
    contract_cols = (((1,), (1,)), ((), ()))
    for member in range(members):
        grad_out = (grad_pred[member] * layer_scale).reshape(rows, chans)
        grad_b_out = grad_b_out + jnp.sum(grad_out, axis=0)
        out_half = grad_out.astype(jnp.bfloat16)
        grad_w_out = grad_w_out + lax.dot_general(
            hiddens[member], out_half, contract_rows, preferred_element_type=jnp.float32
        )
        grad_hidden = lax.dot_general(
            out_half, w_out, contract_cols, preferred_element_type=jnp.float32
        )
        grad_pre = jax.vjp(jax.nn.gelu, pre_acts[member])[1](grad_hidden)[0]
        grad_b_in = grad_b_in + jnp.sum(grad_pre, axis=0)
        pre_half = grad_pre.astype(jnp.bfloat16)
        grad_w_in = grad_w_in + lax.dot_general(
            normed[member].reshape(rows, chans),
            pre_half,
            contract_rows,
            preferred_element_type=jnp.float32,
        )
        normed_grads.append(
            lax.dot_general(
                pre_half, w_in, contract_cols, preferred_element_type=jnp.float32
            ).reshape(lon_dev, lat_rows, chans)
        )
    grad_normed = jnp.stack(normed_grads)
    grad_ln_gain = jnp.sum(grad_normed * unit, axis=(0, 1, 2))
    grad_ln_bias = jnp.sum(grad_normed, axis=(0, 1, 2))
    grad_unit = grad_normed * ln_gain
    grad_depth = inv_std * (
        grad_unit
        - jnp.mean(grad_unit, axis=-1, keepdims=True)
        - unit * jnp.mean(grad_unit * unit, axis=-1, keepdims=True)
    )
    grad_dw_bias = jnp.sum(grad_depth, axis=(0, 1, 2))
    kernel_rows = []
    for lon_off in range(7):
        kernel_cols = []
        for lat_off in range(7):
            kernel_cols.append(
                jnp.sum(
                    grad_depth
                    * extended[
                        :, lon_off : lon_off + lon_dev, lat_off : lat_off + lat_rows, :
                    ].astype(jnp.float32),
                    axis=(0, 1, 2),
                )
            )
        kernel_rows.append(jnp.stack(kernel_cols))
    grad_kernel = jnp.stack(kernel_rows)
    grads = (
        grad_kernel,
        grad_dw_bias,
        grad_ln_gain,
        grad_ln_bias,
        grad_w_in,
        grad_b_in,
        grad_w_out,
        grad_b_out,
        grad_scale,
    )
    return (pred.astype(jnp.bfloat16), crps_field, grad_pred, grad_depth, grads)


def mirrored(x, axis):
    size = lax.axis_size(axis)
    return lax.ppermute(x, axis, [(i, size - 1 - i) for i in range(size)])


def mirror_rows(top_rows):
    return mirrored(top_rows, "lon")[:, ::-1, ::-1, :]


def mirror_grads(fold_rows):
    picked = mirrored(fold_rows.astype(jnp.bfloat16), "lon").astype(fold_rows.dtype)
    return picked[:, ::-1, ::-1, :]


def halving_allreduce(flat, axis, gather_dtype):
    size = lax.axis_size(axis)
    bits = size.bit_length() - 1
    idx = lax.axis_index(axis)
    cur = flat
    for bit in range(bits):
        half = cur.shape[0] // 2
        mine = (idx >> bit) & 1
        keep = lax.dynamic_slice_in_dim(cur, mine * half, half)
        send = lax.dynamic_slice_in_dim(cur, (1 - mine) * half, half)
        cur = keep + swapped(send, axis, bit)
    cur = cur.astype(gather_dtype)
    for bit in reversed(range(bits)):
        mine = (idx >> bit) & 1
        recv = swapped(cur, axis, bit)
        cur = jnp.where(mine == 0, jnp.concatenate([cur, recv]), jnp.concatenate([recv, cur]))
    return cur.astype(flat.dtype)


def radix_allreduce(flat, axis, gather_dtype):
    size = lax.axis_size(axis)
    nbits = size.bit_length() - 1
    groups = [[0]] + [list(range(b, min(b + 2, nbits))) for b in range(1, nbits, 2)]
    idx = lax.axis_index(axis)
    cur = flat
    for bits in groups:
        radix, low = 1 << len(bits), bits[0]
        sub = (idx >> low) & (radix - 1)
        part = cur.shape[0] // radix
        total = lax.dynamic_slice_in_dim(cur, sub * part, part)
        for d in range(1, radix):
            send = lax.dynamic_slice_in_dim(cur, (sub ^ d) * part, part)
            total = total + lax.ppermute(send, axis, [(i, i ^ (d << low)) for i in range(size)])
        cur = total
    cur = cur.astype(gather_dtype)
    for bits in reversed(groups):
        radix, low = 1 << len(bits), bits[0]
        sub = (idx >> low) & (radix - 1)
        pieces = [cur] + [
            lax.ppermute(cur, axis, [(i, i ^ (d << low)) for i in range(size)])
            for d in range(1, radix)
        ]
        placed = []
        for p in range(radix):
            pick = pieces[p ^ (radix - 1)]
            for s in range(radix - 1):
                pick = jnp.where(sub == s, pieces[p ^ s], pick)
            placed.append(pick)
        cur = jnp.concatenate(placed)
    return cur.astype(flat.dtype)


def butterfly_allreduce(flat, axis):
    for bit in range(lax.axis_size(axis).bit_length() - 1):
        flat = flat + swapped(flat, axis, bit)
    return flat


def pack(arrays, multiple):
    flat = jnp.concatenate([a.reshape(-1) for a in arrays])
    extra = -flat.shape[0] % multiple
    return jnp.pad(flat, (0, extra))


def unpack(flat, arrays):
    out, at = [], 0
    for a in arrays:
        out.append(flat[at : at + a.size].reshape(a.shape))
        at += a.size
    return out


def on_device(
    features,
    target,
    south_rim,
    kmt,
    dw_kernel,
    dw_bias,
    ln_gain,
    ln_bias,
    w_in,
    b_in,
    w_out,
    b_out,
    layer_scale,
):
    members, lon_dev, lat_rows, chans = features.shape
    params = (dw_kernel, dw_bias, ln_gain, ln_bias, w_in, b_in, w_out, b_out, layer_scale)
    north_rows = mirror_rows(features[:, :, lat_rows - 3 :, :])
    joined = jnp.concatenate([south_rim, features, north_rows], axis=2)
    extended = with_halo(joined, (("lon", 1),), 3)
    predicted, crps_field, grad_pred, grad_depth, grads = local_step(
        extended, features, target, kmt, *params
    )
    grad_halo = with_halo(grad_depth, (("lon", 1),), 3)
    padded = jnp.pad(grad_halo, ((0, 0), (0, 0), (6, 6), (0, 0)))
    grad_ext = jnp.zeros((members, lon_dev, lat_rows + 6, chans), jnp.float32)
    for lon_off in range(7):
        for lat_off in range(7):
            grad_ext = (
                grad_ext
                + dw_kernel[lon_off, lat_off]
                * padded[
                    :,
                    6 - lon_off : 6 - lon_off + lon_dev,
                    6 - lat_off : 6 - lat_off + lat_rows + 6,
                    :,
                ]
            )
    back_rows = mirror_grads(grad_ext[:, :, lat_rows + 3 :, :])
    inner = grad_pred + grad_ext[:, :, 3 : lat_rows + 3, :]
    grad_features = jnp.concatenate(
        [inner[:, :, : lat_rows - 3, :], inner[:, :, lat_rows - 3 :, :] + back_rows], axis=2
    ).astype(jnp.bfloat16)
    (
        kernel_sum,
        dw_bias_sum,
        gain_sum,
        bias_sum,
        w_in_sum,
        b_in_sum,
        w_out_sum,
        b_out_sum,
        scale_sum,
    ) = grads
    lon_size = lax.axis_size("lon")
    sums = (
        kernel_sum,
        dw_bias_sum,
        gain_sum,
        bias_sum,
        w_in_sum,
        b_in_sum,
        w_out_sum,
        b_out_sum,
        scale_sum,
    )
    totals = unpack(radix_allreduce(pack(sums, lon_size * 1024), "lon", jnp.bfloat16), sums)
    factor = 1.0 / math.sqrt(members * lat_rows * lon_dev * lax.axis_size("lon"))
    return (
        predicted,
        crps_field,
        grad_features,
        totals[0] * factor,
        totals[1] * factor,
        totals[2] * factor,
        totals[3] * factor,
        totals[4] * factor,
        totals[5] * factor,
        totals[6] * factor,
        totals[7] * factor,
        totals[8] * factor,
    )


def solution(mesh):
    placed = (
        P(None, ("groups", "lon"), None, None),
        P(("groups", "lon"), None, None),
        P(None, ("groups", "lon"), None, None),
        P(("groups", "lon"), None),
        P(),
        P(),
        P(),
        P(),
        P(),
        P(),
        P(),
        P(),
        P(),
    )
    return jax.shard_map(
        on_device,
        mesh=mesh,
        in_specs=placed,
        out_specs=(
            P(None, ("groups", "lon"), None, None),
            P(("groups", "lon"), None, None),
            P(None, ("groups", "lon"), None, None),
            P("groups", None, None),
            P("groups"),
            P("groups"),
            P("groups"),
            P("groups", None),
            P("groups"),
            P("groups", None),
            P("groups"),
            P("groups"),
        ),
        check_vma=False,
    )
```

```python
import math

import jax
import jax.numpy as jnp
from jax import lax
from jax.sharding import PartitionSpec as P

LEVELS = 19


SMOOTH = 0.25
EPSILON = 1e-06


def swapped(x, axis, bit):
    return lax.ppermute(x, axis, [(i, i ^ 1 << bit) for i in range(lax.axis_size(axis))])


def with_halo(x, sides, width):
    for axis, dim in sides:
        size, length = (lax.axis_size(axis), x.shape[dim])
        up = [(i, (i + 1) % size) for i in range(size)]
        down = [(j, i) for i, j in up]
        last = lax.slice_in_dim(x, length - width, length, axis=dim)
        leading = lax.slice_in_dim(x, 0, width, axis=dim)
        before = lax.ppermute(last, axis, up)
        after = lax.ppermute(leading, axis, down)
        x = jnp.concatenate([before, x, after], axis=dim)
    return x


def smooth_abs(value):
    return jnp.sqrt(value * value + SMOOTH * SMOOTH) - SMOOTH


def smooth_slope(value):
    return value / jnp.sqrt(value * value + SMOOTH * SMOOTH)


def local_step(
    extended,
    features,
    target,
    kmt,
    dw_kernel,
    dw_bias,
    ln_gain,
    ln_bias,
    w_in,
    b_in,
    w_out,
    b_out,
    layer_scale,
):
    members, lon_dev, lat_rows, chans = features.shape
    depth = jnp.zeros(features.shape, jnp.float32) + dw_bias
    for lon_off in range(7):
        for lat_off in range(7):
            depth = depth + dw_kernel[lon_off, lat_off] * extended[
                :, lon_off : lon_off + lon_dev, lat_off : lat_off + lat_rows, :
            ].astype(jnp.float32)
    mean_val = jnp.mean(depth, axis=-1, keepdims=True)
    centred = depth - mean_val
    variance = jnp.mean(centred * centred, axis=-1, keepdims=True)
    inv_std = lax.rsqrt(variance + EPSILON)
    unit = centred * inv_std
    normed = (unit * ln_gain + ln_bias).astype(jnp.bfloat16)
    level_of = jnp.arange(chans, dtype=jnp.int32) * LEVELS // chans
    wet_mask = (level_of[None, None, :] < kmt[:, :, None]).astype(jnp.float32)
    rows = lon_dev * lat_rows
    pre_acts = []
    hiddens = []
    outputs = []
    for member in range(members):
        flat_rows = normed[member].reshape(rows, chans)
        pre_act = jnp.dot(flat_rows, w_in, preferred_element_type=jnp.float32) + b_in
        hidden = jax.nn.gelu(pre_act).astype(jnp.bfloat16)
        pre_acts.append(pre_act)
        hiddens.append(hidden)
        outputs.append(
            (jnp.dot(hidden, w_out, preferred_element_type=jnp.float32) + b_out).reshape(
                lon_dev, lat_rows, chans
            )
        )
    branch = jnp.stack(outputs)
    pred = wet_mask * (features.astype(jnp.float32) + layer_scale * branch)
    target_full = target.astype(jnp.float32)
    pair_weight = 1.0 / (members * (members - 1))
    skill = jnp.zeros(target.shape, jnp.float32)
    spread = jnp.zeros(target.shape, jnp.float32)
    for member in range(members):
        skill = skill + smooth_abs(pred[member] - target_full)
        for other in range(member + 1, members):
            spread = spread + smooth_abs(pred[member] - pred[other])
    crps_field = wet_mask * (skill / members - pair_weight * spread)
    grad_list = []
    for member in range(members):
        slope_sum = jnp.zeros(target.shape, jnp.float32)
        for other in range(members):
            if other != member:
                slope_sum = slope_sum + smooth_slope(pred[member] - pred[other])
        grad_list.append(
            wet_mask
            * (smooth_slope(pred[member] - target_full) / members - pair_weight * slope_sum)
        )
    grad_pred = jnp.stack(grad_list)
    grad_scale = jnp.sum(grad_pred * branch, axis=(0, 1, 2))
    grad_b_out = jnp.zeros((chans,), jnp.float32)
    grad_w_out = jnp.zeros(w_out.shape, jnp.float32)
    grad_b_in = jnp.zeros(b_in.shape, jnp.float32)
    grad_w_in = jnp.zeros(w_in.shape, jnp.float32)
    normed_grads = []
    contract_rows = (((0,), (0,)), ((), ()))
    contract_cols = (((1,), (1,)), ((), ()))
    for member in range(members):
        grad_out = (grad_pred[member] * layer_scale).reshape(rows, chans)
        grad_b_out = grad_b_out + jnp.sum(grad_out, axis=0)
        out_half = grad_out.astype(jnp.bfloat16)
        grad_w_out = grad_w_out + lax.dot_general(
            hiddens[member], out_half, contract_rows, preferred_element_type=jnp.float32
        )
        grad_hidden = lax.dot_general(
            out_half, w_out, contract_cols, preferred_element_type=jnp.float32
        )
        grad_pre = jax.vjp(jax.nn.gelu, pre_acts[member])[1](grad_hidden)[0]
        grad_b_in = grad_b_in + jnp.sum(grad_pre, axis=0)
        pre_half = grad_pre.astype(jnp.bfloat16)
        grad_w_in = grad_w_in + lax.dot_general(
            normed[member].reshape(rows, chans),
            pre_half,
            contract_rows,
            preferred_element_type=jnp.float32,
        )
        normed_grads.append(
            lax.dot_general(
                pre_half, w_in, contract_cols, preferred_element_type=jnp.float32
            ).reshape(lon_dev, lat_rows, chans)
        )
    grad_normed = jnp.stack(normed_grads)
    grad_ln_gain = jnp.sum(grad_normed * unit, axis=(0, 1, 2))
    grad_ln_bias = jnp.sum(grad_normed, axis=(0, 1, 2))
    grad_unit = grad_normed * ln_gain
    grad_depth = inv_std * (
        grad_unit
        - jnp.mean(grad_unit, axis=-1, keepdims=True)
        - unit * jnp.mean(grad_unit * unit, axis=-1, keepdims=True)
    )
    grad_dw_bias = jnp.sum(grad_depth, axis=(0, 1, 2))
    kernel_rows = []
    for lon_off in range(7):
        kernel_cols = []
        for lat_off in range(7):
            kernel_cols.append(
                jnp.sum(
                    grad_depth
                    * extended[
                        :, lon_off : lon_off + lon_dev, lat_off : lat_off + lat_rows, :
                    ].astype(jnp.float32),
                    axis=(0, 1, 2),
                )
            )
        kernel_rows.append(jnp.stack(kernel_cols))
    grad_kernel = jnp.stack(kernel_rows)
    grads = (
        grad_kernel,
        grad_dw_bias,
        grad_ln_gain,
        grad_ln_bias,
        grad_w_in,
        grad_b_in,
        grad_w_out,
        grad_b_out,
        grad_scale,
    )
    return (pred.astype(jnp.bfloat16), crps_field, grad_pred, grad_depth, grads)


def mirrored(x, axis):
    size = lax.axis_size(axis)
    return lax.ppermute(x, axis, [(i, size - 1 - i) for i in range(size)])


def mirror_rows(top_rows):
    return mirrored(top_rows, "lon")[:, ::-1, ::-1, :]


def mirror_grads(fold_rows):
    picked = mirrored(fold_rows.astype(jnp.bfloat16), "lon").astype(fold_rows.dtype)
    return picked[:, ::-1, ::-1, :]


def halving_allreduce(flat, axis, gather_dtype):
    size = lax.axis_size(axis)
    bits = size.bit_length() - 1
    idx = lax.axis_index(axis)
    cur = flat
    for bit in range(bits):
        half = cur.shape[0] // 2
        mine = (idx >> bit) & 1
        keep = lax.dynamic_slice_in_dim(cur, mine * half, half)
        send = lax.dynamic_slice_in_dim(cur, (1 - mine) * half, half)
        cur = keep + swapped(send, axis, bit)
    cur = cur.astype(gather_dtype)
    for bit in reversed(range(bits)):
        mine = (idx >> bit) & 1
        recv = swapped(cur, axis, bit)
        cur = jnp.where(mine == 0, jnp.concatenate([cur, recv]), jnp.concatenate([recv, cur]))
    return cur.astype(flat.dtype)


def radix_allreduce(flat, axis, gather_dtype, tie):
    size = lax.axis_size(axis)
    nbits = size.bit_length() - 1
    groups = [[0]] + [list(range(b, min(b + 2, nbits))) for b in range(1, nbits, 2)]
    idx = lax.axis_index(axis)
    cur = flat
    for bits in groups:
        radix, low = 1 << len(bits), bits[0]
        sub = (idx >> low) & (radix - 1)
        part = cur.shape[0] // radix
        total = lax.dynamic_slice_in_dim(cur, sub * part, part)
        for d in range(1, radix):
            send = lax.dynamic_slice_in_dim(cur, (sub ^ d) * part, part)
            total = total + lax.ppermute(send, axis, [(i, i ^ (d << low)) for i in range(size)])
        cur = total
        if bits == groups[0]:
            cur, tie = lax.optimization_barrier((cur, tie))
    cur = cur.astype(gather_dtype)
    for bits in reversed(groups):
        radix, low = 1 << len(bits), bits[0]
        sub = (idx >> low) & (radix - 1)
        pieces = [cur] + [
            lax.ppermute(cur, axis, [(i, i ^ (d << low)) for i in range(size)])
            for d in range(1, radix)
        ]
        placed = []
        for p in range(radix):
            pick = pieces[p ^ (radix - 1)]
            for s in range(radix - 1):
                pick = jnp.where(sub == s, pieces[p ^ s], pick)
            placed.append(pick)
        cur = jnp.concatenate(placed)
    return cur.astype(flat.dtype), tie


def butterfly_allreduce(flat, axis):
    for bit in range(lax.axis_size(axis).bit_length() - 1):
        flat = flat + swapped(flat, axis, bit)
    return flat


def pack(arrays, multiple):
    flat = jnp.concatenate([a.reshape(-1) for a in arrays])
    extra = -flat.shape[0] % multiple
    return jnp.pad(flat, (0, extra))


def unpack(flat, arrays):
    out, at = [], 0
    for a in arrays:
        out.append(flat[at : at + a.size].reshape(a.shape))
        at += a.size
    return out


def on_device(
    features,
    target,
    south_rim,
    kmt,
    dw_kernel,
    dw_bias,
    ln_gain,
    ln_bias,
    w_in,
    b_in,
    w_out,
    b_out,
    layer_scale,
):
    members, lon_dev, lat_rows, chans = features.shape
    params = (dw_kernel, dw_bias, ln_gain, ln_bias, w_in, b_in, w_out, b_out, layer_scale)
    north_rows = mirror_rows(features[:, :, lat_rows - 3 :, :])
    joined = jnp.concatenate([south_rim, features, north_rows], axis=2)
    extended = with_halo(joined, (("lon", 1),), 3)
    predicted, crps_field, grad_pred, grad_depth, grads = local_step(
        extended, features, target, kmt, *params
    )
    grad_halo = with_halo(grad_depth, (("lon", 1),), 3)
    padded = jnp.pad(grad_halo, ((0, 0), (0, 0), (6, 6), (0, 0)))
    lon_size = lax.axis_size("lon")
    reduced, padded = radix_allreduce(
        pack(grads, lon_size * 1024), "lon", jnp.bfloat16, padded
    )
    totals = unpack(reduced, grads)
    grad_ext = jnp.zeros((members, lon_dev, lat_rows + 6, chans), jnp.float32)
    for lon_off in range(7):
        for lat_off in range(7):
            grad_ext = (
                grad_ext
                + dw_kernel[lon_off, lat_off]
                * padded[
                    :,
                    6 - lon_off : 6 - lon_off + lon_dev,
                    6 - lat_off : 6 - lat_off + lat_rows + 6,
                    :,
                ]
            )
    back_rows = mirror_grads(grad_ext[:, :, lat_rows + 3 :, :])
    inner = grad_pred + grad_ext[:, :, 3 : lat_rows + 3, :]
    grad_features = jnp.concatenate(
        [inner[:, :, : lat_rows - 3, :], inner[:, :, lat_rows - 3 :, :] + back_rows], axis=2
    ).astype(jnp.bfloat16)
    factor = 1.0 / math.sqrt(members * lat_rows * lon_dev * lax.axis_size("lon"))
    return (
        predicted,
        crps_field,
        grad_features,
        totals[0] * factor,
        totals[1] * factor,
        totals[2] * factor,
        totals[3] * factor,
        totals[4] * factor,
        totals[5] * factor,
        totals[6] * factor,
        totals[7] * factor,
        totals[8] * factor,
    )


def solution(mesh):
    placed = (
        P(None, ("groups", "lon"), None, None),
        P(("groups", "lon"), None, None),
        P(None, ("groups", "lon"), None, None),
        P(("groups", "lon"), None),
        P(),
        P(),
        P(),
        P(),
        P(),
        P(),
        P(),
        P(),
        P(),
    )
    return jax.shard_map(
        on_device,
        mesh=mesh,
        in_specs=placed,
        out_specs=(
            P(None, ("groups", "lon"), None, None),
            P(("groups", "lon"), None, None),
            P(None, ("groups", "lon"), None, None),
            P("groups", None, None),
            P("groups"),
            P("groups"),
            P("groups"),
            P("groups", None),
            P("groups"),
            P("groups", None),
            P("groups"),
            P("groups"),
        ),
        check_vma=False,
    )
```

```python
import math

import jax
import jax.numpy as jnp
from jax import lax
from jax.sharding import PartitionSpec as P

LEVELS = 19


SMOOTH = 0.25
EPSILON = 1e-06


def swapped(x, axis, bit):
    return lax.ppermute(x, axis, [(i, i ^ 1 << bit) for i in range(lax.axis_size(axis))])


def with_halo(x, sides, width):
    for axis, dim in sides:
        size, length = (lax.axis_size(axis), x.shape[dim])
        up = [(i, (i + 1) % size) for i in range(size)]
        down = [(j, i) for i, j in up]
        last = lax.slice_in_dim(x, length - width, length, axis=dim)
        leading = lax.slice_in_dim(x, 0, width, axis=dim)
        before = lax.ppermute(last, axis, up)
        after = lax.ppermute(leading, axis, down)
        x = jnp.concatenate([before, x, after], axis=dim)
    return x


def smooth_abs(value):
    return jnp.sqrt(value * value + SMOOTH * SMOOTH) - SMOOTH


def smooth_slope(value):
    return value / jnp.sqrt(value * value + SMOOTH * SMOOTH)


def local_step(
    extended,
    features,
    target,
    kmt,
    dw_kernel,
    dw_bias,
    ln_gain,
    ln_bias,
    w_in,
    b_in,
    w_out,
    b_out,
    layer_scale,
):
    members, lon_dev, lat_rows, chans = features.shape
    depth = jnp.zeros(features.shape, jnp.float32) + dw_bias
    for lon_off in range(7):
        for lat_off in range(7):
            depth = depth + dw_kernel[lon_off, lat_off] * extended[
                :, lon_off : lon_off + lon_dev, lat_off : lat_off + lat_rows, :
            ].astype(jnp.float32)
    mean_val = jnp.mean(depth, axis=-1, keepdims=True)
    centred = depth - mean_val
    variance = jnp.mean(centred * centred, axis=-1, keepdims=True)
    inv_std = lax.rsqrt(variance + EPSILON)
    unit = centred * inv_std
    normed = (unit * ln_gain + ln_bias).astype(jnp.bfloat16)
    level_of = jnp.arange(chans, dtype=jnp.int32) * LEVELS // chans
    wet_mask = (level_of[None, None, :] < kmt[:, :, None]).astype(jnp.float32)
    rows = lon_dev * lat_rows
    pre_acts = []
    hiddens = []
    outputs = []
    for member in range(members):
        flat_rows = normed[member].reshape(rows, chans)
        pre_act = jnp.dot(flat_rows, w_in, preferred_element_type=jnp.float32) + b_in
        hidden = jax.nn.gelu(pre_act).astype(jnp.bfloat16)
        pre_acts.append(pre_act)
        hiddens.append(hidden)
        outputs.append(
            (jnp.dot(hidden, w_out, preferred_element_type=jnp.float32) + b_out).reshape(
                lon_dev, lat_rows, chans
            )
        )
    branch = jnp.stack(outputs)
    pred = wet_mask * (features.astype(jnp.float32) + layer_scale * branch)
    target_full = target.astype(jnp.float32)
    pair_weight = 1.0 / (members * (members - 1))
    skill = jnp.zeros(target.shape, jnp.float32)
    spread = jnp.zeros(target.shape, jnp.float32)
    for member in range(members):
        skill = skill + smooth_abs(pred[member] - target_full)
        for other in range(member + 1, members):
            spread = spread + smooth_abs(pred[member] - pred[other])
    crps_field = wet_mask * (skill / members - pair_weight * spread)
    grad_list = []
    for member in range(members):
        slope_sum = jnp.zeros(target.shape, jnp.float32)
        for other in range(members):
            if other != member:
                slope_sum = slope_sum + smooth_slope(pred[member] - pred[other])
        grad_list.append(
            wet_mask
            * (smooth_slope(pred[member] - target_full) / members - pair_weight * slope_sum)
        )
    grad_pred = jnp.stack(grad_list)
    grad_scale = jnp.sum(grad_pred * branch, axis=(0, 1, 2))
    grad_b_out = jnp.zeros((chans,), jnp.float32)
    grad_w_out = jnp.zeros(w_out.shape[::-1], jnp.float32)
    grad_b_in = jnp.zeros(b_in.shape, jnp.float32)
    grad_w_in = jnp.zeros(w_in.shape, jnp.float32)
    normed_grads = []
    contract_rows = (((0,), (0,)), ((), ()))
    contract_cols = (((1,), (1,)), ((), ()))
    for member in range(members):
        grad_out = (grad_pred[member] * layer_scale).reshape(rows, chans)
        grad_b_out = grad_b_out + jnp.sum(grad_out, axis=0)
        out_half = grad_out.astype(jnp.bfloat16)
        grad_w_out = grad_w_out + lax.dot_general(
            out_half, hiddens[member], contract_rows, preferred_element_type=jnp.float32
        )
        grad_hidden = lax.dot_general(
            out_half, w_out, contract_cols, preferred_element_type=jnp.float32
        )
        grad_pre = jax.vjp(jax.nn.gelu, pre_acts[member])[1](grad_hidden)[0]
        grad_b_in = grad_b_in + jnp.sum(grad_pre, axis=0)
        pre_half = grad_pre.astype(jnp.bfloat16)
        grad_w_in = grad_w_in + lax.dot_general(
            normed[member].reshape(rows, chans),
            pre_half,
            contract_rows,
            preferred_element_type=jnp.float32,
        )
        normed_grads.append(
            lax.dot_general(
                pre_half, w_in, contract_cols, preferred_element_type=jnp.float32
            ).reshape(lon_dev, lat_rows, chans)
        )
    grad_normed = jnp.stack(normed_grads)
    grad_ln_gain = jnp.sum(grad_normed * unit, axis=(0, 1, 2))
    grad_ln_bias = jnp.sum(grad_normed, axis=(0, 1, 2))
    grad_unit = grad_normed * ln_gain
    grad_depth = inv_std * (
        grad_unit
        - jnp.mean(grad_unit, axis=-1, keepdims=True)
        - unit * jnp.mean(grad_unit * unit, axis=-1, keepdims=True)
    )
    grad_dw_bias = jnp.sum(grad_depth, axis=(0, 1, 2))
    kernel_rows = []
    for lon_off in range(7):
        kernel_cols = []
        for lat_off in range(7):
            kernel_cols.append(
                jnp.sum(
                    grad_depth
                    * extended[
                        :, lon_off : lon_off + lon_dev, lat_off : lat_off + lat_rows, :
                    ].astype(jnp.float32),
                    axis=(0, 1, 2),
                )
            )
        kernel_rows.append(jnp.stack(kernel_cols))
    grad_kernel = jnp.stack(kernel_rows)
    grads = (
        grad_kernel,
        grad_dw_bias,
        grad_ln_gain,
        grad_ln_bias,
        grad_w_in,
        grad_b_in,
        grad_w_out,
        grad_b_out,
        grad_scale,
    )
    return (pred.astype(jnp.bfloat16), crps_field, grad_pred, grad_depth, grads)


def mirrored(x, axis):
    size = lax.axis_size(axis)
    return lax.ppermute(x, axis, [(i, size - 1 - i) for i in range(size)])


def mirror_rows(top_rows):
    return mirrored(top_rows, "lon")[:, ::-1, ::-1, :]


def mirror_grads(fold_rows):
    picked = mirrored(fold_rows.astype(jnp.bfloat16), "lon").astype(fold_rows.dtype)
    return picked[:, ::-1, ::-1, :]


def halving_allreduce(flat, axis, gather_dtype):
    size = lax.axis_size(axis)
    bits = size.bit_length() - 1
    idx = lax.axis_index(axis)
    cur = flat
    for bit in range(bits):
        half = cur.shape[0] // 2
        mine = (idx >> bit) & 1
        keep = lax.dynamic_slice_in_dim(cur, mine * half, half)
        send = lax.dynamic_slice_in_dim(cur, (1 - mine) * half, half)
        cur = keep + swapped(send, axis, bit)
    cur = cur.astype(gather_dtype)
    for bit in reversed(range(bits)):
        mine = (idx >> bit) & 1
        recv = swapped(cur, axis, bit)
        cur = jnp.where(mine == 0, jnp.concatenate([cur, recv]), jnp.concatenate([recv, cur]))
    return cur.astype(flat.dtype)


def radix_allreduce(block, axis, gather_dtype):
    size = lax.axis_size(axis)
    nbits = size.bit_length() - 1
    groups = [[0]] + [list(range(b, min(b + 2, nbits))) for b in range(1, nbits, 2)]
    idx = lax.axis_index(axis)
    cur = block
    dims = []
    for bits in groups:
        radix, low = 1 << len(bits), bits[0]
        sub = (idx >> low) & (radix - 1)
        dim = 1 if cur.shape[1] // radix >= 128 else 0
        part = cur.shape[dim] // radix
        total = lax.dynamic_slice_in_dim(cur, sub * part, part, axis=dim)
        for d in range(1, radix):
            send = lax.dynamic_slice_in_dim(cur, (sub ^ d) * part, part, axis=dim)
            total = total + lax.ppermute(send, axis, [(i, i ^ (d << low)) for i in range(size)])
        cur = total
        dims.append(dim)
    cur = cur.astype(gather_dtype)
    for bits, dim in reversed(list(zip(groups, dims))):
        radix, low = 1 << len(bits), bits[0]
        sub = (idx >> low) & (radix - 1)
        pieces = [cur] + [
            lax.ppermute(cur, axis, [(i, i ^ (d << low)) for i in range(size)])
            for d in range(1, radix)
        ]
        placed = []
        for p in range(radix):
            pick = pieces[p ^ (radix - 1)]
            for s in range(radix - 1):
                pick = jnp.where(sub == s, pieces[p ^ s], pick)
            placed.append(pick)
        cur = jnp.concatenate(placed, axis=dim)
    return cur.astype(block.dtype)


def butterfly_allreduce(flat, axis):
    for bit in range(lax.axis_size(axis).bit_length() - 1):
        flat = flat + swapped(flat, axis, bit)
    return flat


def pack(arrays, multiple):
    flat = jnp.concatenate([a.reshape(-1) for a in arrays])
    extra = -flat.shape[0] % multiple
    return jnp.pad(flat, (0, extra))


def unpack(flat, arrays):
    out, at = [], 0
    for a in arrays:
        out.append(flat[at : at + a.size].reshape(a.shape))
        at += a.size
    return out


def on_device(
    features,
    target,
    south_rim,
    kmt,
    dw_kernel,
    dw_bias,
    ln_gain,
    ln_bias,
    w_in,
    b_in,
    w_out,
    b_out,
    layer_scale,
):
    members, lon_dev, lat_rows, chans = features.shape
    params = (dw_kernel, dw_bias, ln_gain, ln_bias, w_in, b_in, w_out, b_out, layer_scale)
    north_rows = mirror_rows(features[:, :, lat_rows - 3 :, :])
    joined = jnp.concatenate([south_rim, features, north_rows], axis=2)
    extended = with_halo(joined, (("lon", 1),), 3)
    predicted, crps_field, grad_pred, grad_depth, grads = local_step(
        extended, features, target, kmt, *params
    )
    grad_halo = with_halo(grad_depth, (("lon", 1),), 3)
    padded = jnp.pad(grad_halo, ((0, 0), (0, 0), (6, 6), (0, 0)))
    grad_ext = jnp.zeros((members, lon_dev, lat_rows + 6, chans), jnp.float32)
    for lon_off in range(7):
        for lat_off in range(7):
            grad_ext = (
                grad_ext
                + dw_kernel[lon_off, lat_off]
                * padded[
                    :,
                    6 - lon_off : 6 - lon_off + lon_dev,
                    6 - lat_off : 6 - lat_off + lat_rows + 6,
                    :,
                ]
            )
    back_rows = mirror_grads(grad_ext[:, :, lat_rows + 3 :, :])
    inner = grad_pred + grad_ext[:, :, 3 : lat_rows + 3, :]
    grad_features = jnp.concatenate(
        [inner[:, :, : lat_rows - 3, :], inner[:, :, lat_rows - 3 :, :] + back_rows], axis=2
    ).astype(jnp.bfloat16)
    (
        kernel_sum,
        dw_bias_sum,
        gain_sum,
        bias_sum,
        w_in_sum,
        b_in_sum,
        w_out_sum,
        b_out_sum,
        scale_sum,
    ) = grads
    lon_size = lax.axis_size("lon")
    small = (kernel_sum, dw_bias_sum, gain_sum, bias_sum, b_in_sum, b_out_sum, scale_sum)
    width = w_in_sum.shape[1]
    big_rows = w_in_sum.shape[0] + w_out_sum.shape[0]
    small_rows = -(-sum(a.size for a in small) // width)
    small_rows += -(big_rows + small_rows) % lon_size
    block = jnp.concatenate(
        [w_in_sum, w_out_sum, pack(small, small_rows * width).reshape(small_rows, width)]
    )
    block = radix_allreduce(block, "lon", jnp.bfloat16)
    small_tot = unpack(block[big_rows:].reshape(-1), small)
    totals = (
        small_tot[0],
        small_tot[1],
        small_tot[2],
        small_tot[3],
        block[: w_in_sum.shape[0]],
        small_tot[4],
        block[w_in_sum.shape[0] : big_rows].T,
        small_tot[5],
        small_tot[6],
    )
    factor = 1.0 / math.sqrt(members * lat_rows * lon_dev * lax.axis_size("lon"))
    return (
        predicted,
        crps_field,
        grad_features,
        totals[0] * factor,
        totals[1] * factor,
        totals[2] * factor,
        totals[3] * factor,
        totals[4] * factor,
        totals[5] * factor,
        totals[6] * factor,
        totals[7] * factor,
        totals[8] * factor,
    )


def solution(mesh):
    placed = (
        P(None, ("groups", "lon"), None, None),
        P(("groups", "lon"), None, None),
        P(None, ("groups", "lon"), None, None),
        P(("groups", "lon"), None),
        P(),
        P(),
        P(),
        P(),
        P(),
        P(),
        P(),
        P(),
        P(),
    )
    return jax.shard_map(
        on_device,
        mesh=mesh,
        in_specs=placed,
        out_specs=(
            P(None, ("groups", "lon"), None, None),
            P(("groups", "lon"), None, None),
            P(None, ("groups", "lon"), None, None),
            P("groups", None, None),
            P("groups"),
            P("groups"),
            P("groups"),
            P("groups", None),
            P("groups"),
            P("groups", None),
            P("groups"),
            P("groups"),
        ),
        check_vma=False,
    )
```

```python
import math

import jax
import jax.numpy as jnp
from jax import lax
from jax.sharding import PartitionSpec as P

LEVELS = 19


SMOOTH = 0.25
EPSILON = 1e-06


def swapped(x, axis, bit):
    return lax.ppermute(x, axis, [(i, i ^ 1 << bit) for i in range(lax.axis_size(axis))])


def with_halo(x, sides, width):
    for axis, dim in sides:
        size, length = (lax.axis_size(axis), x.shape[dim])
        up = [(i, (i + 1) % size) for i in range(size)]
        down = [(j, i) for i, j in up]
        last = lax.slice_in_dim(x, length - width, length, axis=dim)
        leading = lax.slice_in_dim(x, 0, width, axis=dim)
        before = lax.ppermute(last, axis, up)
        after = lax.ppermute(leading, axis, down)
        x = jnp.concatenate([before, x, after], axis=dim)
    return x


def smooth_abs(value):
    return jnp.sqrt(value * value + SMOOTH * SMOOTH) - SMOOTH


def smooth_slope(value):
    return value / jnp.sqrt(value * value + SMOOTH * SMOOTH)


def local_step(
    extended,
    features,
    target,
    kmt,
    dw_kernel,
    dw_bias,
    ln_gain,
    ln_bias,
    w_in,
    b_in,
    w_out,
    b_out,
    layer_scale,
):
    members, lon_dev, lat_rows, chans = features.shape
    depth = jnp.zeros(features.shape, jnp.float32) + dw_bias
    for lon_off in range(7):
        for lat_off in range(7):
            depth = depth + dw_kernel[lon_off, lat_off] * extended[
                :, lon_off : lon_off + lon_dev, lat_off : lat_off + lat_rows, :
            ].astype(jnp.float32)
    mean_val = jnp.mean(depth, axis=-1, keepdims=True)
    centred = depth - mean_val
    variance = jnp.mean(centred * centred, axis=-1, keepdims=True)
    inv_std = lax.rsqrt(variance + EPSILON)
    unit = centred * inv_std
    normed = (unit * ln_gain + ln_bias).astype(jnp.bfloat16)
    level_of = jnp.arange(chans, dtype=jnp.int32) * LEVELS // chans
    wet_mask = (level_of[None, None, :] < kmt[:, :, None]).astype(jnp.float32)
    rows = lon_dev * lat_rows
    pre_acts = []
    hiddens = []
    outputs = []
    for member in range(members):
        flat_rows = normed[member].reshape(rows, chans)
        pre_act = jnp.dot(flat_rows, w_in, preferred_element_type=jnp.float32) + b_in
        hidden = jax.nn.gelu(pre_act).astype(jnp.bfloat16)
        pre_acts.append(pre_act)
        hiddens.append(hidden)
        outputs.append(
            (jnp.dot(hidden, w_out, preferred_element_type=jnp.float32) + b_out).reshape(
                lon_dev, lat_rows, chans
            )
        )
    branch = jnp.stack(outputs)
    pred = wet_mask * (features.astype(jnp.float32) + layer_scale * branch)
    target_full = target.astype(jnp.float32)
    pair_weight = 1.0 / (members * (members - 1))
    skill = jnp.zeros(target.shape, jnp.float32)
    spread = jnp.zeros(target.shape, jnp.float32)
    for member in range(members):
        skill = skill + smooth_abs(pred[member] - target_full)
        for other in range(member + 1, members):
            spread = spread + smooth_abs(pred[member] - pred[other])
    crps_field = wet_mask * (skill / members - pair_weight * spread)
    grad_list = []
    for member in range(members):
        slope_sum = jnp.zeros(target.shape, jnp.float32)
        for other in range(members):
            if other != member:
                slope_sum = slope_sum + smooth_slope(pred[member] - pred[other])
        grad_list.append(
            wet_mask
            * (smooth_slope(pred[member] - target_full) / members - pair_weight * slope_sum)
        )
    grad_pred = jnp.stack(grad_list)
    grad_scale = jnp.sum(grad_pred * branch, axis=(0, 1, 2))
    grad_b_out = jnp.zeros((chans,), jnp.float32)
    grad_w_out = jnp.zeros(w_out.shape, jnp.float32)
    grad_b_in = jnp.zeros(b_in.shape, jnp.float32)
    grad_w_in = jnp.zeros(w_in.shape, jnp.float32)
    normed_grads = []
    contract_rows = (((0,), (0,)), ((), ()))
    contract_cols = (((1,), (1,)), ((), ()))
    for member in range(members):
        grad_out = (grad_pred[member] * layer_scale).reshape(rows, chans)
        grad_b_out = grad_b_out + jnp.sum(grad_out, axis=0)
        out_half = grad_out.astype(jnp.bfloat16)
        grad_w_out = grad_w_out + lax.dot_general(
            hiddens[member], out_half, contract_rows, preferred_element_type=jnp.float32
        )
        grad_hidden = lax.dot_general(
            out_half, w_out, contract_cols, preferred_element_type=jnp.float32
        )
        grad_pre = jax.vjp(jax.nn.gelu, pre_acts[member])[1](grad_hidden)[0]
        grad_b_in = grad_b_in + jnp.sum(grad_pre, axis=0)
        pre_half = grad_pre.astype(jnp.bfloat16)
        grad_w_in = grad_w_in + lax.dot_general(
            normed[member].reshape(rows, chans),
            pre_half,
            contract_rows,
            preferred_element_type=jnp.float32,
        )
        normed_grads.append(
            lax.dot_general(
                pre_half, w_in, contract_cols, preferred_element_type=jnp.float32
            ).reshape(lon_dev, lat_rows, chans)
        )
    grad_normed = jnp.stack(normed_grads)
    grad_ln_gain = jnp.sum(grad_normed * unit, axis=(0, 1, 2))
    grad_ln_bias = jnp.sum(grad_normed, axis=(0, 1, 2))
    grad_unit = grad_normed * ln_gain
    grad_depth = inv_std * (
        grad_unit
        - jnp.mean(grad_unit, axis=-1, keepdims=True)
        - unit * jnp.mean(grad_unit * unit, axis=-1, keepdims=True)
    )
    grad_dw_bias = jnp.sum(grad_depth, axis=(0, 1, 2))
    kernel_rows = []
    for lon_off in range(7):
        kernel_cols = []
        for lat_off in range(7):
            kernel_cols.append(
                jnp.sum(
                    grad_depth
                    * extended[
                        :, lon_off : lon_off + lon_dev, lat_off : lat_off + lat_rows, :
                    ].astype(jnp.float32),
                    axis=(0, 1, 2),
                )
            )
        kernel_rows.append(jnp.stack(kernel_cols))
    grad_kernel = jnp.stack(kernel_rows)
    grads = (
        grad_kernel,
        grad_dw_bias,
        grad_ln_gain,
        grad_ln_bias,
        grad_w_in,
        grad_b_in,
        grad_w_out,
        grad_b_out,
        grad_scale,
    )
    return (pred.astype(jnp.bfloat16), crps_field, grad_pred, grad_depth, grads)


def mirrored(x, axis):
    size = lax.axis_size(axis)
    return lax.ppermute(x, axis, [(i, size - 1 - i) for i in range(size)])


def mirror_rows(top_rows):
    return mirrored(top_rows, "lon")[:, ::-1, ::-1, :]


def mirror_grads(fold_rows):
    picked = mirrored(fold_rows.astype(jnp.bfloat16), "lon").astype(fold_rows.dtype)
    return picked[:, ::-1, ::-1, :]


def halving_allreduce(flat, axis, gather_dtype):
    size = lax.axis_size(axis)
    bits = size.bit_length() - 1
    idx = lax.axis_index(axis)
    cur = flat
    for bit in range(bits):
        half = cur.shape[0] // 2
        mine = (idx >> bit) & 1
        keep = lax.dynamic_slice_in_dim(cur, mine * half, half)
        send = lax.dynamic_slice_in_dim(cur, (1 - mine) * half, half)
        cur = keep + swapped(send, axis, bit)
    cur = cur.astype(gather_dtype)
    for bit in reversed(range(bits)):
        mine = (idx >> bit) & 1
        recv = swapped(cur, axis, bit)
        cur = jnp.where(mine == 0, jnp.concatenate([cur, recv]), jnp.concatenate([recv, cur]))
    return cur.astype(flat.dtype)


def radix_allreduce(block, axis, gather_dtype):
    size = lax.axis_size(axis)
    nbits = size.bit_length() - 1
    groups = [[0]] + [list(range(b, min(b + 2, nbits))) for b in range(1, nbits, 2)]
    idx = lax.axis_index(axis)
    cur = block
    dims = []
    for bits in groups:
        radix, low = 1 << len(bits), bits[0]
        sub = (idx >> low) & (radix - 1)
        dim = 1 if cur.shape[1] // radix >= 128 else 0
        part = cur.shape[dim] // radix
        total = lax.dynamic_slice_in_dim(cur, sub * part, part, axis=dim)
        for d in range(1, radix):
            send = lax.dynamic_slice_in_dim(cur, (sub ^ d) * part, part, axis=dim)
            total = total + lax.ppermute(send, axis, [(i, i ^ (d << low)) for i in range(size)])
        cur = total
        dims.append(dim)
    cur = cur.astype(gather_dtype)
    for bits, dim in reversed(list(zip(groups, dims))):
        radix, low = 1 << len(bits), bits[0]
        sub = (idx >> low) & (radix - 1)
        pieces = [cur] + [
            lax.ppermute(cur, axis, [(i, i ^ (d << low)) for i in range(size)])
            for d in range(1, radix)
        ]
        placed = []
        for p in range(radix):
            pick = pieces[p ^ (radix - 1)]
            for s in range(radix - 1):
                pick = jnp.where(sub == s, pieces[p ^ s], pick)
            placed.append(pick)
        cur = jnp.concatenate(placed, axis=dim)
    return cur.astype(block.dtype)


def butterfly_allreduce(flat, axis):
    for bit in range(lax.axis_size(axis).bit_length() - 1):
        flat = flat + swapped(flat, axis, bit)
    return flat


def pack(arrays, multiple):
    flat = jnp.concatenate([a.reshape(-1) for a in arrays])
    extra = -flat.shape[0] % multiple
    return jnp.pad(flat, (0, extra))


def unpack(flat, arrays):
    out, at = [], 0
    for a in arrays:
        out.append(flat[at : at + a.size].reshape(a.shape))
        at += a.size
    return out


def on_device(
    features,
    target,
    south_rim,
    kmt,
    dw_kernel,
    dw_bias,
    ln_gain,
    ln_bias,
    w_in,
    b_in,
    w_out,
    b_out,
    layer_scale,
):
    members, lon_dev, lat_rows, chans = features.shape
    params = (dw_kernel, dw_bias, ln_gain, ln_bias, w_in, b_in, w_out, b_out, layer_scale)
    north_rows = mirror_rows(features[:, :, lat_rows - 3 :, :])
    joined = jnp.concatenate([south_rim, features, north_rows], axis=2)
    extended = with_halo(joined, (("lon", 1),), 3)
    predicted, crps_field, grad_pred, grad_depth, grads = local_step(
        extended, features, target, kmt, *params
    )
    grad_halo = with_halo(grad_depth, (("lon", 1),), 3)
    padded = jnp.pad(grad_halo, ((0, 0), (0, 0), (6, 6), (0, 0)))
    grad_ext = jnp.zeros((members, lon_dev, lat_rows + 6, chans), jnp.float32)
    for lon_off in range(7):
        for lat_off in range(7):
            grad_ext = (
                grad_ext
                + dw_kernel[lon_off, lat_off]
                * padded[
                    :,
                    6 - lon_off : 6 - lon_off + lon_dev,
                    6 - lat_off : 6 - lat_off + lat_rows + 6,
                    :,
                ]
            )
    back_rows = mirror_grads(grad_ext[:, :, lat_rows + 3 :, :])
    inner = grad_pred + grad_ext[:, :, 3 : lat_rows + 3, :]
    grad_features = jnp.concatenate(
        [inner[:, :, : lat_rows - 3, :], inner[:, :, lat_rows - 3 :, :] + back_rows], axis=2
    ).astype(jnp.bfloat16)
    (
        kernel_sum,
        dw_bias_sum,
        gain_sum,
        bias_sum,
        w_in_sum,
        b_in_sum,
        w_out_sum,
        b_out_sum,
        scale_sum,
    ) = grads
    lon_size = lax.axis_size("lon")
    small = (kernel_sum, dw_bias_sum, gain_sum, bias_sum, b_in_sum, b_out_sum, scale_sum)
    width = w_in_sum.shape[1]
    big_rows = (w_in_sum.size + w_out_sum.size) // width
    small_rows = -(-sum(a.size for a in small) // width)
    small_rows += -(big_rows + small_rows) % lon_size
    block = jnp.concatenate(
        [
            w_in_sum,
            w_out_sum.reshape(-1, width),
            pack(small, small_rows * width).reshape(small_rows, width),
        ]
    )
    block = radix_allreduce(block, "lon", jnp.bfloat16)
    small_tot = unpack(block[big_rows:].reshape(-1), small)
    totals = (
        small_tot[0],
        small_tot[1],
        small_tot[2],
        small_tot[3],
        block[: w_in_sum.shape[0]],
        small_tot[4],
        block[w_in_sum.shape[0] : big_rows].reshape(w_out_sum.shape),
        small_tot[5],
        small_tot[6],
    )
    factor = 1.0 / math.sqrt(members * lat_rows * lon_dev * lax.axis_size("lon"))
    return (
        predicted,
        crps_field,
        grad_features,
        totals[0] * factor,
        totals[1] * factor,
        totals[2] * factor,
        totals[3] * factor,
        totals[4] * factor,
        totals[5] * factor,
        totals[6] * factor,
        totals[7] * factor,
        totals[8] * factor,
    )


def solution(mesh):
    placed = (
        P(None, ("groups", "lon"), None, None),
        P(("groups", "lon"), None, None),
        P(None, ("groups", "lon"), None, None),
        P(("groups", "lon"), None),
        P(),
        P(),
        P(),
        P(),
        P(),
        P(),
        P(),
        P(),
        P(),
    )
    return jax.shard_map(
        on_device,
        mesh=mesh,
        in_specs=placed,
        out_specs=(
            P(None, ("groups", "lon"), None, None),
            P(("groups", "lon"), None, None),
            P(None, ("groups", "lon"), None, None),
            P("groups", None, None),
            P("groups"),
            P("groups"),
            P("groups"),
            P("groups", None),
            P("groups"),
            P("groups", None),
            P("groups"),
            P("groups"),
        ),
        check_vma=False,
    )
```

```python
import math

import jax
import jax.numpy as jnp
from jax import lax
from jax.sharding import PartitionSpec as P

LEVELS = 19


SMOOTH = 0.25
EPSILON = 1e-06


def swapped(x, axis, bit):
    return lax.ppermute(x, axis, [(i, i ^ 1 << bit) for i in range(lax.axis_size(axis))])


def with_halo(x, sides, width):
    for axis, dim in sides:
        size, length = (lax.axis_size(axis), x.shape[dim])
        up = [(i, (i + 1) % size) for i in range(size)]
        down = [(j, i) for i, j in up]
        last = lax.slice_in_dim(x, length - width, length, axis=dim)
        leading = lax.slice_in_dim(x, 0, width, axis=dim)
        before = lax.ppermute(last, axis, up)
        after = lax.ppermute(leading, axis, down)
        x = jnp.concatenate([before, x, after], axis=dim)
    return x


def smooth_abs(value):
    return jnp.sqrt(value * value + SMOOTH * SMOOTH) - SMOOTH


def smooth_slope(value):
    return value / jnp.sqrt(value * value + SMOOTH * SMOOTH)


def local_step(
    extended,
    features,
    target,
    kmt,
    dw_kernel,
    dw_bias,
    ln_gain,
    ln_bias,
    w_in,
    b_in,
    w_out,
    b_out,
    layer_scale,
):
    members, lon_dev, lat_rows, chans = features.shape
    depth = jnp.zeros(features.shape, jnp.float32) + dw_bias
    for lon_off in range(7):
        for lat_off in range(7):
            depth = depth + dw_kernel[lon_off, lat_off] * extended[
                :, lon_off : lon_off + lon_dev, lat_off : lat_off + lat_rows, :
            ].astype(jnp.float32)
    mean_val = jnp.mean(depth, axis=-1, keepdims=True)
    centred = depth - mean_val
    variance = jnp.mean(centred * centred, axis=-1, keepdims=True)
    inv_std = lax.rsqrt(variance + EPSILON)
    unit = centred * inv_std
    normed = (unit * ln_gain + ln_bias).astype(jnp.bfloat16)
    level_of = jnp.arange(chans, dtype=jnp.int32) * LEVELS // chans
    wet_mask = (level_of[None, None, :] < kmt[:, :, None]).astype(jnp.float32)
    rows = lon_dev * lat_rows
    pre_acts = []
    hiddens = []
    outputs = []
    for member in range(members):
        flat_rows = normed[member].reshape(rows, chans)
        pre_act = jnp.dot(flat_rows, w_in, preferred_element_type=jnp.float32) + b_in
        hidden = jax.nn.gelu(pre_act).astype(jnp.bfloat16)
        pre_acts.append(pre_act)
        hiddens.append(hidden)
        outputs.append(
            (jnp.dot(hidden, w_out, preferred_element_type=jnp.float32) + b_out).reshape(
                lon_dev, lat_rows, chans
            )
        )
    branch = jnp.stack(outputs)
    pred = wet_mask * (features.astype(jnp.float32) + layer_scale * branch)
    target_full = target.astype(jnp.float32)
    pair_weight = 1.0 / (members * (members - 1))
    skill = jnp.zeros(target.shape, jnp.float32)
    spread = jnp.zeros(target.shape, jnp.float32)
    for member in range(members):
        skill = skill + smooth_abs(pred[member] - target_full)
        for other in range(member + 1, members):
            spread = spread + smooth_abs(pred[member] - pred[other])
    crps_field = wet_mask * (skill / members - pair_weight * spread)
    grad_list = []
    for member in range(members):
        slope_sum = jnp.zeros(target.shape, jnp.float32)
        for other in range(members):
            if other != member:
                slope_sum = slope_sum + smooth_slope(pred[member] - pred[other])
        grad_list.append(
            wet_mask
            * (smooth_slope(pred[member] - target_full) / members - pair_weight * slope_sum)
        )
    grad_pred = jnp.stack(grad_list)
    grad_scale = jnp.sum(grad_pred * branch, axis=(0, 1, 2))
    grad_b_out = jnp.zeros((chans,), jnp.float32)
    grad_w_out = jnp.zeros(w_out.shape, jnp.float32)
    grad_b_in = jnp.zeros(b_in.shape, jnp.float32)
    grad_w_in = jnp.zeros(w_in.shape, jnp.float32)
    normed_grads = []
    contract_rows = (((0,), (0,)), ((), ()))
    contract_cols = (((1,), (1,)), ((), ()))
    for member in range(members):
        grad_out = (grad_pred[member] * layer_scale).reshape(rows, chans)
        grad_b_out = grad_b_out + jnp.sum(grad_out, axis=0)
        out_half = grad_out.astype(jnp.bfloat16)
        grad_w_out = grad_w_out + lax.dot_general(
            hiddens[member], out_half, contract_rows, preferred_element_type=jnp.float32
        )
        grad_hidden = lax.dot_general(
            out_half, w_out, contract_cols, preferred_element_type=jnp.float32
        )
        grad_pre = jax.vjp(jax.nn.gelu, pre_acts[member])[1](grad_hidden)[0]
        grad_b_in = grad_b_in + jnp.sum(grad_pre, axis=0)
        pre_half = grad_pre.astype(jnp.bfloat16)
        grad_w_in = grad_w_in + lax.dot_general(
            normed[member].reshape(rows, chans),
            pre_half,
            contract_rows,
            preferred_element_type=jnp.float32,
        )
        normed_grads.append(
            lax.dot_general(
                pre_half, w_in, contract_cols, preferred_element_type=jnp.float32
            ).reshape(lon_dev, lat_rows, chans)
        )
    grad_normed = jnp.stack(normed_grads)
    grad_ln_gain = jnp.sum(grad_normed * unit, axis=(0, 1, 2))
    grad_ln_bias = jnp.sum(grad_normed, axis=(0, 1, 2))
    grad_unit = grad_normed * ln_gain
    grad_depth = inv_std * (
        grad_unit
        - jnp.mean(grad_unit, axis=-1, keepdims=True)
        - unit * jnp.mean(grad_unit * unit, axis=-1, keepdims=True)
    )
    grad_dw_bias = jnp.sum(grad_depth, axis=(0, 1, 2))
    kernel_rows = []
    for lon_off in range(7):
        kernel_cols = []
        for lat_off in range(7):
            kernel_cols.append(
                jnp.sum(
                    grad_depth
                    * extended[
                        :, lon_off : lon_off + lon_dev, lat_off : lat_off + lat_rows, :
                    ].astype(jnp.float32),
                    axis=(0, 1, 2),
                )
            )
        kernel_rows.append(jnp.stack(kernel_cols))
    grad_kernel = jnp.stack(kernel_rows)
    grads = (
        grad_kernel,
        grad_dw_bias,
        grad_ln_gain,
        grad_ln_bias,
        grad_w_in,
        grad_b_in,
        grad_w_out,
        grad_b_out,
        grad_scale,
    )
    return (pred.astype(jnp.bfloat16), crps_field, grad_pred, grad_depth, grads)


def mirrored(x, axis):
    size = lax.axis_size(axis)
    return lax.ppermute(x, axis, [(i, size - 1 - i) for i in range(size)])


def mirror_rows(top_rows):
    return mirrored(top_rows, "lon")[:, ::-1, ::-1, :]


def mirror_grads(fold_rows):
    picked = mirrored(fold_rows.astype(jnp.bfloat16), "lon").astype(fold_rows.dtype)
    return picked[:, ::-1, ::-1, :]


def halving_allreduce(flat, axis, gather_dtype):
    size = lax.axis_size(axis)
    bits = size.bit_length() - 1
    idx = lax.axis_index(axis)
    cur = flat
    for bit in range(bits):
        half = cur.shape[0] // 2
        mine = (idx >> bit) & 1
        keep = lax.dynamic_slice_in_dim(cur, mine * half, half)
        send = lax.dynamic_slice_in_dim(cur, (1 - mine) * half, half)
        cur = keep + swapped(send, axis, bit)
    cur = cur.astype(gather_dtype)
    for bit in reversed(range(bits)):
        mine = (idx >> bit) & 1
        recv = swapped(cur, axis, bit)
        cur = jnp.where(mine == 0, jnp.concatenate([cur, recv]), jnp.concatenate([recv, cur]))
    return cur.astype(flat.dtype)


def radix_allreduce(flat, axis, gather_dtype, operand, work):
    size = lax.axis_size(axis)
    nbits = size.bit_length() - 1
    groups = [[0]] + [list(range(b, min(b + 2, nbits))) for b in range(1, nbits, 2)]
    idx = lax.axis_index(axis)
    cur = flat
    for bits in groups:
        radix, low = 1 << len(bits), bits[0]
        sub = (idx >> low) & (radix - 1)
        part = cur.shape[0] // radix
        total = lax.dynamic_slice_in_dim(cur, sub * part, part)
        for d in range(1, radix):
            send = lax.dynamic_slice_in_dim(cur, (sub ^ d) * part, part)
            total = total + lax.ppermute(send, axis, [(i, i ^ (d << low)) for i in range(size)])
        cur = total
        if bits == groups[0]:
            cur, operand = lax.optimization_barrier((cur, operand))
            result = work(operand)
        elif bits == groups[1]:
            cur, result = lax.optimization_barrier((cur, result))
    cur = cur.astype(gather_dtype)
    for bits in reversed(groups):
        radix, low = 1 << len(bits), bits[0]
        sub = (idx >> low) & (radix - 1)
        pieces = [cur] + [
            lax.ppermute(cur, axis, [(i, i ^ (d << low)) for i in range(size)])
            for d in range(1, radix)
        ]
        placed = []
        for p in range(radix):
            pick = pieces[p ^ (radix - 1)]
            for s in range(radix - 1):
                pick = jnp.where(sub == s, pieces[p ^ s], pick)
            placed.append(pick)
        cur = jnp.concatenate(placed)
    return cur.astype(flat.dtype), result


def butterfly_allreduce(flat, axis):
    for bit in range(lax.axis_size(axis).bit_length() - 1):
        flat = flat + swapped(flat, axis, bit)
    return flat


def pack(arrays, multiple):
    flat = jnp.concatenate([a.reshape(-1) for a in arrays])
    extra = -flat.shape[0] % multiple
    return jnp.pad(flat, (0, extra))


def unpack(flat, arrays):
    out, at = [], 0
    for a in arrays:
        out.append(flat[at : at + a.size].reshape(a.shape))
        at += a.size
    return out


def on_device(
    features,
    target,
    south_rim,
    kmt,
    dw_kernel,
    dw_bias,
    ln_gain,
    ln_bias,
    w_in,
    b_in,
    w_out,
    b_out,
    layer_scale,
):
    members, lon_dev, lat_rows, chans = features.shape
    params = (dw_kernel, dw_bias, ln_gain, ln_bias, w_in, b_in, w_out, b_out, layer_scale)
    north_rows = mirror_rows(features[:, :, lat_rows - 3 :, :])
    joined = jnp.concatenate([south_rim, features, north_rows], axis=2)
    extended = with_halo(joined, (("lon", 1),), 3)
    predicted, crps_field, grad_pred, grad_depth, grads = local_step(
        extended, features, target, kmt, *params
    )
    grad_halo = with_halo(grad_depth, (("lon", 1),), 3)
    padded = jnp.pad(grad_halo, ((0, 0), (0, 0), (6, 6), (0, 0)))

    def backward_conv(operand):
        grad_ext = jnp.zeros((members, lon_dev, lat_rows + 6, chans), jnp.float32)
        for lon_off in range(7):
            for lat_off in range(7):
                grad_ext = (
                    grad_ext
                    + dw_kernel[lon_off, lat_off]
                    * operand[
                        :,
                        6 - lon_off : 6 - lon_off + lon_dev,
                        6 - lat_off : 6 - lat_off + lat_rows + 6,
                        :,
                    ]
                )
        return grad_ext

    (
        kernel_sum,
        dw_bias_sum,
        gain_sum,
        bias_sum,
        w_in_sum,
        b_in_sum,
        w_out_sum,
        b_out_sum,
        scale_sum,
    ) = grads
    lon_size = lax.axis_size("lon")
    sums = (
        kernel_sum,
        dw_bias_sum,
        gain_sum,
        bias_sum,
        w_in_sum,
        b_in_sum,
        w_out_sum,
        b_out_sum,
        scale_sum,
    )
    reduced, grad_ext = radix_allreduce(
        pack(sums, lon_size * 1024), "lon", jnp.bfloat16, padded, backward_conv
    )
    totals = unpack(reduced, sums)
    back_rows = mirror_grads(grad_ext[:, :, lat_rows + 3 :, :])
    inner = grad_pred + grad_ext[:, :, 3 : lat_rows + 3, :]
    grad_features = jnp.concatenate(
        [inner[:, :, : lat_rows - 3, :], inner[:, :, lat_rows - 3 :, :] + back_rows], axis=2
    ).astype(jnp.bfloat16)
    factor = 1.0 / math.sqrt(members * lat_rows * lon_dev * lax.axis_size("lon"))
    return (
        predicted,
        crps_field,
        grad_features,
        totals[0] * factor,
        totals[1] * factor,
        totals[2] * factor,
        totals[3] * factor,
        totals[4] * factor,
        totals[5] * factor,
        totals[6] * factor,
        totals[7] * factor,
        totals[8] * factor,
    )


def solution(mesh):
    placed = (
        P(None, ("groups", "lon"), None, None),
        P(("groups", "lon"), None, None),
        P(None, ("groups", "lon"), None, None),
        P(("groups", "lon"), None),
        P(),
        P(),
        P(),
        P(),
        P(),
        P(),
        P(),
        P(),
        P(),
    )
    return jax.shard_map(
        on_device,
        mesh=mesh,
        in_specs=placed,
        out_specs=(
            P(None, ("groups", "lon"), None, None),
            P(("groups", "lon"), None, None),
            P(None, ("groups", "lon"), None, None),
            P("groups", None, None),
            P("groups"),
            P("groups"),
            P("groups"),
            P("groups", None),
            P("groups"),
            P("groups", None),
            P("groups"),
            P("groups"),
        ),
        check_vma=False,
    )
```

```python
import math

import jax
import jax.numpy as jnp
from jax import lax
from jax.sharding import PartitionSpec as P

LEVELS = 19


SMOOTH = 0.25
EPSILON = 1e-06


def swapped(x, axis, bit):
    return lax.ppermute(x, axis, [(i, i ^ 1 << bit) for i in range(lax.axis_size(axis))])


def with_halo(x, sides, width):
    for axis, dim in sides:
        size, length = (lax.axis_size(axis), x.shape[dim])
        up = [(i, (i + 1) % size) for i in range(size)]
        down = [(j, i) for i, j in up]
        last = lax.slice_in_dim(x, length - width, length, axis=dim)
        leading = lax.slice_in_dim(x, 0, width, axis=dim)
        before = lax.ppermute(last, axis, up)
        after = lax.ppermute(leading, axis, down)
        x = jnp.concatenate([before, x, after], axis=dim)
    return x


def smooth_abs(value):
    return jnp.sqrt(value * value + SMOOTH * SMOOTH) - SMOOTH


def smooth_slope(value):
    return value / jnp.sqrt(value * value + SMOOTH * SMOOTH)


def local_step(
    extended,
    features,
    target,
    kmt,
    dw_kernel,
    dw_bias,
    ln_gain,
    ln_bias,
    w_in,
    b_in,
    w_out,
    b_out,
    layer_scale,
):
    members, lon_dev, lat_rows, chans = features.shape
    depth = jnp.zeros(features.shape, jnp.float32) + dw_bias
    for lon_off in range(7):
        for lat_off in range(7):
            depth = depth + dw_kernel[lon_off, lat_off] * extended[
                :, lon_off : lon_off + lon_dev, lat_off : lat_off + lat_rows, :
            ].astype(jnp.float32)
    mean_val = jnp.mean(depth, axis=-1, keepdims=True)
    centred = depth - mean_val
    variance = jnp.mean(centred * centred, axis=-1, keepdims=True)
    inv_std = lax.rsqrt(variance + EPSILON)
    unit = centred * inv_std
    normed = (unit * ln_gain + ln_bias).astype(jnp.bfloat16)
    level_of = jnp.arange(chans, dtype=jnp.int32) * LEVELS // chans
    wet_mask = (level_of[None, None, :] < kmt[:, :, None]).astype(jnp.float32)
    rows = lon_dev * lat_rows
    pre_acts = []
    hiddens = []
    outputs = []
    for member in range(members):
        flat_rows = normed[member].reshape(rows, chans)
        pre_act = jnp.dot(flat_rows, w_in, preferred_element_type=jnp.float32) + b_in
        hidden = jax.nn.gelu(pre_act).astype(jnp.bfloat16)
        pre_acts.append(pre_act)
        hiddens.append(hidden)
        outputs.append(
            (jnp.dot(hidden, w_out, preferred_element_type=jnp.float32) + b_out).reshape(
                lon_dev, lat_rows, chans
            )
        )
    branch = jnp.stack(outputs)
    pred = wet_mask * (features.astype(jnp.float32) + layer_scale * branch)
    target_full = target.astype(jnp.float32)
    pair_weight = 1.0 / (members * (members - 1))
    skill = jnp.zeros(target.shape, jnp.float32)
    spread = jnp.zeros(target.shape, jnp.float32)
    for member in range(members):
        skill = skill + smooth_abs(pred[member] - target_full)
        for other in range(member + 1, members):
            spread = spread + smooth_abs(pred[member] - pred[other])
    crps_field = wet_mask * (skill / members - pair_weight * spread)
    grad_list = []
    for member in range(members):
        slope_sum = jnp.zeros(target.shape, jnp.float32)
        for other in range(members):
            if other != member:
                slope_sum = slope_sum + smooth_slope(pred[member] - pred[other])
        grad_list.append(
            wet_mask
            * (smooth_slope(pred[member] - target_full) / members - pair_weight * slope_sum)
        )
    grad_pred = jnp.stack(grad_list)
    grad_scale = jnp.sum(grad_pred * branch, axis=(0, 1, 2))
    grad_b_out = jnp.zeros((chans,), jnp.float32)
    grad_w_out = jnp.zeros(w_out.shape, jnp.float32)
    grad_b_in = jnp.zeros(b_in.shape, jnp.float32)
    grad_w_in = jnp.zeros(w_in.shape, jnp.float32)
    normed_grads = []
    contract_rows = (((0,), (0,)), ((), ()))
    contract_cols = (((1,), (1,)), ((), ()))
    for member in range(members):
        grad_out = (grad_pred[member] * layer_scale).reshape(rows, chans)
        grad_b_out = grad_b_out + jnp.sum(grad_out, axis=0)
        out_half = grad_out.astype(jnp.bfloat16)
        grad_w_out = grad_w_out + lax.dot_general(
            hiddens[member], out_half, contract_rows, preferred_element_type=jnp.float32
        )
        grad_hidden = lax.dot_general(
            out_half, w_out, contract_cols, preferred_element_type=jnp.float32
        )
        grad_pre = jax.vjp(jax.nn.gelu, pre_acts[member])[1](grad_hidden)[0]
        grad_b_in = grad_b_in + jnp.sum(grad_pre, axis=0)
        pre_half = grad_pre.astype(jnp.bfloat16)
        grad_w_in = grad_w_in + lax.dot_general(
            normed[member].reshape(rows, chans),
            pre_half,
            contract_rows,
            preferred_element_type=jnp.float32,
        )
        normed_grads.append(
            lax.dot_general(
                pre_half, w_in, contract_cols, preferred_element_type=jnp.float32
            ).reshape(lon_dev, lat_rows, chans)
        )
    grad_normed = jnp.stack(normed_grads)
    grad_ln_gain = jnp.sum(grad_normed * unit, axis=(0, 1, 2))
    grad_ln_bias = jnp.sum(grad_normed, axis=(0, 1, 2))

    def depth_backward(grad_normed):
        grad_unit = grad_normed * ln_gain
        grad_depth = inv_std * (
            grad_unit
            - jnp.mean(grad_unit, axis=-1, keepdims=True)
            - unit * jnp.mean(grad_unit * unit, axis=-1, keepdims=True)
        )
        grad_dw_bias = jnp.sum(grad_depth, axis=(0, 1, 2))
        kernel_rows = []
        for lon_off in range(7):
            kernel_cols = []
            for lat_off in range(7):
                kernel_cols.append(
                    jnp.sum(
                        grad_depth
                        * extended[
                            :, lon_off : lon_off + lon_dev, lat_off : lat_off + lat_rows, :
                        ].astype(jnp.float32),
                        axis=(0, 1, 2),
                    )
                )
            kernel_rows.append(jnp.stack(kernel_cols))
        grad_kernel = jnp.stack(kernel_rows)
        return grad_depth, grad_kernel, grad_dw_bias

    sums = (grad_ln_gain, grad_ln_bias, grad_w_in, grad_b_in, grad_w_out, grad_b_out, grad_scale)
    return (pred.astype(jnp.bfloat16), crps_field, grad_pred, grad_normed, sums, depth_backward)


def mirrored(x, axis):
    size = lax.axis_size(axis)
    return lax.ppermute(x, axis, [(i, size - 1 - i) for i in range(size)])


def mirror_rows(top_rows):
    return mirrored(top_rows, "lon")[:, ::-1, ::-1, :]


def mirror_grads(fold_rows):
    picked = mirrored(fold_rows.astype(jnp.bfloat16), "lon").astype(fold_rows.dtype)
    return picked[:, ::-1, ::-1, :]


def halving_allreduce(flat, axis, gather_dtype):
    size = lax.axis_size(axis)
    bits = size.bit_length() - 1
    idx = lax.axis_index(axis)
    cur = flat
    for bit in range(bits):
        half = cur.shape[0] // 2
        mine = (idx >> bit) & 1
        keep = lax.dynamic_slice_in_dim(cur, mine * half, half)
        send = lax.dynamic_slice_in_dim(cur, (1 - mine) * half, half)
        cur = keep + swapped(send, axis, bit)
    cur = cur.astype(gather_dtype)
    for bit in reversed(range(bits)):
        mine = (idx >> bit) & 1
        recv = swapped(cur, axis, bit)
        cur = jnp.where(mine == 0, jnp.concatenate([cur, recv]), jnp.concatenate([recv, cur]))
    return cur.astype(flat.dtype)


def radix_allreduce(flat, axis, gather_dtype, operand, work):
    size = lax.axis_size(axis)
    nbits = size.bit_length() - 1
    groups = [[0]] + [list(range(b, min(b + 2, nbits))) for b in range(1, nbits, 2)]
    idx = lax.axis_index(axis)
    cur = flat
    for bits in groups:
        radix, low = 1 << len(bits), bits[0]
        sub = (idx >> low) & (radix - 1)
        part = cur.shape[0] // radix
        total = lax.dynamic_slice_in_dim(cur, sub * part, part)
        for d in range(1, radix):
            send = lax.dynamic_slice_in_dim(cur, (sub ^ d) * part, part)
            total = total + lax.ppermute(send, axis, [(i, i ^ (d << low)) for i in range(size)])
        cur = total
        if bits == groups[0]:
            cur, operand = lax.optimization_barrier((cur, operand))
            result = work(operand)
        elif bits == groups[1]:
            cur, first = lax.optimization_barrier((cur, result[0]))
            result = (first,) + tuple(result[1:])
    cur = cur.astype(gather_dtype)
    for bits in reversed(groups):
        radix, low = 1 << len(bits), bits[0]
        sub = (idx >> low) & (radix - 1)
        pieces = [cur] + [
            lax.ppermute(cur, axis, [(i, i ^ (d << low)) for i in range(size)])
            for d in range(1, radix)
        ]
        placed = []
        for p in range(radix):
            pick = pieces[p ^ (radix - 1)]
            for s in range(radix - 1):
                pick = jnp.where(sub == s, pieces[p ^ s], pick)
            placed.append(pick)
        cur = jnp.concatenate(placed)
    return cur.astype(flat.dtype), result


def butterfly_allreduce(flat, axis):
    for bit in range(lax.axis_size(axis).bit_length() - 1):
        flat = flat + swapped(flat, axis, bit)
    return flat


def pack(arrays, multiple):
    flat = jnp.concatenate([a.reshape(-1) for a in arrays])
    extra = -flat.shape[0] % multiple
    return jnp.pad(flat, (0, extra))


def unpack(flat, arrays):
    out, at = [], 0
    for a in arrays:
        out.append(flat[at : at + a.size].reshape(a.shape))
        at += a.size
    return out


def on_device(
    features,
    target,
    south_rim,
    kmt,
    dw_kernel,
    dw_bias,
    ln_gain,
    ln_bias,
    w_in,
    b_in,
    w_out,
    b_out,
    layer_scale,
):
    members, lon_dev, lat_rows, chans = features.shape
    params = (dw_kernel, dw_bias, ln_gain, ln_bias, w_in, b_in, w_out, b_out, layer_scale)
    north_rows = mirror_rows(features[:, :, lat_rows - 3 :, :])
    joined = jnp.concatenate([south_rim, features, north_rows], axis=2)
    extended = with_halo(joined, (("lon", 1),), 3)
    predicted, crps_field, grad_pred, grad_normed, sums, depth_backward = local_step(
        extended, features, target, kmt, *params
    )

    def backward(grad_normed):
        grad_depth, kernel_sum, dw_bias_sum = depth_backward(grad_normed)
        grad_halo = with_halo(grad_depth, (("lon", 1),), 3)
        padded = jnp.pad(grad_halo, ((0, 0), (0, 0), (6, 6), (0, 0)))
        grad_ext = jnp.zeros((members, lon_dev, lat_rows + 6, chans), jnp.float32)
        for lon_off in range(7):
            for lat_off in range(7):
                grad_ext = (
                    grad_ext
                    + dw_kernel[lon_off, lat_off]
                    * padded[
                        :,
                        6 - lon_off : 6 - lon_off + lon_dev,
                        6 - lat_off : 6 - lat_off + lat_rows + 6,
                        :,
                    ]
                )
        return grad_ext, kernel_sum, dw_bias_sum

    lon_size = lax.axis_size("lon")
    reduced, (grad_ext, kernel_sum, dw_bias_sum) = radix_allreduce(
        pack(sums, lon_size * 1024), "lon", jnp.bfloat16, grad_normed, backward
    )
    gain_sum, bias_sum, w_in_sum, b_in_sum, w_out_sum, b_out_sum, scale_sum = unpack(reduced, sums)
    small = (kernel_sum, dw_bias_sum)
    kernel_tot, dw_bias_tot = unpack(butterfly_allreduce(pack(small, 128), "lon"), small)
    totals = (
        kernel_tot,
        dw_bias_tot,
        gain_sum,
        bias_sum,
        w_in_sum,
        b_in_sum,
        w_out_sum,
        b_out_sum,
        scale_sum,
    )
    back_rows = mirror_grads(grad_ext[:, :, lat_rows + 3 :, :])
    inner = grad_pred + grad_ext[:, :, 3 : lat_rows + 3, :]
    grad_features = jnp.concatenate(
        [inner[:, :, : lat_rows - 3, :], inner[:, :, lat_rows - 3 :, :] + back_rows], axis=2
    ).astype(jnp.bfloat16)
    factor = 1.0 / math.sqrt(members * lat_rows * lon_dev * lax.axis_size("lon"))
    return (
        predicted,
        crps_field,
        grad_features,
        totals[0] * factor,
        totals[1] * factor,
        totals[2] * factor,
        totals[3] * factor,
        totals[4] * factor,
        totals[5] * factor,
        totals[6] * factor,
        totals[7] * factor,
        totals[8] * factor,
    )


def solution(mesh):
    placed = (
        P(None, ("groups", "lon"), None, None),
        P(("groups", "lon"), None, None),
        P(None, ("groups", "lon"), None, None),
        P(("groups", "lon"), None),
        P(),
        P(),
        P(),
        P(),
        P(),
        P(),
        P(),
        P(),
        P(),
    )
    return jax.shard_map(
        on_device,
        mesh=mesh,
        in_specs=placed,
        out_specs=(
            P(None, ("groups", "lon"), None, None),
            P(("groups", "lon"), None, None),
            P(None, ("groups", "lon"), None, None),
            P("groups", None, None),
            P("groups"),
            P("groups"),
            P("groups"),
            P("groups", None),
            P("groups"),
            P("groups", None),
            P("groups"),
            P("groups"),
        ),
        check_vma=False,
    )
```

```python
import math

import jax
import jax.numpy as jnp
from jax import lax
from jax.sharding import PartitionSpec as P

LEVELS = 19


SMOOTH = 0.25
EPSILON = 1e-06


def swapped(x, axis, bit):
    return lax.ppermute(x, axis, [(i, i ^ 1 << bit) for i in range(lax.axis_size(axis))])


def with_halo(x, sides, width):
    for axis, dim in sides:
        size, length = (lax.axis_size(axis), x.shape[dim])
        up = [(i, (i + 1) % size) for i in range(size)]
        down = [(j, i) for i, j in up]
        last = lax.slice_in_dim(x, length - width, length, axis=dim)
        leading = lax.slice_in_dim(x, 0, width, axis=dim)
        before = lax.ppermute(last, axis, up)
        after = lax.ppermute(leading, axis, down)
        x = jnp.concatenate([before, x, after], axis=dim)
    return x


def smooth_abs(value):
    return jnp.sqrt(value * value + SMOOTH * SMOOTH) - SMOOTH


def smooth_slope(value):
    return value / jnp.sqrt(value * value + SMOOTH * SMOOTH)


def local_step(
    extended,
    features,
    target,
    kmt,
    dw_kernel,
    dw_bias,
    ln_gain,
    ln_bias,
    w_in,
    b_in,
    w_out,
    b_out,
    layer_scale,
):
    members, lon_dev, lat_rows, chans = features.shape
    depth = jnp.zeros(features.shape, jnp.float32) + dw_bias
    for lon_off in range(7):
        for lat_off in range(7):
            depth = depth + dw_kernel[lon_off, lat_off] * extended[
                :, lon_off : lon_off + lon_dev, lat_off : lat_off + lat_rows, :
            ].astype(jnp.float32)
    mean_val = jnp.mean(depth, axis=-1, keepdims=True)
    centred = depth - mean_val
    variance = jnp.mean(centred * centred, axis=-1, keepdims=True)
    inv_std = lax.rsqrt(variance + EPSILON)
    unit = centred * inv_std
    normed = (unit * ln_gain + ln_bias).astype(jnp.bfloat16)
    level_of = jnp.arange(chans, dtype=jnp.int32) * LEVELS // chans
    wet_mask = (level_of[None, None, :] < kmt[:, :, None]).astype(jnp.float32)
    rows = lon_dev * lat_rows
    pre_acts = []
    hiddens = []
    outputs = []
    for member in range(members):
        flat_rows = normed[member].reshape(rows, chans)
        pre_act = jnp.dot(flat_rows, w_in, preferred_element_type=jnp.float32) + b_in
        hidden = jax.nn.gelu(pre_act).astype(jnp.bfloat16)
        pre_acts.append(pre_act)
        hiddens.append(hidden)
        outputs.append(
            (jnp.dot(hidden, w_out, preferred_element_type=jnp.float32) + b_out).reshape(
                lon_dev, lat_rows, chans
            )
        )
    branch = jnp.stack(outputs)
    pred = wet_mask * (features.astype(jnp.float32) + layer_scale * branch)
    target_full = target.astype(jnp.float32)
    pair_weight = 1.0 / (members * (members - 1))
    skill = jnp.zeros(target.shape, jnp.float32)
    spread = jnp.zeros(target.shape, jnp.float32)
    for member in range(members):
        skill = skill + smooth_abs(pred[member] - target_full)
        for other in range(member + 1, members):
            spread = spread + smooth_abs(pred[member] - pred[other])
    crps_field = wet_mask * (skill / members - pair_weight * spread)
    grad_list = []
    for member in range(members):
        slope_sum = jnp.zeros(target.shape, jnp.float32)
        for other in range(members):
            if other != member:
                slope_sum = slope_sum + smooth_slope(pred[member] - pred[other])
        grad_list.append(
            wet_mask
            * (smooth_slope(pred[member] - target_full) / members - pair_weight * slope_sum)
        )
    grad_pred = jnp.stack(grad_list)
    grad_scale = jnp.sum(grad_pred * branch, axis=(0, 1, 2))
    grad_b_out = jnp.zeros((chans,), jnp.float32)
    grad_w_out = jnp.zeros(w_out.shape, jnp.float32)
    grad_b_in = jnp.zeros(b_in.shape, jnp.float32)
    grad_w_in = jnp.zeros(w_in.shape, jnp.float32)
    normed_grads = []
    contract_rows = (((0,), (0,)), ((), ()))
    contract_cols = (((1,), (1,)), ((), ()))
    for member in range(members):
        grad_out = (grad_pred[member] * layer_scale).reshape(rows, chans)
        grad_b_out = grad_b_out + jnp.sum(grad_out, axis=0)
        out_half = grad_out.astype(jnp.bfloat16)
        grad_w_out = grad_w_out + lax.dot_general(
            hiddens[member], out_half, contract_rows, preferred_element_type=jnp.float32
        )
        grad_hidden = lax.dot_general(
            out_half, w_out, contract_cols, preferred_element_type=jnp.float32
        )
        grad_pre = jax.vjp(jax.nn.gelu, pre_acts[member])[1](grad_hidden)[0]
        grad_b_in = grad_b_in + jnp.sum(grad_pre, axis=0)
        pre_half = grad_pre.astype(jnp.bfloat16)
        grad_w_in = grad_w_in + lax.dot_general(
            normed[member].reshape(rows, chans),
            pre_half,
            contract_rows,
            preferred_element_type=jnp.float32,
        )
        normed_grads.append(
            lax.dot_general(
                pre_half, w_in, contract_cols, preferred_element_type=jnp.float32
            ).reshape(lon_dev, lat_rows, chans)
        )
    grad_normed = jnp.stack(normed_grads)
    grad_ln_gain = jnp.sum(grad_normed * unit, axis=(0, 1, 2))
    grad_ln_bias = jnp.sum(grad_normed, axis=(0, 1, 2))

    def depth_backward(grad_normed):
        grad_unit = grad_normed * ln_gain
        grad_depth = inv_std * (
            grad_unit
            - jnp.mean(grad_unit, axis=-1, keepdims=True)
            - unit * jnp.mean(grad_unit * unit, axis=-1, keepdims=True)
        )
        grad_dw_bias = jnp.sum(grad_depth, axis=(0, 1, 2))
        kernel_rows = []
        for lon_off in range(7):
            kernel_cols = []
            for lat_off in range(7):
                kernel_cols.append(
                    jnp.sum(
                        grad_depth
                        * extended[
                            :, lon_off : lon_off + lon_dev, lat_off : lat_off + lat_rows, :
                        ].astype(jnp.float32),
                        axis=(0, 1, 2),
                    )
                )
            kernel_rows.append(jnp.stack(kernel_cols))
        grad_kernel = jnp.stack(kernel_rows)
        return grad_depth, grad_kernel, grad_dw_bias

    sums = (grad_ln_gain, grad_ln_bias, grad_w_in, grad_b_in, grad_w_out, grad_b_out, grad_scale)
    return (pred.astype(jnp.bfloat16), crps_field, grad_pred, grad_normed, sums, depth_backward)


def mirrored(x, axis):
    size = lax.axis_size(axis)
    return lax.ppermute(x, axis, [(i, size - 1 - i) for i in range(size)])


def mirror_rows(top_rows):
    return mirrored(top_rows, "lon")[:, ::-1, ::-1, :]


def mirror_grads(fold_rows):
    picked = mirrored(fold_rows.astype(jnp.bfloat16), "lon").astype(fold_rows.dtype)
    return picked[:, ::-1, ::-1, :]


def halving_allreduce(flat, axis, gather_dtype):
    size = lax.axis_size(axis)
    bits = size.bit_length() - 1
    idx = lax.axis_index(axis)
    cur = flat
    for bit in range(bits):
        half = cur.shape[0] // 2
        mine = (idx >> bit) & 1
        keep = lax.dynamic_slice_in_dim(cur, mine * half, half)
        send = lax.dynamic_slice_in_dim(cur, (1 - mine) * half, half)
        cur = keep + swapped(send, axis, bit)
    cur = cur.astype(gather_dtype)
    for bit in reversed(range(bits)):
        mine = (idx >> bit) & 1
        recv = swapped(cur, axis, bit)
        cur = jnp.where(mine == 0, jnp.concatenate([cur, recv]), jnp.concatenate([recv, cur]))
    return cur.astype(flat.dtype)


def radix_allreduce(flat, axis, gather_dtype, operand, start, finish):
    size = lax.axis_size(axis)
    nbits = size.bit_length() - 1
    groups = [[0]] + [list(range(b, min(b + 2, nbits))) for b in range(1, nbits, 2)]
    idx = lax.axis_index(axis)
    cur = flat
    for bits in groups:
        if bits == groups[1]:
            cur, handoff = lax.optimization_barrier((cur, first[0]))
            second = finish(handoff)
        radix, low = 1 << len(bits), bits[0]
        sub = (idx >> low) & (radix - 1)
        part = cur.shape[0] // radix
        total = lax.dynamic_slice_in_dim(cur, sub * part, part)
        for d in range(1, radix):
            send = lax.dynamic_slice_in_dim(cur, (sub ^ d) * part, part)
            total = total + lax.ppermute(send, axis, [(i, i ^ (d << low)) for i in range(size)])
        cur = total
        if bits == groups[0]:
            cur, operand = lax.optimization_barrier((cur, operand))
            first = start(operand)
        elif bits == groups[1]:
            cur, second = lax.optimization_barrier((cur, second))
    cur = cur.astype(gather_dtype)
    for bits in reversed(groups):
        radix, low = 1 << len(bits), bits[0]
        sub = (idx >> low) & (radix - 1)
        pieces = [cur] + [
            lax.ppermute(cur, axis, [(i, i ^ (d << low)) for i in range(size)])
            for d in range(1, radix)
        ]
        placed = []
        for p in range(radix):
            pick = pieces[p ^ (radix - 1)]
            for s in range(radix - 1):
                pick = jnp.where(sub == s, pieces[p ^ s], pick)
            placed.append(pick)
        cur = jnp.concatenate(placed)
    return cur.astype(flat.dtype), first[1:], second


def butterfly_allreduce(flat, axis):
    for bit in range(lax.axis_size(axis).bit_length() - 1):
        flat = flat + swapped(flat, axis, bit)
    return flat


def pack(arrays, multiple):
    flat = jnp.concatenate([a.reshape(-1) for a in arrays])
    extra = -flat.shape[0] % multiple
    return jnp.pad(flat, (0, extra))


def unpack(flat, arrays):
    out, at = [], 0
    for a in arrays:
        out.append(flat[at : at + a.size].reshape(a.shape))
        at += a.size
    return out


def on_device(
    features,
    target,
    south_rim,
    kmt,
    dw_kernel,
    dw_bias,
    ln_gain,
    ln_bias,
    w_in,
    b_in,
    w_out,
    b_out,
    layer_scale,
):
    members, lon_dev, lat_rows, chans = features.shape
    params = (dw_kernel, dw_bias, ln_gain, ln_bias, w_in, b_in, w_out, b_out, layer_scale)
    north_rows = mirror_rows(features[:, :, lat_rows - 3 :, :])
    joined = jnp.concatenate([south_rim, features, north_rows], axis=2)
    extended = with_halo(joined, (("lon", 1),), 3)
    predicted, crps_field, grad_pred, grad_normed, sums, depth_backward = local_step(
        extended, features, target, kmt, *params
    )

    def backward(grad_normed):
        grad_depth, kernel_sum, dw_bias_sum = depth_backward(grad_normed)
        grad_halo = with_halo(grad_depth, (("lon", 1),), 3)
        return grad_halo, kernel_sum, dw_bias_sum

    def backward_conv(grad_halo):
        padded = jnp.pad(grad_halo, ((0, 0), (0, 0), (6, 6), (0, 0)))
        grad_ext = jnp.zeros((members, lon_dev, lat_rows + 6, chans), jnp.float32)
        for lon_off in range(7):
            for lat_off in range(7):
                grad_ext = (
                    grad_ext
                    + dw_kernel[lon_off, lat_off]
                    * padded[
                        :,
                        6 - lon_off : 6 - lon_off + lon_dev,
                        6 - lat_off : 6 - lat_off + lat_rows + 6,
                        :,
                    ]
                )
        return grad_ext

    lon_size = lax.axis_size("lon")
    reduced, (kernel_sum, dw_bias_sum), grad_ext = radix_allreduce(
        pack(sums, lon_size * 1024), "lon", jnp.bfloat16, grad_normed, backward, backward_conv
    )
    gain_sum, bias_sum, w_in_sum, b_in_sum, w_out_sum, b_out_sum, scale_sum = unpack(reduced, sums)
    small = (kernel_sum, dw_bias_sum)
    kernel_tot, dw_bias_tot = unpack(butterfly_allreduce(pack(small, 128), "lon"), small)
    totals = (
        kernel_tot,
        dw_bias_tot,
        gain_sum,
        bias_sum,
        w_in_sum,
        b_in_sum,
        w_out_sum,
        b_out_sum,
        scale_sum,
    )
    back_rows = mirror_grads(grad_ext[:, :, lat_rows + 3 :, :])
    inner = grad_pred + grad_ext[:, :, 3 : lat_rows + 3, :]
    grad_features = jnp.concatenate(
        [inner[:, :, : lat_rows - 3, :], inner[:, :, lat_rows - 3 :, :] + back_rows], axis=2
    ).astype(jnp.bfloat16)
    factor = 1.0 / math.sqrt(members * lat_rows * lon_dev * lax.axis_size("lon"))
    return (
        predicted,
        crps_field,
        grad_features,
        totals[0] * factor,
        totals[1] * factor,
        totals[2] * factor,
        totals[3] * factor,
        totals[4] * factor,
        totals[5] * factor,
        totals[6] * factor,
        totals[7] * factor,
        totals[8] * factor,
    )


def solution(mesh):
    placed = (
        P(None, ("groups", "lon"), None, None),
        P(("groups", "lon"), None, None),
        P(None, ("groups", "lon"), None, None),
        P(("groups", "lon"), None),
        P(),
        P(),
        P(),
        P(),
        P(),
        P(),
        P(),
        P(),
        P(),
    )
    return jax.shard_map(
        on_device,
        mesh=mesh,
        in_specs=placed,
        out_specs=(
            P(None, ("groups", "lon"), None, None),
            P(("groups", "lon"), None, None),
            P(None, ("groups", "lon"), None, None),
            P("groups", None, None),
            P("groups"),
            P("groups"),
            P("groups"),
            P("groups", None),
            P("groups"),
            P("groups", None),
            P("groups"),
            P("groups"),
        ),
        check_vma=False,
    )
```

```python
import math

import jax
import jax.numpy as jnp
from jax import lax
from jax.sharding import PartitionSpec as P

LEVELS = 19


SMOOTH = 0.25
EPSILON = 1e-06


def swapped(x, axis, bit):
    return lax.ppermute(x, axis, [(i, i ^ 1 << bit) for i in range(lax.axis_size(axis))])


def with_halo(x, sides, width):
    for axis, dim in sides:
        size, length = (lax.axis_size(axis), x.shape[dim])
        up = [(i, (i + 1) % size) for i in range(size)]
        down = [(j, i) for i, j in up]
        last = lax.slice_in_dim(x, length - width, length, axis=dim)
        leading = lax.slice_in_dim(x, 0, width, axis=dim)
        before = lax.ppermute(last, axis, up)
        after = lax.ppermute(leading, axis, down)
        x = jnp.concatenate([before, x, after], axis=dim)
    return x


def smooth_abs(value):
    return jnp.sqrt(value * value + SMOOTH * SMOOTH) - SMOOTH


def smooth_slope(value):
    return value / jnp.sqrt(value * value + SMOOTH * SMOOTH)


def local_step(
    extended,
    features,
    target,
    kmt,
    dw_kernel,
    dw_bias,
    ln_gain,
    ln_bias,
    w_in,
    b_in,
    w_out,
    b_out,
    layer_scale,
):
    members, lon_dev, lat_rows, chans = features.shape
    depth = jnp.zeros(features.shape, jnp.float32) + dw_bias
    for lon_off in range(7):
        for lat_off in range(7):
            depth = depth + dw_kernel[lon_off, lat_off] * extended[
                :, lon_off : lon_off + lon_dev, lat_off : lat_off + lat_rows, :
            ].astype(jnp.float32)
    mean_val = jnp.mean(depth, axis=-1, keepdims=True)
    centred = depth - mean_val
    variance = jnp.mean(centred * centred, axis=-1, keepdims=True)
    inv_std = lax.rsqrt(variance + EPSILON)
    unit = centred * inv_std
    normed = (unit * ln_gain + ln_bias).astype(jnp.bfloat16)
    level_of = jnp.arange(chans, dtype=jnp.int32) * LEVELS // chans
    wet_mask = (level_of[None, None, :] < kmt[:, :, None]).astype(jnp.float32)
    rows = lon_dev * lat_rows
    pre_acts = []
    hiddens = []
    outputs = []
    for member in range(members):
        flat_rows = normed[member].reshape(rows, chans)
        pre_act = jnp.dot(flat_rows, w_in, preferred_element_type=jnp.float32) + b_in
        hidden = jax.nn.gelu(pre_act).astype(jnp.bfloat16)
        pre_acts.append(pre_act)
        hiddens.append(hidden)
        outputs.append(
            (jnp.dot(hidden, w_out, preferred_element_type=jnp.float32) + b_out).reshape(
                lon_dev, lat_rows, chans
            )
        )
    branch = jnp.stack(outputs)
    pred = wet_mask * (features.astype(jnp.float32) + layer_scale * branch)
    target_full = target.astype(jnp.float32)
    pair_weight = 1.0 / (members * (members - 1))
    skill = jnp.zeros(target.shape, jnp.float32)
    spread = jnp.zeros(target.shape, jnp.float32)
    for member in range(members):
        skill = skill + smooth_abs(pred[member] - target_full)
        for other in range(member + 1, members):
            spread = spread + smooth_abs(pred[member] - pred[other])
    crps_field = wet_mask * (skill / members - pair_weight * spread)
    grad_list = []
    for member in range(members):
        slope_sum = jnp.zeros(target.shape, jnp.float32)
        for other in range(members):
            if other != member:
                slope_sum = slope_sum + smooth_slope(pred[member] - pred[other])
        grad_list.append(
            wet_mask
            * (smooth_slope(pred[member] - target_full) / members - pair_weight * slope_sum)
        )
    grad_pred = jnp.stack(grad_list)
    grad_scale = jnp.sum(grad_pred * branch, axis=(0, 1, 2))
    grad_b_out = jnp.zeros((chans,), jnp.float32)
    grad_w_out = jnp.zeros(w_out.shape, jnp.float32)
    grad_b_in = jnp.zeros(b_in.shape, jnp.float32)
    grad_w_in = jnp.zeros(w_in.shape, jnp.float32)
    normed_grads = []
    contract_rows = (((0,), (0,)), ((), ()))
    contract_cols = (((1,), (1,)), ((), ()))
    for member in range(members):
        grad_out = (grad_pred[member] * layer_scale).reshape(rows, chans)
        grad_b_out = grad_b_out + jnp.sum(grad_out, axis=0)
        out_half = grad_out.astype(jnp.bfloat16)
        grad_w_out = grad_w_out + lax.dot_general(
            hiddens[member], out_half, contract_rows, preferred_element_type=jnp.float32
        )
        grad_hidden = lax.dot_general(
            out_half, w_out, contract_cols, preferred_element_type=jnp.float32
        )
        grad_pre = jax.vjp(jax.nn.gelu, pre_acts[member])[1](grad_hidden)[0]
        grad_b_in = grad_b_in + jnp.sum(grad_pre, axis=0)
        pre_half = grad_pre.astype(jnp.bfloat16)
        grad_w_in = grad_w_in + lax.dot_general(
            normed[member].reshape(rows, chans),
            pre_half,
            contract_rows,
            preferred_element_type=jnp.float32,
        )
        normed_grads.append(
            lax.dot_general(
                pre_half, w_in, contract_cols, preferred_element_type=jnp.float32
            ).reshape(lon_dev, lat_rows, chans)
        )
    grad_normed = jnp.stack(normed_grads)
    grad_ln_gain = jnp.sum(grad_normed * unit, axis=(0, 1, 2))
    grad_ln_bias = jnp.sum(grad_normed, axis=(0, 1, 2))

    def depth_backward(grad_normed):
        grad_unit = grad_normed * ln_gain
        grad_depth = inv_std * (
            grad_unit
            - jnp.mean(grad_unit, axis=-1, keepdims=True)
            - unit * jnp.mean(grad_unit * unit, axis=-1, keepdims=True)
        )
        grad_dw_bias = jnp.sum(grad_depth, axis=(0, 1, 2))
        kernel_rows = []
        for lon_off in range(7):
            kernel_cols = []
            for lat_off in range(7):
                kernel_cols.append(
                    jnp.sum(
                        grad_depth
                        * extended[
                            :, lon_off : lon_off + lon_dev, lat_off : lat_off + lat_rows, :
                        ].astype(jnp.float32),
                        axis=(0, 1, 2),
                    )
                )
            kernel_rows.append(jnp.stack(kernel_cols))
        grad_kernel = jnp.stack(kernel_rows)
        return grad_depth, grad_kernel, grad_dw_bias

    sums = (grad_ln_gain, grad_ln_bias, grad_w_in, grad_b_in, grad_w_out, grad_b_out, grad_scale)
    return (pred.astype(jnp.bfloat16), crps_field, grad_pred, grad_normed, sums, depth_backward)


def mirrored(x, axis):
    size = lax.axis_size(axis)
    return lax.ppermute(x, axis, [(i, size - 1 - i) for i in range(size)])


def mirror_rows(top_rows):
    return mirrored(top_rows, "lon")[:, ::-1, ::-1, :]


def mirror_grads(fold_rows):
    picked = mirrored(fold_rows.astype(jnp.bfloat16), "lon").astype(fold_rows.dtype)
    return picked[:, ::-1, ::-1, :]


def halving_allreduce(flat, axis, gather_dtype):
    size = lax.axis_size(axis)
    bits = size.bit_length() - 1
    idx = lax.axis_index(axis)
    cur = flat
    for bit in range(bits):
        half = cur.shape[0] // 2
        mine = (idx >> bit) & 1
        keep = lax.dynamic_slice_in_dim(cur, mine * half, half)
        send = lax.dynamic_slice_in_dim(cur, (1 - mine) * half, half)
        cur = keep + swapped(send, axis, bit)
    cur = cur.astype(gather_dtype)
    for bit in reversed(range(bits)):
        mine = (idx >> bit) & 1
        recv = swapped(cur, axis, bit)
        cur = jnp.where(mine == 0, jnp.concatenate([cur, recv]), jnp.concatenate([recv, cur]))
    return cur.astype(flat.dtype)


def radix_allreduce(flat, axis, gather_dtype, operand, start, finish):
    size = lax.axis_size(axis)
    nbits = size.bit_length() - 1
    groups = [[0]] + [list(range(b, min(b + 2, nbits))) for b in range(1, nbits, 2)]
    idx = lax.axis_index(axis)
    cur = flat
    for bits in groups:
        if bits == groups[1]:
            cur, handoff = lax.optimization_barrier((cur, first[0]))
            second = finish(handoff)
        radix, low = 1 << len(bits), bits[0]
        sub = (idx >> low) & (radix - 1)
        part = cur.shape[0] // radix
        total = lax.dynamic_slice_in_dim(cur, sub * part, part)
        for d in range(1, radix):
            send = lax.dynamic_slice_in_dim(cur, (sub ^ d) * part, part)
            total = total + lax.ppermute(send, axis, [(i, i ^ (d << low)) for i in range(size)])
        cur = total
        if bits == groups[0]:
            cur, operand = lax.optimization_barrier((cur, operand))
            first = start(operand)
        elif bits == groups[1]:
            cur, second = lax.optimization_barrier((cur, second))
    cur = cur.astype(gather_dtype)
    merged = 1
    while merged < len(groups) and (1 << sum(len(g) for g in groups[-merged - 1 :])) <= 8:
        merged += 1
    gathers = [groups[:-merged][k : k + 1] for k in range(len(groups) - merged)]
    gathers.append(groups[-merged:])
    for rounds in reversed(gathers):
        radices = [1 << len(bits) for bits in rounds]
        mask = sum(1 << b for bits in rounds for b in bits)
        values = [w for w in range(size) if w & ~mask == 0]

        def position(w):
            pos = 0
            for bits, radix in zip(rounds, radices):
                pos = pos * radix + ((w >> bits[0]) & (radix - 1))
            return pos

        pieces = {0: cur}
        for m in values[1:]:
            pieces[m] = lax.ppermute(cur, axis, [(i, i ^ m) for i in range(size)])
        own = idx & mask
        placed = [None] * len(values)
        for w in values:
            pick = pieces[values[-1] ^ w]
            for v in values[:-1]:
                pick = jnp.where(own == v, pieces[v ^ w], pick)
            placed[position(w)] = pick
        cur = jnp.concatenate(placed)
    return cur.astype(flat.dtype), first[1:], second


def butterfly_allreduce(flat, axis):
    for bit in range(lax.axis_size(axis).bit_length() - 1):
        flat = flat + swapped(flat, axis, bit)
    return flat


def pack(arrays, multiple):
    flat = jnp.concatenate([a.reshape(-1) for a in arrays])
    extra = -flat.shape[0] % multiple
    return jnp.pad(flat, (0, extra))


def unpack(flat, arrays):
    out, at = [], 0
    for a in arrays:
        out.append(flat[at : at + a.size].reshape(a.shape))
        at += a.size
    return out


def on_device(
    features,
    target,
    south_rim,
    kmt,
    dw_kernel,
    dw_bias,
    ln_gain,
    ln_bias,
    w_in,
    b_in,
    w_out,
    b_out,
    layer_scale,
):
    members, lon_dev, lat_rows, chans = features.shape
    params = (dw_kernel, dw_bias, ln_gain, ln_bias, w_in, b_in, w_out, b_out, layer_scale)
    north_rows = mirror_rows(features[:, :, lat_rows - 3 :, :])
    joined = jnp.concatenate([south_rim, features, north_rows], axis=2)
    extended = with_halo(joined, (("lon", 1),), 3)
    predicted, crps_field, grad_pred, grad_normed, sums, depth_backward = local_step(
        extended, features, target, kmt, *params
    )

    def backward(grad_normed):
        grad_depth, kernel_sum, dw_bias_sum = depth_backward(grad_normed)
        grad_halo = with_halo(grad_depth, (("lon", 1),), 3)
        return grad_halo, kernel_sum, dw_bias_sum

    def backward_conv(grad_halo):
        padded = jnp.pad(grad_halo, ((0, 0), (0, 0), (6, 6), (0, 0)))
        grad_ext = jnp.zeros((members, lon_dev, lat_rows + 6, chans), jnp.float32)
        for lon_off in range(7):
            for lat_off in range(7):
                grad_ext = (
                    grad_ext
                    + dw_kernel[lon_off, lat_off]
                    * padded[
                        :,
                        6 - lon_off : 6 - lon_off + lon_dev,
                        6 - lat_off : 6 - lat_off + lat_rows + 6,
                        :,
                    ]
                )
        return grad_ext

    lon_size = lax.axis_size("lon")
    reduced, (kernel_sum, dw_bias_sum), grad_ext = radix_allreduce(
        pack(sums, lon_size * 1024), "lon", jnp.bfloat16, grad_normed, backward, backward_conv
    )
    gain_sum, bias_sum, w_in_sum, b_in_sum, w_out_sum, b_out_sum, scale_sum = unpack(reduced, sums)
    small = (kernel_sum, dw_bias_sum)
    kernel_tot, dw_bias_tot = unpack(butterfly_allreduce(pack(small, 128), "lon"), small)
    totals = (
        kernel_tot,
        dw_bias_tot,
        gain_sum,
        bias_sum,
        w_in_sum,
        b_in_sum,
        w_out_sum,
        b_out_sum,
        scale_sum,
    )
    back_rows = mirror_grads(grad_ext[:, :, lat_rows + 3 :, :])
    inner = grad_pred + grad_ext[:, :, 3 : lat_rows + 3, :]
    grad_features = jnp.concatenate(
        [inner[:, :, : lat_rows - 3, :], inner[:, :, lat_rows - 3 :, :] + back_rows], axis=2
    ).astype(jnp.bfloat16)
    factor = 1.0 / math.sqrt(members * lat_rows * lon_dev * lax.axis_size("lon"))
    return (
        predicted,
        crps_field,
        grad_features,
        totals[0] * factor,
        totals[1] * factor,
        totals[2] * factor,
        totals[3] * factor,
        totals[4] * factor,
        totals[5] * factor,
        totals[6] * factor,
        totals[7] * factor,
        totals[8] * factor,
    )


def solution(mesh):
    placed = (
        P(None, ("groups", "lon"), None, None),
        P(("groups", "lon"), None, None),
        P(None, ("groups", "lon"), None, None),
        P(("groups", "lon"), None),
        P(),
        P(),
        P(),
        P(),
        P(),
        P(),
        P(),
        P(),
        P(),
    )
    return jax.shard_map(
        on_device,
        mesh=mesh,
        in_specs=placed,
        out_specs=(
            P(None, ("groups", "lon"), None, None),
            P(("groups", "lon"), None, None),
            P(None, ("groups", "lon"), None, None),
            P("groups", None, None),
            P("groups"),
            P("groups"),
            P("groups"),
            P("groups", None),
            P("groups"),
            P("groups", None),
            P("groups"),
            P("groups"),
        ),
        check_vma=False,
    )
```

```python
import math

import jax
import jax.numpy as jnp
from jax import lax
from jax.sharding import PartitionSpec as P

LEVELS = 19


SMOOTH = 0.25
EPSILON = 1e-06


def swapped(x, axis, bit):
    return lax.ppermute(x, axis, [(i, i ^ 1 << bit) for i in range(lax.axis_size(axis))])


def with_halo(x, sides, width):
    for axis, dim in sides:
        size, length = (lax.axis_size(axis), x.shape[dim])
        up = [(i, (i + 1) % size) for i in range(size)]
        down = [(j, i) for i, j in up]
        last = lax.slice_in_dim(x, length - width, length, axis=dim)
        leading = lax.slice_in_dim(x, 0, width, axis=dim)
        before = lax.ppermute(last, axis, up)
        after = lax.ppermute(leading, axis, down)
        x = jnp.concatenate([before, x, after], axis=dim)
    return x


def smooth_abs(value):
    return jnp.sqrt(value * value + SMOOTH * SMOOTH) - SMOOTH


def smooth_slope(value):
    return value / jnp.sqrt(value * value + SMOOTH * SMOOTH)


def local_step(
    extended,
    features,
    target,
    kmt,
    dw_kernel,
    dw_bias,
    ln_gain,
    ln_bias,
    w_in,
    b_in,
    w_out,
    b_out,
    layer_scale,
):
    members, lon_dev, lat_rows, chans = features.shape
    depth = jnp.zeros(features.shape, jnp.float32) + dw_bias
    for lon_off in range(7):
        for lat_off in range(7):
            depth = depth + dw_kernel[lon_off, lat_off] * extended[
                :, lon_off : lon_off + lon_dev, lat_off : lat_off + lat_rows, :
            ].astype(jnp.float32)
    mean_val = jnp.mean(depth, axis=-1, keepdims=True)
    centred = depth - mean_val
    variance = jnp.mean(centred * centred, axis=-1, keepdims=True)
    inv_std = lax.rsqrt(variance + EPSILON)
    unit = centred * inv_std
    normed = (unit * ln_gain + ln_bias).astype(jnp.bfloat16)
    level_of = jnp.arange(chans, dtype=jnp.int32) * LEVELS // chans
    wet_mask = (level_of[None, None, :] < kmt[:, :, None]).astype(jnp.float32)
    rows = lon_dev * lat_rows
    pre_acts = []
    hiddens = []
    outputs = []
    for member in range(members):
        flat_rows = normed[member].reshape(rows, chans)
        pre_act = jnp.dot(flat_rows, w_in, preferred_element_type=jnp.float32) + b_in
        hidden = jax.nn.gelu(pre_act).astype(jnp.bfloat16)
        pre_acts.append(pre_act)
        hiddens.append(hidden)
        outputs.append(
            (jnp.dot(hidden, w_out, preferred_element_type=jnp.float32) + b_out).reshape(
                lon_dev, lat_rows, chans
            )
        )
    branch = jnp.stack(outputs)
    pred = wet_mask * (features.astype(jnp.float32) + layer_scale * branch)
    target_full = target.astype(jnp.float32)
    pair_weight = 1.0 / (members * (members - 1))
    skill = jnp.zeros(target.shape, jnp.float32)
    spread = jnp.zeros(target.shape, jnp.float32)
    for member in range(members):
        skill = skill + smooth_abs(pred[member] - target_full)
        for other in range(member + 1, members):
            spread = spread + smooth_abs(pred[member] - pred[other])
    crps_field = wet_mask * (skill / members - pair_weight * spread)
    grad_list = []
    for member in range(members):
        slope_sum = jnp.zeros(target.shape, jnp.float32)
        for other in range(members):
            if other != member:
                slope_sum = slope_sum + smooth_slope(pred[member] - pred[other])
        grad_list.append(
            wet_mask
            * (smooth_slope(pred[member] - target_full) / members - pair_weight * slope_sum)
        )
    grad_pred = jnp.stack(grad_list)
    grad_scale = jnp.sum(grad_pred * branch, axis=(0, 1, 2))
    grad_b_out = jnp.zeros((chans,), jnp.float32)
    grad_w_out = jnp.zeros(w_out.shape, jnp.float32)
    grad_b_in = jnp.zeros(b_in.shape, jnp.float32)
    grad_w_in = jnp.zeros(w_in.shape, jnp.float32)
    normed_grads = []
    contract_rows = (((0,), (0,)), ((), ()))
    contract_cols = (((1,), (1,)), ((), ()))
    for member in range(members):
        grad_out = (grad_pred[member] * layer_scale).reshape(rows, chans)
        grad_b_out = grad_b_out + jnp.sum(grad_out, axis=0)
        out_half = grad_out.astype(jnp.bfloat16)
        grad_w_out = grad_w_out + lax.dot_general(
            hiddens[member], out_half, contract_rows, preferred_element_type=jnp.float32
        )
        grad_hidden = lax.dot_general(
            out_half, w_out, contract_cols, preferred_element_type=jnp.float32
        )
        grad_pre = jax.vjp(jax.nn.gelu, pre_acts[member])[1](grad_hidden)[0]
        grad_b_in = grad_b_in + jnp.sum(grad_pre, axis=0)
        pre_half = grad_pre.astype(jnp.bfloat16)
        grad_w_in = grad_w_in + lax.dot_general(
            normed[member].reshape(rows, chans),
            pre_half,
            contract_rows,
            preferred_element_type=jnp.float32,
        )
        normed_grads.append(
            lax.dot_general(
                pre_half, w_in, contract_cols, preferred_element_type=jnp.float32
            ).reshape(lon_dev, lat_rows, chans)
        )
    grad_normed = jnp.stack(normed_grads)
    grad_ln_gain = jnp.sum(grad_normed * unit, axis=(0, 1, 2))
    grad_ln_bias = jnp.sum(grad_normed, axis=(0, 1, 2))

    def depth_backward(grad_normed):
        grad_unit = grad_normed * ln_gain
        grad_depth = inv_std * (
            grad_unit
            - jnp.mean(grad_unit, axis=-1, keepdims=True)
            - unit * jnp.mean(grad_unit * unit, axis=-1, keepdims=True)
        )
        grad_dw_bias = jnp.sum(grad_depth, axis=(0, 1, 2))
        kernel_rows = []
        for lon_off in range(7):
            kernel_cols = []
            for lat_off in range(7):
                kernel_cols.append(
                    jnp.sum(
                        grad_depth
                        * extended[
                            :, lon_off : lon_off + lon_dev, lat_off : lat_off + lat_rows, :
                        ].astype(jnp.float32),
                        axis=(0, 1, 2),
                    )
                )
            kernel_rows.append(jnp.stack(kernel_cols))
        grad_kernel = jnp.stack(kernel_rows)
        return grad_depth, grad_kernel, grad_dw_bias

    sums = (grad_ln_gain, grad_ln_bias, grad_w_in, grad_b_in, grad_w_out, grad_b_out, grad_scale)
    return (pred.astype(jnp.bfloat16), crps_field, grad_pred, grad_normed, sums, depth_backward)


def mirrored(x, axis):
    size = lax.axis_size(axis)
    return lax.ppermute(x, axis, [(i, size - 1 - i) for i in range(size)])


def mirror_rows(top_rows):
    return mirrored(top_rows, "lon")[:, ::-1, ::-1, :]


def mirror_grads(fold_rows):
    picked = mirrored(fold_rows.astype(jnp.bfloat16), "lon").astype(fold_rows.dtype)
    return picked[:, ::-1, ::-1, :]


def halving_allreduce(flat, axis, gather_dtype):
    size = lax.axis_size(axis)
    bits = size.bit_length() - 1
    idx = lax.axis_index(axis)
    cur = flat
    for bit in range(bits):
        half = cur.shape[0] // 2
        mine = (idx >> bit) & 1
        keep = lax.dynamic_slice_in_dim(cur, mine * half, half)
        send = lax.dynamic_slice_in_dim(cur, (1 - mine) * half, half)
        cur = keep + swapped(send, axis, bit)
    cur = cur.astype(gather_dtype)
    for bit in reversed(range(bits)):
        mine = (idx >> bit) & 1
        recv = swapped(cur, axis, bit)
        cur = jnp.where(mine == 0, jnp.concatenate([cur, recv]), jnp.concatenate([recv, cur]))
    return cur.astype(flat.dtype)


def radix_allreduce(flat, axis, gather_dtype, scale, operand, start, finish):
    size = lax.axis_size(axis)
    nbits = size.bit_length() - 1
    groups = [[0]] + [list(range(b, min(b + 2, nbits))) for b in range(1, nbits, 2)]
    idx = lax.axis_index(axis)
    cur = flat
    for bits in groups:
        if bits == groups[1]:
            cur, handoff = lax.optimization_barrier((cur, first[0]))
            second = finish(handoff)
        radix, low = 1 << len(bits), bits[0]
        sub = (idx >> low) & (radix - 1)
        part = cur.shape[0] // radix
        total = lax.dynamic_slice_in_dim(cur, sub * part, part)
        for d in range(1, radix):
            send = lax.dynamic_slice_in_dim(cur, (sub ^ d) * part, part)
            total = total + lax.ppermute(send, axis, [(i, i ^ (d << low)) for i in range(size)])
        cur = total
        if bits == groups[0]:
            cur, operand = lax.optimization_barrier((cur, operand))
            first = start(operand)
        elif bits == groups[1]:
            cur, second = lax.optimization_barrier((cur, second))
    cur = (cur * scale).astype(gather_dtype)
    for bits in reversed(groups):
        radix, low = 1 << len(bits), bits[0]
        sub = (idx >> low) & (radix - 1)
        pieces = [cur] + [
            lax.ppermute(cur, axis, [(i, i ^ (d << low)) for i in range(size)])
            for d in range(1, radix)
        ]
        placed = []
        for p in range(radix):
            pick = pieces[p ^ (radix - 1)]
            for s in range(radix - 1):
                pick = jnp.where(sub == s, pieces[p ^ s], pick)
            placed.append(pick)
        cur = jnp.concatenate(placed)
    return cur.astype(flat.dtype), first[1:], second


def butterfly_allreduce(flat, axis):
    for bit in range(lax.axis_size(axis).bit_length() - 1):
        flat = flat + swapped(flat, axis, bit)
    return flat


def pack(arrays, multiple):
    flat = jnp.concatenate([a.reshape(-1) for a in arrays])
    extra = -flat.shape[0] % multiple
    return jnp.pad(flat, (0, extra))


def unpack(flat, arrays):
    out, at = [], 0
    for a in arrays:
        out.append(flat[at : at + a.size].reshape(a.shape))
        at += a.size
    return out


def on_device(
    features,
    target,
    south_rim,
    kmt,
    dw_kernel,
    dw_bias,
    ln_gain,
    ln_bias,
    w_in,
    b_in,
    w_out,
    b_out,
    layer_scale,
):
    members, lon_dev, lat_rows, chans = features.shape
    params = (dw_kernel, dw_bias, ln_gain, ln_bias, w_in, b_in, w_out, b_out, layer_scale)
    north_rows = mirror_rows(features[:, :, lat_rows - 3 :, :])
    joined = jnp.concatenate([south_rim, features, north_rows], axis=2)
    extended = with_halo(joined, (("lon", 1),), 3)
    predicted, crps_field, grad_pred, grad_normed, sums, depth_backward = local_step(
        extended, features, target, kmt, *params
    )

    def backward(grad_normed):
        grad_depth, kernel_sum, dw_bias_sum = depth_backward(grad_normed)
        grad_halo = with_halo(grad_depth, (("lon", 1),), 3)
        return grad_halo, kernel_sum, dw_bias_sum

    def backward_conv(grad_halo):
        padded = jnp.pad(grad_halo, ((0, 0), (0, 0), (6, 6), (0, 0)))
        grad_ext = jnp.zeros((members, lon_dev, lat_rows + 6, chans), jnp.float32)
        for lon_off in range(7):
            for lat_off in range(7):
                grad_ext = (
                    grad_ext
                    + dw_kernel[lon_off, lat_off]
                    * padded[
                        :,
                        6 - lon_off : 6 - lon_off + lon_dev,
                        6 - lat_off : 6 - lat_off + lat_rows + 6,
                        :,
                    ]
                )
        return grad_ext

    lon_size = lax.axis_size("lon")
    factor = 1.0 / math.sqrt(members * lat_rows * lon_dev * lon_size)
    reduced, (kernel_sum, dw_bias_sum), grad_ext = radix_allreduce(
        pack(sums, lon_size * 1024), "lon", jnp.bfloat16, factor, grad_normed, backward, backward_conv
    )
    gain_sum, bias_sum, w_in_sum, b_in_sum, w_out_sum, b_out_sum, scale_sum = unpack(reduced, sums)
    small = (kernel_sum, dw_bias_sum)
    kernel_tot, dw_bias_tot = unpack(butterfly_allreduce(pack(small, 128), "lon"), small)
    totals = (
        kernel_tot,
        dw_bias_tot,
        gain_sum,
        bias_sum,
        w_in_sum,
        b_in_sum,
        w_out_sum,
        b_out_sum,
        scale_sum,
    )
    back_rows = mirror_grads(grad_ext[:, :, lat_rows + 3 :, :])
    inner = grad_pred + grad_ext[:, :, 3 : lat_rows + 3, :]
    grad_features = jnp.concatenate(
        [inner[:, :, : lat_rows - 3, :], inner[:, :, lat_rows - 3 :, :] + back_rows], axis=2
    ).astype(jnp.bfloat16)
    return (
        predicted,
        crps_field,
        grad_features,
        totals[0] * factor,
        totals[1] * factor,
        *totals[2:],
    )


def solution(mesh):
    placed = (
        P(None, ("groups", "lon"), None, None),
        P(("groups", "lon"), None, None),
        P(None, ("groups", "lon"), None, None),
        P(("groups", "lon"), None),
        P(),
        P(),
        P(),
        P(),
        P(),
        P(),
        P(),
        P(),
        P(),
    )
    return jax.shard_map(
        on_device,
        mesh=mesh,
        in_specs=placed,
        out_specs=(
            P(None, ("groups", "lon"), None, None),
            P(("groups", "lon"), None, None),
            P(None, ("groups", "lon"), None, None),
            P("groups", None, None),
            P("groups"),
            P("groups"),
            P("groups"),
            P("groups", None),
            P("groups"),
            P("groups", None),
            P("groups"),
            P("groups"),
        ),
        check_vma=False,
    )
```

```python
import math

import jax
import jax.numpy as jnp
from jax import lax
from jax.sharding import PartitionSpec as P

LEVELS = 19


SMOOTH = 0.25
EPSILON = 1e-06


def swapped(x, axis, bit):
    return lax.ppermute(x, axis, [(i, i ^ 1 << bit) for i in range(lax.axis_size(axis))])


def with_halo(x, sides, width):
    for axis, dim in sides:
        size, length = (lax.axis_size(axis), x.shape[dim])
        up = [(i, (i + 1) % size) for i in range(size)]
        down = [(j, i) for i, j in up]
        last = lax.slice_in_dim(x, length - width, length, axis=dim)
        leading = lax.slice_in_dim(x, 0, width, axis=dim)
        before = lax.ppermute(last, axis, up)
        after = lax.ppermute(leading, axis, down)
        x = jnp.concatenate([before, x, after], axis=dim)
    return x


def smooth_abs(value):
    return jnp.sqrt(value * value + SMOOTH * SMOOTH) - SMOOTH


def smooth_slope(value):
    return value / jnp.sqrt(value * value + SMOOTH * SMOOTH)


def local_step(
    extended,
    features,
    target,
    kmt,
    dw_kernel,
    dw_bias,
    ln_gain,
    ln_bias,
    w_in,
    b_in,
    w_out,
    b_out,
    layer_scale,
):
    members, lon_dev, lat_rows, chans = features.shape
    depth = jnp.zeros(features.shape, jnp.float32) + dw_bias
    for lon_off in range(7):
        for lat_off in range(7):
            depth = depth + dw_kernel[lon_off, lat_off] * extended[
                :, lon_off : lon_off + lon_dev, lat_off : lat_off + lat_rows, :
            ].astype(jnp.float32)
    mean_val = jnp.mean(depth, axis=-1, keepdims=True)
    centred = depth - mean_val
    variance = jnp.mean(centred * centred, axis=-1, keepdims=True)
    inv_std = lax.rsqrt(variance + EPSILON)
    unit = centred * inv_std
    normed = (unit * ln_gain + ln_bias).astype(jnp.bfloat16)
    level_of = jnp.arange(chans, dtype=jnp.int32) * LEVELS // chans
    wet_mask = (level_of[None, None, :] < kmt[:, :, None]).astype(jnp.float32)
    rows = lon_dev * lat_rows
    pre_acts = []
    hiddens = []
    outputs = []
    for member in range(members):
        flat_rows = normed[member].reshape(rows, chans)
        pre_act = jnp.dot(flat_rows, w_in, preferred_element_type=jnp.float32) + b_in
        hidden = jax.nn.gelu(pre_act).astype(jnp.bfloat16)
        pre_acts.append(pre_act)
        hiddens.append(hidden)
        outputs.append(
            (jnp.dot(hidden, w_out, preferred_element_type=jnp.float32) + b_out).reshape(
                lon_dev, lat_rows, chans
            )
        )
    branch = jnp.stack(outputs)
    pred = wet_mask * (features.astype(jnp.float32) + layer_scale * branch)
    target_full = target.astype(jnp.float32)
    pair_weight = 1.0 / (members * (members - 1))
    skill = jnp.zeros(target.shape, jnp.float32)
    spread = jnp.zeros(target.shape, jnp.float32)
    for member in range(members):
        skill = skill + smooth_abs(pred[member] - target_full)
        for other in range(member + 1, members):
            spread = spread + smooth_abs(pred[member] - pred[other])
    crps_field = wet_mask * (skill / members - pair_weight * spread)
    grad_list = []
    for member in range(members):
        slope_sum = jnp.zeros(target.shape, jnp.float32)
        for other in range(members):
            if other != member:
                slope_sum = slope_sum + smooth_slope(pred[member] - pred[other])
        grad_list.append(
            wet_mask
            * (smooth_slope(pred[member] - target_full) / members - pair_weight * slope_sum)
        )
    grad_pred = jnp.stack(grad_list)
    grad_scale = jnp.sum(grad_pred * branch, axis=(0, 1, 2))
    grad_b_out = jnp.zeros((chans,), jnp.float32)
    grad_w_out = jnp.zeros(w_out.shape, jnp.float32)
    grad_b_in = jnp.zeros(b_in.shape, jnp.float32)
    grad_w_in = jnp.zeros(w_in.shape, jnp.float32)
    normed_grads = []
    contract_rows = (((0,), (0,)), ((), ()))
    contract_cols = (((1,), (1,)), ((), ()))
    for member in range(members):
        grad_out = (grad_pred[member] * layer_scale).reshape(rows, chans)
        grad_b_out = grad_b_out + jnp.sum(grad_out, axis=0)
        out_half = grad_out.astype(jnp.bfloat16)
        grad_w_out = grad_w_out + lax.dot_general(
            hiddens[member], out_half, contract_rows, preferred_element_type=jnp.float32
        )
        grad_hidden = lax.dot_general(
            out_half, w_out, contract_cols, preferred_element_type=jnp.float32
        )
        grad_pre = jax.vjp(jax.nn.gelu, pre_acts[member])[1](grad_hidden)[0]
        grad_b_in = grad_b_in + jnp.sum(grad_pre, axis=0)
        pre_half = grad_pre.astype(jnp.bfloat16)
        grad_w_in = grad_w_in + lax.dot_general(
            normed[member].reshape(rows, chans),
            pre_half,
            contract_rows,
            preferred_element_type=jnp.float32,
        )
        normed_grads.append(
            lax.dot_general(
                pre_half, w_in, contract_cols, preferred_element_type=jnp.float32
            ).reshape(lon_dev, lat_rows, chans)
        )
    grad_normed = jnp.stack(normed_grads)
    grad_ln_gain = jnp.sum(grad_normed * unit, axis=(0, 1, 2))
    grad_ln_bias = jnp.sum(grad_normed, axis=(0, 1, 2))

    def depth_backward(grad_normed):
        grad_unit = grad_normed * ln_gain
        grad_depth = inv_std * (
            grad_unit
            - jnp.mean(grad_unit, axis=-1, keepdims=True)
            - unit * jnp.mean(grad_unit * unit, axis=-1, keepdims=True)
        )
        grad_dw_bias = jnp.sum(grad_depth, axis=(0, 1, 2))
        kernel_rows = []
        for lon_off in range(7):
            kernel_cols = []
            for lat_off in range(7):
                kernel_cols.append(
                    jnp.sum(
                        grad_depth
                        * extended[
                            :, lon_off : lon_off + lon_dev, lat_off : lat_off + lat_rows, :
                        ].astype(jnp.float32),
                        axis=(0, 1, 2),
                    )
                )
            kernel_rows.append(jnp.stack(kernel_cols))
        grad_kernel = jnp.stack(kernel_rows)
        return grad_depth, grad_kernel, grad_dw_bias

    sums = (grad_ln_gain, grad_ln_bias, grad_w_in, grad_b_in, grad_w_out, grad_b_out, grad_scale)
    return (pred.astype(jnp.bfloat16), crps_field, grad_pred, grad_normed, sums, depth_backward)


def mirrored(x, axis):
    size = lax.axis_size(axis)
    return lax.ppermute(x, axis, [(i, size - 1 - i) for i in range(size)])


def mirror_rows(top_rows):
    return mirrored(top_rows, "lon")[:, ::-1, ::-1, :]


def mirror_grads(fold_rows):
    picked = mirrored(fold_rows.astype(jnp.bfloat16), "lon").astype(fold_rows.dtype)
    return picked[:, ::-1, ::-1, :]


def halving_allreduce(flat, axis, gather_dtype):
    size = lax.axis_size(axis)
    bits = size.bit_length() - 1
    idx = lax.axis_index(axis)
    cur = flat
    for bit in range(bits):
        half = cur.shape[0] // 2
        mine = (idx >> bit) & 1
        keep = lax.dynamic_slice_in_dim(cur, mine * half, half)
        send = lax.dynamic_slice_in_dim(cur, (1 - mine) * half, half)
        cur = keep + swapped(send, axis, bit)
    cur = cur.astype(gather_dtype)
    for bit in reversed(range(bits)):
        mine = (idx >> bit) & 1
        recv = swapped(cur, axis, bit)
        cur = jnp.where(mine == 0, jnp.concatenate([cur, recv]), jnp.concatenate([recv, cur]))
    return cur.astype(flat.dtype)


def radix_allreduce(flat, axis, gather_dtype, operand, start, finish, fill):
    size = lax.axis_size(axis)
    nbits = size.bit_length() - 1
    groups = [[0]] + [list(range(b, min(b + 2, nbits))) for b in range(1, nbits, 2)]
    idx = lax.axis_index(axis)
    cur = flat
    for bits in groups:
        if bits == groups[1]:
            cur, handoff = lax.optimization_barrier((cur, first[0]))
            second = finish(handoff)
        radix, low = 1 << len(bits), bits[0]
        sub = (idx >> low) & (radix - 1)
        part = cur.shape[0] // radix
        total = lax.dynamic_slice_in_dim(cur, sub * part, part)
        for d in range(1, radix):
            send = lax.dynamic_slice_in_dim(cur, (sub ^ d) * part, part)
            total = total + lax.ppermute(send, axis, [(i, i ^ (d << low)) for i in range(size)])
        cur = total
        if bits == groups[0]:
            cur, operand = lax.optimization_barrier((cur, operand))
            first = start(operand)
        elif bits == groups[1]:
            cur, second = lax.optimization_barrier((cur, second))
            third = fill(second)
        elif bits == groups[2]:
            cur, third = lax.optimization_barrier((cur, third))
    cur = cur.astype(gather_dtype)
    for bits in reversed(groups):
        radix, low = 1 << len(bits), bits[0]
        sub = (idx >> low) & (radix - 1)
        pieces = [cur] + [
            lax.ppermute(cur, axis, [(i, i ^ (d << low)) for i in range(size)])
            for d in range(1, radix)
        ]
        placed = []
        for p in range(radix):
            pick = pieces[p ^ (radix - 1)]
            for s in range(radix - 1):
                pick = jnp.where(sub == s, pieces[p ^ s], pick)
            placed.append(pick)
        cur = jnp.concatenate(placed)
    return cur.astype(flat.dtype), first[1:], second, third


def butterfly_allreduce(flat, axis):
    for bit in range(lax.axis_size(axis).bit_length() - 1):
        flat = flat + swapped(flat, axis, bit)
    return flat


def pack(arrays, multiple):
    flat = jnp.concatenate([a.reshape(-1) for a in arrays])
    extra = -flat.shape[0] % multiple
    return jnp.pad(flat, (0, extra))


def unpack(flat, arrays):
    out, at = [], 0
    for a in arrays:
        out.append(flat[at : at + a.size].reshape(a.shape))
        at += a.size
    return out


def on_device(
    features,
    target,
    south_rim,
    kmt,
    dw_kernel,
    dw_bias,
    ln_gain,
    ln_bias,
    w_in,
    b_in,
    w_out,
    b_out,
    layer_scale,
):
    members, lon_dev, lat_rows, chans = features.shape
    params = (dw_kernel, dw_bias, ln_gain, ln_bias, w_in, b_in, w_out, b_out, layer_scale)
    north_rows = mirror_rows(features[:, :, lat_rows - 3 :, :])
    joined = jnp.concatenate([south_rim, features, north_rows], axis=2)
    extended = with_halo(joined, (("lon", 1),), 3)
    predicted, crps_field, grad_pred, grad_normed, sums, depth_backward = local_step(
        extended, features, target, kmt, *params
    )

    def backward(grad_normed):
        grad_depth, kernel_sum, dw_bias_sum = depth_backward(grad_normed)
        grad_halo = with_halo(grad_depth, (("lon", 1),), 3)
        return grad_halo, kernel_sum, dw_bias_sum

    def backward_conv(grad_halo):
        padded = jnp.pad(grad_halo, ((0, 0), (0, 0), (6, 6), (0, 0)))
        grad_ext = jnp.zeros((members, lon_dev, lat_rows + 6, chans), jnp.float32)
        for lon_off in range(7):
            for lat_off in range(7):
                grad_ext = (
                    grad_ext
                    + dw_kernel[lon_off, lat_off]
                    * padded[
                        :,
                        6 - lon_off : 6 - lon_off + lon_dev,
                        6 - lat_off : 6 - lat_off + lat_rows + 6,
                        :,
                    ]
                )
        return grad_ext

    lon_size = lax.axis_size("lon")
    def grad_features_main(grad_ext):
        return (grad_pred[:, :, : lat_rows - 3] + grad_ext[:, :, 3:lat_rows]).astype(jnp.bfloat16)

    reduced, (kernel_sum, dw_bias_sum), grad_ext, main_rows = radix_allreduce(
        pack(sums, lon_size * 1024),
        "lon",
        jnp.bfloat16,
        grad_normed,
        backward,
        backward_conv,
        grad_features_main,
    )
    gain_sum, bias_sum, w_in_sum, b_in_sum, w_out_sum, b_out_sum, scale_sum = unpack(reduced, sums)
    small = (kernel_sum, dw_bias_sum)
    kernel_tot, dw_bias_tot = unpack(butterfly_allreduce(pack(small, 128), "lon"), small)
    totals = (
        kernel_tot,
        dw_bias_tot,
        gain_sum,
        bias_sum,
        w_in_sum,
        b_in_sum,
        w_out_sum,
        b_out_sum,
        scale_sum,
    )
    back_rows = mirror_grads(grad_ext[:, :, lat_rows + 3 :, :])
    fold_rows = (
        grad_pred[:, :, lat_rows - 3 :] + grad_ext[:, :, lat_rows : lat_rows + 3]
    ) + back_rows
    grad_features = jnp.concatenate([main_rows, fold_rows.astype(jnp.bfloat16)], axis=2)
    factor = 1.0 / math.sqrt(members * lat_rows * lon_dev * lax.axis_size("lon"))
    return (
        predicted,
        crps_field,
        grad_features,
        totals[0] * factor,
        totals[1] * factor,
        totals[2] * factor,
        totals[3] * factor,
        totals[4] * factor,
        totals[5] * factor,
        totals[6] * factor,
        totals[7] * factor,
        totals[8] * factor,
    )


def solution(mesh):
    placed = (
        P(None, ("groups", "lon"), None, None),
        P(("groups", "lon"), None, None),
        P(None, ("groups", "lon"), None, None),
        P(("groups", "lon"), None),
        P(),
        P(),
        P(),
        P(),
        P(),
        P(),
        P(),
        P(),
        P(),
    )
    return jax.shard_map(
        on_device,
        mesh=mesh,
        in_specs=placed,
        out_specs=(
            P(None, ("groups", "lon"), None, None),
            P(("groups", "lon"), None, None),
            P(None, ("groups", "lon"), None, None),
            P("groups", None, None),
            P("groups"),
            P("groups"),
            P("groups"),
            P("groups", None),
            P("groups"),
            P("groups", None),
            P("groups"),
            P("groups"),
        ),
        check_vma=False,
    )
```

```python
import math

import jax
import jax.numpy as jnp
from jax import lax
from jax.sharding import PartitionSpec as P

LEVELS = 19


SMOOTH = 0.25
EPSILON = 1e-06


def swapped(x, axis, bit):
    return lax.ppermute(x, axis, [(i, i ^ 1 << bit) for i in range(lax.axis_size(axis))])


def with_halo(x, sides, width):
    for axis, dim in sides:
        size, length = (lax.axis_size(axis), x.shape[dim])
        up = [(i, (i + 1) % size) for i in range(size)]
        down = [(j, i) for i, j in up]
        last = lax.slice_in_dim(x, length - width, length, axis=dim)
        leading = lax.slice_in_dim(x, 0, width, axis=dim)
        before = lax.ppermute(last, axis, up)
        after = lax.ppermute(leading, axis, down)
        x = jnp.concatenate([before, x, after], axis=dim)
    return x


def smooth_abs(value):
    return jnp.sqrt(value * value + SMOOTH * SMOOTH) - SMOOTH


def smooth_slope(value):
    return value / jnp.sqrt(value * value + SMOOTH * SMOOTH)


def local_step(
    extended,
    features,
    target,
    kmt,
    dw_kernel,
    dw_bias,
    ln_gain,
    ln_bias,
    w_in,
    b_in,
    w_out,
    b_out,
    layer_scale,
):
    members, lon_dev, lat_rows, chans = features.shape
    depth = jnp.zeros(features.shape, jnp.float32) + dw_bias
    for lon_off in range(7):
        for lat_off in range(7):
            depth = depth + dw_kernel[lon_off, lat_off] * extended[
                :, lon_off : lon_off + lon_dev, lat_off : lat_off + lat_rows, :
            ].astype(jnp.float32)
    mean_val = jnp.mean(depth, axis=-1, keepdims=True)
    centred = depth - mean_val
    variance = jnp.mean(centred * centred, axis=-1, keepdims=True)
    inv_std = lax.rsqrt(variance + EPSILON)
    unit = centred * inv_std
    normed = (unit * ln_gain + ln_bias).astype(jnp.bfloat16)
    level_of = jnp.arange(chans, dtype=jnp.int32) * LEVELS // chans
    wet_mask = (level_of[None, None, :] < kmt[:, :, None]).astype(jnp.float32)
    rows = lon_dev * lat_rows
    pre_acts = []
    hiddens = []
    outputs = []
    for member in range(members):
        flat_rows = normed[member].reshape(rows, chans)
        pre_act = jnp.dot(flat_rows, w_in, preferred_element_type=jnp.float32) + b_in
        hidden = jax.nn.gelu(pre_act).astype(jnp.bfloat16)
        pre_acts.append(pre_act)
        hiddens.append(hidden)
        outputs.append(
            (jnp.dot(hidden, w_out, preferred_element_type=jnp.float32) + b_out).reshape(
                lon_dev, lat_rows, chans
            )
        )
    branch = jnp.stack(outputs)
    pred = wet_mask * (features.astype(jnp.float32) + layer_scale * branch)
    target_full = target.astype(jnp.float32)
    pair_weight = 1.0 / (members * (members - 1))

    def crps_of(pred):
        skill = jnp.zeros(target.shape, jnp.float32)
        spread = jnp.zeros(target.shape, jnp.float32)
        for member in range(members):
            skill = skill + smooth_abs(pred[member] - target_full)
            for other in range(member + 1, members):
                spread = spread + smooth_abs(pred[member] - pred[other])
        return wet_mask * (skill / members - pair_weight * spread)

    grad_list = []
    for member in range(members):
        slope_sum = jnp.zeros(target.shape, jnp.float32)
        for other in range(members):
            if other != member:
                slope_sum = slope_sum + smooth_slope(pred[member] - pred[other])
        grad_list.append(
            wet_mask
            * (smooth_slope(pred[member] - target_full) / members - pair_weight * slope_sum)
        )
    grad_pred = jnp.stack(grad_list)
    grad_scale = jnp.sum(grad_pred * branch, axis=(0, 1, 2))
    grad_b_out = jnp.zeros((chans,), jnp.float32)
    grad_w_out = jnp.zeros(w_out.shape, jnp.float32)
    grad_b_in = jnp.zeros(b_in.shape, jnp.float32)
    grad_w_in = jnp.zeros(w_in.shape, jnp.float32)
    normed_grads = []
    contract_rows = (((0,), (0,)), ((), ()))
    contract_cols = (((1,), (1,)), ((), ()))
    for member in range(members):
        grad_out = (grad_pred[member] * layer_scale).reshape(rows, chans)
        grad_b_out = grad_b_out + jnp.sum(grad_out, axis=0)
        out_half = grad_out.astype(jnp.bfloat16)
        grad_w_out = grad_w_out + lax.dot_general(
            hiddens[member], out_half, contract_rows, preferred_element_type=jnp.float32
        )
        grad_hidden = lax.dot_general(
            out_half, w_out, contract_cols, preferred_element_type=jnp.float32
        )
        grad_pre = jax.vjp(jax.nn.gelu, pre_acts[member])[1](grad_hidden)[0]
        grad_b_in = grad_b_in + jnp.sum(grad_pre, axis=0)
        pre_half = grad_pre.astype(jnp.bfloat16)
        grad_w_in = grad_w_in + lax.dot_general(
            normed[member].reshape(rows, chans),
            pre_half,
            contract_rows,
            preferred_element_type=jnp.float32,
        )
        normed_grads.append(
            lax.dot_general(
                pre_half, w_in, contract_cols, preferred_element_type=jnp.float32
            ).reshape(lon_dev, lat_rows, chans)
        )
    grad_normed = jnp.stack(normed_grads)
    grad_ln_gain = jnp.sum(grad_normed * unit, axis=(0, 1, 2))
    grad_ln_bias = jnp.sum(grad_normed, axis=(0, 1, 2))

    def depth_backward(grad_normed):
        grad_unit = grad_normed * ln_gain
        grad_depth = inv_std * (
            grad_unit
            - jnp.mean(grad_unit, axis=-1, keepdims=True)
            - unit * jnp.mean(grad_unit * unit, axis=-1, keepdims=True)
        )
        grad_dw_bias = jnp.sum(grad_depth, axis=(0, 1, 2))
        kernel_rows = []
        for lon_off in range(7):
            kernel_cols = []
            for lat_off in range(7):
                kernel_cols.append(
                    jnp.sum(
                        grad_depth
                        * extended[
                            :, lon_off : lon_off + lon_dev, lat_off : lat_off + lat_rows, :
                        ].astype(jnp.float32),
                        axis=(0, 1, 2),
                    )
                )
            kernel_rows.append(jnp.stack(kernel_cols))
        grad_kernel = jnp.stack(kernel_rows)
        return grad_depth, grad_kernel, grad_dw_bias

    sums = (grad_ln_gain, grad_ln_bias, grad_w_in, grad_b_in, grad_w_out, grad_b_out, grad_scale)
    deferred = (pred, crps_of)
    return (pred.astype(jnp.bfloat16), deferred, grad_pred, grad_normed, sums, depth_backward)


def mirrored(x, axis):
    size = lax.axis_size(axis)
    return lax.ppermute(x, axis, [(i, size - 1 - i) for i in range(size)])


def mirror_rows(top_rows):
    return mirrored(top_rows, "lon")[:, ::-1, ::-1, :]


def mirror_grads(fold_rows):
    picked = mirrored(fold_rows.astype(jnp.bfloat16), "lon").astype(fold_rows.dtype)
    return picked[:, ::-1, ::-1, :]


def halving_allreduce(flat, axis, gather_dtype):
    size = lax.axis_size(axis)
    bits = size.bit_length() - 1
    idx = lax.axis_index(axis)
    cur = flat
    for bit in range(bits):
        half = cur.shape[0] // 2
        mine = (idx >> bit) & 1
        keep = lax.dynamic_slice_in_dim(cur, mine * half, half)
        send = lax.dynamic_slice_in_dim(cur, (1 - mine) * half, half)
        cur = keep + swapped(send, axis, bit)
    cur = cur.astype(gather_dtype)
    for bit in reversed(range(bits)):
        mine = (idx >> bit) & 1
        recv = swapped(cur, axis, bit)
        cur = jnp.where(mine == 0, jnp.concatenate([cur, recv]), jnp.concatenate([recv, cur]))
    return cur.astype(flat.dtype)


def radix_allreduce(flat, axis, gather_dtype, operand, start, finish, fill):
    size = lax.axis_size(axis)
    nbits = size.bit_length() - 1
    groups = [[0]] + [list(range(b, min(b + 2, nbits))) for b in range(1, nbits, 2)]
    idx = lax.axis_index(axis)
    cur = flat
    for bits in groups:
        if bits == groups[1]:
            cur, handoff = lax.optimization_barrier((cur, first[0]))
            second = finish(handoff)
        radix, low = 1 << len(bits), bits[0]
        sub = (idx >> low) & (radix - 1)
        part = cur.shape[0] // radix
        total = lax.dynamic_slice_in_dim(cur, sub * part, part)
        for d in range(1, radix):
            send = lax.dynamic_slice_in_dim(cur, (sub ^ d) * part, part)
            total = total + lax.ppermute(send, axis, [(i, i ^ (d << low)) for i in range(size)])
        cur = total
        if bits == groups[0]:
            cur, operand = lax.optimization_barrier((cur, operand))
            first = start(operand)
        elif bits == groups[1]:
            cur, second = lax.optimization_barrier((cur, second))
            third = fill(second)
        elif bits == groups[2]:
            cur, third = lax.optimization_barrier((cur, third))
    cur = cur.astype(gather_dtype)
    for bits in reversed(groups):
        radix, low = 1 << len(bits), bits[0]
        sub = (idx >> low) & (radix - 1)
        pieces = [cur] + [
            lax.ppermute(cur, axis, [(i, i ^ (d << low)) for i in range(size)])
            for d in range(1, radix)
        ]
        placed = []
        for p in range(radix):
            pick = pieces[p ^ (radix - 1)]
            for s in range(radix - 1):
                pick = jnp.where(sub == s, pieces[p ^ s], pick)
            placed.append(pick)
        cur = jnp.concatenate(placed)
    return cur.astype(flat.dtype), first[1:], second, third


def butterfly_allreduce(flat, axis):
    for bit in range(lax.axis_size(axis).bit_length() - 1):
        flat = flat + swapped(flat, axis, bit)
    return flat


def pack(arrays, multiple):
    flat = jnp.concatenate([a.reshape(-1) for a in arrays])
    extra = -flat.shape[0] % multiple
    return jnp.pad(flat, (0, extra))


def unpack(flat, arrays):
    out, at = [], 0
    for a in arrays:
        out.append(flat[at : at + a.size].reshape(a.shape))
        at += a.size
    return out


def on_device(
    features,
    target,
    south_rim,
    kmt,
    dw_kernel,
    dw_bias,
    ln_gain,
    ln_bias,
    w_in,
    b_in,
    w_out,
    b_out,
    layer_scale,
):
    members, lon_dev, lat_rows, chans = features.shape
    params = (dw_kernel, dw_bias, ln_gain, ln_bias, w_in, b_in, w_out, b_out, layer_scale)
    north_rows = mirror_rows(features[:, :, lat_rows - 3 :, :])
    joined = jnp.concatenate([south_rim, features, north_rows], axis=2)
    extended = with_halo(joined, (("lon", 1),), 3)
    predicted, deferred, grad_pred, grad_normed, sums, depth_backward = local_step(
        extended, features, target, kmt, *params
    )

    def backward(grad_normed):
        grad_depth, kernel_sum, dw_bias_sum = depth_backward(grad_normed)
        grad_halo = with_halo(grad_depth, (("lon", 1),), 3)
        return grad_halo, kernel_sum, dw_bias_sum

    def backward_conv(grad_halo):
        padded = jnp.pad(grad_halo, ((0, 0), (0, 0), (6, 6), (0, 0)))
        grad_ext = jnp.zeros((members, lon_dev, lat_rows + 6, chans), jnp.float32)
        for lon_off in range(7):
            for lat_off in range(7):
                grad_ext = (
                    grad_ext
                    + dw_kernel[lon_off, lat_off]
                    * padded[
                        :,
                        6 - lon_off : 6 - lon_off + lon_dev,
                        6 - lat_off : 6 - lat_off + lat_rows + 6,
                        :,
                    ]
                )
        return grad_ext

    pred_full, crps_fn = deferred

    def crps_of(grad_ext):
        _, held = lax.optimization_barrier((grad_ext, pred_full))
        return crps_fn(held)

    lon_size = lax.axis_size("lon")
    reduced, (kernel_sum, dw_bias_sum), grad_ext, crps_field = radix_allreduce(
        pack(sums, lon_size * 1024),
        "lon",
        jnp.bfloat16,
        grad_normed,
        backward,
        backward_conv,
        crps_of,
    )
    gain_sum, bias_sum, w_in_sum, b_in_sum, w_out_sum, b_out_sum, scale_sum = unpack(reduced, sums)
    small = (kernel_sum, dw_bias_sum)
    kernel_tot, dw_bias_tot = unpack(butterfly_allreduce(pack(small, 128), "lon"), small)
    totals = (
        kernel_tot,
        dw_bias_tot,
        gain_sum,
        bias_sum,
        w_in_sum,
        b_in_sum,
        w_out_sum,
        b_out_sum,
        scale_sum,
    )
    back_rows = mirror_grads(grad_ext[:, :, lat_rows + 3 :, :])
    inner = grad_pred + grad_ext[:, :, 3 : lat_rows + 3, :]
    grad_features = jnp.concatenate(
        [inner[:, :, : lat_rows - 3, :], inner[:, :, lat_rows - 3 :, :] + back_rows], axis=2
    ).astype(jnp.bfloat16)
    factor = 1.0 / math.sqrt(members * lat_rows * lon_dev * lax.axis_size("lon"))
    return (
        predicted,
        crps_field,
        grad_features,
        totals[0] * factor,
        totals[1] * factor,
        totals[2] * factor,
        totals[3] * factor,
        totals[4] * factor,
        totals[5] * factor,
        totals[6] * factor,
        totals[7] * factor,
        totals[8] * factor,
    )


def solution(mesh):
    placed = (
        P(None, ("groups", "lon"), None, None),
        P(("groups", "lon"), None, None),
        P(None, ("groups", "lon"), None, None),
        P(("groups", "lon"), None),
        P(),
        P(),
        P(),
        P(),
        P(),
        P(),
        P(),
        P(),
        P(),
    )
    return jax.shard_map(
        on_device,
        mesh=mesh,
        in_specs=placed,
        out_specs=(
            P(None, ("groups", "lon"), None, None),
            P(("groups", "lon"), None, None),
            P(None, ("groups", "lon"), None, None),
            P("groups", None, None),
            P("groups"),
            P("groups"),
            P("groups"),
            P("groups", None),
            P("groups"),
            P("groups", None),
            P("groups"),
            P("groups"),
        ),
        check_vma=False,
    )
```

```python
import math

import jax
import jax.numpy as jnp
from jax import lax
from jax.sharding import PartitionSpec as P

LEVELS = 19


SMOOTH = 0.25
EPSILON = 1e-06


def swapped(x, axis, bit):
    return lax.ppermute(x, axis, [(i, i ^ 1 << bit) for i in range(lax.axis_size(axis))])


def with_halo(x, sides, width, send_dtype=None):
    for axis, dim in sides:
        size, length = (lax.axis_size(axis), x.shape[dim])
        up = [(i, (i + 1) % size) for i in range(size)]
        down = [(j, i) for i, j in up]
        last = lax.slice_in_dim(x, length - width, length, axis=dim)
        leading = lax.slice_in_dim(x, 0, width, axis=dim)
        if send_dtype is not None:
            last, leading = last.astype(send_dtype), leading.astype(send_dtype)
        before = lax.ppermute(last, axis, up).astype(x.dtype)
        after = lax.ppermute(leading, axis, down).astype(x.dtype)
        x = jnp.concatenate([before, x, after], axis=dim)
    return x


def smooth_abs(value):
    return jnp.sqrt(value * value + SMOOTH * SMOOTH) - SMOOTH


def smooth_slope(value):
    return value / jnp.sqrt(value * value + SMOOTH * SMOOTH)


def local_step(
    extended,
    features,
    target,
    kmt,
    dw_kernel,
    dw_bias,
    ln_gain,
    ln_bias,
    w_in,
    b_in,
    w_out,
    b_out,
    layer_scale,
):
    members, lon_dev, lat_rows, chans = features.shape
    depth = jnp.zeros(features.shape, jnp.float32) + dw_bias
    for lon_off in range(7):
        for lat_off in range(7):
            depth = depth + dw_kernel[lon_off, lat_off] * extended[
                :, lon_off : lon_off + lon_dev, lat_off : lat_off + lat_rows, :
            ].astype(jnp.float32)
    mean_val = jnp.mean(depth, axis=-1, keepdims=True)
    centred = depth - mean_val
    variance = jnp.mean(centred * centred, axis=-1, keepdims=True)
    inv_std = lax.rsqrt(variance + EPSILON)
    unit = centred * inv_std
    normed = (unit * ln_gain + ln_bias).astype(jnp.bfloat16)
    level_of = jnp.arange(chans, dtype=jnp.int32) * LEVELS // chans
    wet_mask = (level_of[None, None, :] < kmt[:, :, None]).astype(jnp.float32)
    rows = lon_dev * lat_rows
    pre_acts = []
    hiddens = []
    outputs = []
    for member in range(members):
        flat_rows = normed[member].reshape(rows, chans)
        pre_act = jnp.dot(flat_rows, w_in, preferred_element_type=jnp.float32) + b_in
        hidden = jax.nn.gelu(pre_act).astype(jnp.bfloat16)
        pre_acts.append(pre_act)
        hiddens.append(hidden)
        outputs.append(
            (jnp.dot(hidden, w_out, preferred_element_type=jnp.float32) + b_out).reshape(
                lon_dev, lat_rows, chans
            )
        )
    branch = jnp.stack(outputs)
    pred = wet_mask * (features.astype(jnp.float32) + layer_scale * branch)
    target_full = target.astype(jnp.float32)
    pair_weight = 1.0 / (members * (members - 1))
    skill = jnp.zeros(target.shape, jnp.float32)
    spread = jnp.zeros(target.shape, jnp.float32)
    for member in range(members):
        skill = skill + smooth_abs(pred[member] - target_full)
        for other in range(member + 1, members):
            spread = spread + smooth_abs(pred[member] - pred[other])
    crps_field = wet_mask * (skill / members - pair_weight * spread)
    grad_list = []
    for member in range(members):
        slope_sum = jnp.zeros(target.shape, jnp.float32)
        for other in range(members):
            if other != member:
                slope_sum = slope_sum + smooth_slope(pred[member] - pred[other])
        grad_list.append(
            wet_mask
            * (smooth_slope(pred[member] - target_full) / members - pair_weight * slope_sum)
        )
    grad_pred = jnp.stack(grad_list)
    grad_scale = jnp.sum(grad_pred * branch, axis=(0, 1, 2))
    grad_b_out = jnp.zeros((chans,), jnp.float32)
    grad_w_out = jnp.zeros(w_out.shape, jnp.float32)
    grad_b_in = jnp.zeros(b_in.shape, jnp.float32)
    grad_w_in = jnp.zeros(w_in.shape, jnp.float32)
    normed_grads = []
    contract_rows = (((0,), (0,)), ((), ()))
    contract_cols = (((1,), (1,)), ((), ()))
    for member in range(members):
        grad_out = (grad_pred[member] * layer_scale).reshape(rows, chans)
        grad_b_out = grad_b_out + jnp.sum(grad_out, axis=0)
        out_half = grad_out.astype(jnp.bfloat16)
        grad_w_out = grad_w_out + lax.dot_general(
            hiddens[member], out_half, contract_rows, preferred_element_type=jnp.float32
        )
        grad_hidden = lax.dot_general(
            out_half, w_out, contract_cols, preferred_element_type=jnp.float32
        )
        grad_pre = jax.vjp(jax.nn.gelu, pre_acts[member])[1](grad_hidden)[0]
        grad_b_in = grad_b_in + jnp.sum(grad_pre, axis=0)
        pre_half = grad_pre.astype(jnp.bfloat16)
        grad_w_in = grad_w_in + lax.dot_general(
            normed[member].reshape(rows, chans),
            pre_half,
            contract_rows,
            preferred_element_type=jnp.float32,
        )
        normed_grads.append(
            lax.dot_general(
                pre_half, w_in, contract_cols, preferred_element_type=jnp.float32
            ).reshape(lon_dev, lat_rows, chans)
        )
    grad_normed = jnp.stack(normed_grads)
    grad_ln_gain = jnp.sum(grad_normed * unit, axis=(0, 1, 2))
    grad_ln_bias = jnp.sum(grad_normed, axis=(0, 1, 2))

    def depth_backward(grad_normed):
        grad_unit = grad_normed * ln_gain
        grad_depth = inv_std * (
            grad_unit
            - jnp.mean(grad_unit, axis=-1, keepdims=True)
            - unit * jnp.mean(grad_unit * unit, axis=-1, keepdims=True)
        )
        grad_dw_bias = jnp.sum(grad_depth, axis=(0, 1, 2))
        kernel_rows = []
        for lon_off in range(7):
            kernel_cols = []
            for lat_off in range(7):
                kernel_cols.append(
                    jnp.sum(
                        grad_depth
                        * extended[
                            :, lon_off : lon_off + lon_dev, lat_off : lat_off + lat_rows, :
                        ].astype(jnp.float32),
                        axis=(0, 1, 2),
                    )
                )
            kernel_rows.append(jnp.stack(kernel_cols))
        grad_kernel = jnp.stack(kernel_rows)
        return grad_depth, grad_kernel, grad_dw_bias

    sums = (grad_ln_gain, grad_ln_bias, grad_w_in, grad_b_in, grad_w_out, grad_b_out, grad_scale)
    return (pred.astype(jnp.bfloat16), crps_field, grad_pred, grad_normed, sums, depth_backward)


def mirrored(x, axis):
    size = lax.axis_size(axis)
    return lax.ppermute(x, axis, [(i, size - 1 - i) for i in range(size)])


def mirror_rows(top_rows):
    return mirrored(top_rows, "lon")[:, ::-1, ::-1, :]


def mirror_grads(fold_rows):
    picked = mirrored(fold_rows.astype(jnp.bfloat16), "lon").astype(fold_rows.dtype)
    return picked[:, ::-1, ::-1, :]


def halving_allreduce(flat, axis, gather_dtype):
    size = lax.axis_size(axis)
    bits = size.bit_length() - 1
    idx = lax.axis_index(axis)
    cur = flat
    for bit in range(bits):
        half = cur.shape[0] // 2
        mine = (idx >> bit) & 1
        keep = lax.dynamic_slice_in_dim(cur, mine * half, half)
        send = lax.dynamic_slice_in_dim(cur, (1 - mine) * half, half)
        cur = keep + swapped(send, axis, bit)
    cur = cur.astype(gather_dtype)
    for bit in reversed(range(bits)):
        mine = (idx >> bit) & 1
        recv = swapped(cur, axis, bit)
        cur = jnp.where(mine == 0, jnp.concatenate([cur, recv]), jnp.concatenate([recv, cur]))
    return cur.astype(flat.dtype)


def radix_allreduce(flat, axis, gather_dtype, operand, start, finish):
    size = lax.axis_size(axis)
    nbits = size.bit_length() - 1
    groups = [[0]] + [list(range(b, min(b + 2, nbits))) for b in range(1, nbits, 2)]
    idx = lax.axis_index(axis)
    cur = flat
    for bits in groups:
        if bits == groups[1]:
            cur, handoff = lax.optimization_barrier((cur, first[0]))
            second = finish(handoff)
        radix, low = 1 << len(bits), bits[0]
        sub = (idx >> low) & (radix - 1)
        part = cur.shape[0] // radix
        total = lax.dynamic_slice_in_dim(cur, sub * part, part)
        for d in range(1, radix):
            send = lax.dynamic_slice_in_dim(cur, (sub ^ d) * part, part)
            total = total + lax.ppermute(send, axis, [(i, i ^ (d << low)) for i in range(size)])
        cur = total
        if bits == groups[0]:
            cur, operand = lax.optimization_barrier((cur, operand))
            first = start(operand)
        elif bits == groups[1]:
            cur, second = lax.optimization_barrier((cur, second))
    cur = cur.astype(gather_dtype)
    for bits in reversed(groups):
        radix, low = 1 << len(bits), bits[0]
        sub = (idx >> low) & (radix - 1)
        pieces = [cur] + [
            lax.ppermute(cur, axis, [(i, i ^ (d << low)) for i in range(size)])
            for d in range(1, radix)
        ]
        placed = []
        for p in range(radix):
            pick = pieces[p ^ (radix - 1)]
            for s in range(radix - 1):
                pick = jnp.where(sub == s, pieces[p ^ s], pick)
            placed.append(pick)
        cur = jnp.concatenate(placed)
    return cur.astype(flat.dtype), first[1:], second


def butterfly_allreduce(flat, axis):
    for bit in range(lax.axis_size(axis).bit_length() - 1):
        flat = flat + swapped(flat, axis, bit)
    return flat


def pack(arrays, multiple):
    flat = jnp.concatenate([a.reshape(-1) for a in arrays])
    extra = -flat.shape[0] % multiple
    return jnp.pad(flat, (0, extra))


def unpack(flat, arrays):
    out, at = [], 0
    for a in arrays:
        out.append(flat[at : at + a.size].reshape(a.shape))
        at += a.size
    return out


def on_device(
    features,
    target,
    south_rim,
    kmt,
    dw_kernel,
    dw_bias,
    ln_gain,
    ln_bias,
    w_in,
    b_in,
    w_out,
    b_out,
    layer_scale,
):
    members, lon_dev, lat_rows, chans = features.shape
    params = (dw_kernel, dw_bias, ln_gain, ln_bias, w_in, b_in, w_out, b_out, layer_scale)
    north_rows = mirror_rows(features[:, :, lat_rows - 3 :, :])
    joined = jnp.concatenate([south_rim, features, north_rows], axis=2)
    extended = with_halo(joined, (("lon", 1),), 3)
    predicted, crps_field, grad_pred, grad_normed, sums, depth_backward = local_step(
        extended, features, target, kmt, *params
    )

    def backward(grad_normed):
        grad_depth, kernel_sum, dw_bias_sum = depth_backward(grad_normed)
        grad_halo = with_halo(grad_depth, (("lon", 1),), 3, jnp.bfloat16)
        return grad_halo, kernel_sum, dw_bias_sum

    def backward_conv(grad_halo):
        padded = jnp.pad(grad_halo, ((0, 0), (0, 0), (6, 6), (0, 0)))
        grad_ext = jnp.zeros((members, lon_dev, lat_rows + 6, chans), jnp.float32)
        for lon_off in range(7):
            for lat_off in range(7):
                grad_ext = (
                    grad_ext
                    + dw_kernel[lon_off, lat_off]
                    * padded[
                        :,
                        6 - lon_off : 6 - lon_off + lon_dev,
                        6 - lat_off : 6 - lat_off + lat_rows + 6,
                        :,
                    ]
                )
        return grad_ext

    lon_size = lax.axis_size("lon")
    reduced, (kernel_sum, dw_bias_sum), grad_ext = radix_allreduce(
        pack(sums, lon_size * 1024), "lon", jnp.bfloat16, grad_normed, backward, backward_conv
    )
    gain_sum, bias_sum, w_in_sum, b_in_sum, w_out_sum, b_out_sum, scale_sum = unpack(reduced, sums)
    small = (kernel_sum, dw_bias_sum)
    kernel_tot, dw_bias_tot = unpack(butterfly_allreduce(pack(small, 128), "lon"), small)
    totals = (
        kernel_tot,
        dw_bias_tot,
        gain_sum,
        bias_sum,
        w_in_sum,
        b_in_sum,
        w_out_sum,
        b_out_sum,
        scale_sum,
    )
    back_rows = mirror_grads(grad_ext[:, :, lat_rows + 3 :, :])
    inner = grad_pred + grad_ext[:, :, 3 : lat_rows + 3, :]
    grad_features = jnp.concatenate(
        [inner[:, :, : lat_rows - 3, :], inner[:, :, lat_rows - 3 :, :] + back_rows], axis=2
    ).astype(jnp.bfloat16)
    factor = 1.0 / math.sqrt(members * lat_rows * lon_dev * lax.axis_size("lon"))
    return (
        predicted,
        crps_field,
        grad_features,
        totals[0] * factor,
        totals[1] * factor,
        totals[2] * factor,
        totals[3] * factor,
        totals[4] * factor,
        totals[5] * factor,
        totals[6] * factor,
        totals[7] * factor,
        totals[8] * factor,
    )


def solution(mesh):
    placed = (
        P(None, ("groups", "lon"), None, None),
        P(("groups", "lon"), None, None),
        P(None, ("groups", "lon"), None, None),
        P(("groups", "lon"), None),
        P(),
        P(),
        P(),
        P(),
        P(),
        P(),
        P(),
        P(),
        P(),
    )
    return jax.shard_map(
        on_device,
        mesh=mesh,
        in_specs=placed,
        out_specs=(
            P(None, ("groups", "lon"), None, None),
            P(("groups", "lon"), None, None),
            P(None, ("groups", "lon"), None, None),
            P("groups", None, None),
            P("groups"),
            P("groups"),
            P("groups"),
            P("groups", None),
            P("groups"),
            P("groups", None),
            P("groups"),
            P("groups"),
        ),
        check_vma=False,
    )
```
